32 devices in a mesh: fsdp: 8 (over y, x, core), dp: 4 (over z).
Axes of the slice: x: 2, y: 2, z: 4, core: 2. Of those that a mesh axis runs over, the one named last changes fastest.
Arguments:
- tokens: bfloat16 [2, 32, 128, 2560], P(None, ('fsdp', 'dp')), may hold values from -24 to 24
- lengths: int32 [2, 32], P(None, ('fsdp', 'dp')), may hold values from 64 to 128, as said below
- attn_gain: bfloat16 [2560], P(('fsdp', 'dp')), may hold values from 0.099609375 to 1.8984375
- query_down: bfloat16 [2560, 768], P(('fsdp', 'dp')), may hold values from -0.125 to 0.125
- query_gain: bfloat16 [768], P(('fsdp', 'dp')), may hold values from 0.099609375 to 1.8984375
- query_up: bfloat16 [768, 3840], P(('fsdp', 'dp')), may hold values from -0.21875 to 0.21875
- latent_down: bfloat16 [2560, 288], P(('fsdp', 'dp')), may hold values from -0.125 to 0.125
- latent_gain: bfloat16 [256], P(('fsdp', 'dp')), may hold values from 0.099609375 to 1.8984375
- latent_up: bfloat16 [256, 5120], P(('fsdp', 'dp')), may hold values from -0.375 to 0.375
- output_weight: bfloat16 [2560, 2560], P(('fsdp', 'dp')), may hold values from -2 to 2
- feed_gain: bfloat16 [2560], P(('fsdp', 'dp')), may hold values from 0.099609375 to 1.8984375
- gate_weight: bfloat16 [2560, 6400], P(('fsdp', 'dp')), may hold values from -0.125 to 0.125
- up_weight: bfloat16 [2560, 6400], P(('fsdp', 'dp')), may hold values from -0.125 to 0.125
- down_weight: bfloat16 [6400, 2560], P(('fsdp', 'dp')), may hold values from -0.75 to 0.75
- cotangent: bfloat16 [2, 32, 128, 2560], P(None, ('fsdp', 'dp')), may hold values from -6 to 6
Outputs:
- output: bfloat16 [2, 32, 128, 2560], P(None, ('fsdp', 'dp'))
- input_grad: float32 [2, 32, 128, 2560], P(None, ('fsdp', 'dp'))
- attn_gain_grad: float32 [2560], P(('fsdp', 'dp'))
- query_down_grad: float32 [2560, 768], P(('fsdp', 'dp'))
- query_gain_grad: float32 [768], P(('fsdp', 'dp'))
- query_up_grad: float32 [768, 3840], P(('fsdp', 'dp'))
- latent_down_grad: float32 [2560, 288], P(('fsdp', 'dp'))
- latent_gain_grad: float32 [256], P(('fsdp', 'dp'))
- latent_up_grad: float32 [256, 5120], P(('fsdp', 'dp'))
- output_weight_grad: float32 [2560, 2560], P(('fsdp', 'dp'))
- feed_gain_grad: float32 [2560], P(('fsdp', 'dp'))
- gate_weight_grad: float32 [2560, 6400], P(('fsdp', 'dp'))
- up_weight_grad: float32 [2560, 6400], P(('fsdp', 'dp'))
- down_weight_grad: float32 [6400, 2560], P(('fsdp', 'dp'))
The draws below stay inside these ranges and needn't reach their ends.
Inputs may be any that keep to these rules, and one draw needn't show every extreme that they name: `lengths`: each sequence fills at least half of its slot of 128 token slots, and some sequence fills its whole slot.
All inputs are finite; a program needn't handle non-finite values.
Results may differ from the reference program's by a relative error of at most 0.018.
Values may be sent and summed in bfloat16 or wider, within the bound.
No kernel may reach another device: no remote copies, remote signals or barrier semaphores. Data moves between devices by JAX's collectives and lax.ppermute only.
A program may use at most 960 MiB of HBM per device.

```python
import math
import jax
import jax.numpy as jnp
from jax import lax

D = 2560
HEADS = 40
NOPE = 64
ROPE = 32
VDIM = 64
QRANK = 768
KVRANK = 256
FF = 6400
SLOT = 128
MICRO = 2
SEQS = 32


def draw_tokens(key, part):
    keys = jax.random.split(key, 3)
    shape = (MICRO, SEQS, SLOT, D)
    row_scale = jnp.exp(jax.random.uniform(keys[1], (MICRO, SEQS, SLOT, 1), jnp.float32, math.log(0.3), math.log(3.0)))
    column_scale = jnp.exp(jax.random.uniform(keys[2], (D,), jnp.float32, math.log(0.3), math.log(3.0)))
    base = jax.random.normal(keys[0], shape, jnp.float32)
    return jnp.clip(base * row_scale * column_scale, -24.0, 24.0).astype(jnp.bfloat16)


def draw_lengths(key, part):
    drawn = jax.random.randint(key, (MICRO, SEQS), SLOT // 2, SLOT + 1)
    return drawn.at[0, 0].set(SLOT).astype(jnp.int32)


def block_levels(key, shape, cuts, low, high):
    level, own = 1.0, jax.random.fold_in(key, 6)
    for axis_at, parts in cuts:
        heights = jnp.exp(jax.random.uniform(jax.random.fold_in(own, axis_at), (parts,), jnp.float32, low / len(cuts), high / len(cuts)))
        level = level * jnp.repeat(heights, shape[axis_at] // parts).reshape([-1 if axis == axis_at else 1 for axis in range(len(shape))])
    return level


def bell_draw(key, extent, spread, limit, cuts=(), kind=jnp.bfloat16):
    entries = spread * jax.random.normal(key, extent, jnp.float32)
    if cuts:
        entries = entries * block_levels(key, extent, cuts, -0.22, 0.18)
    return jnp.clip(entries, -limit, limit).astype(kind)


def setup_inputs(seed: int = 0) -> dict:
    key_of = jax.random.split(jax.random.key(seed), 16)
    tokens = draw_tokens(jax.random.fold_in(key_of[15], 71), 0)
    lengths = draw_lengths(jax.random.fold_in(key_of[15], 71), 0)
    attn_gain = jnp.clip(1.0 + 0.18 * jax.random.normal(key_of[2], (D,), jnp.float32), 0.099609375, 1.8984375).astype(jnp.bfloat16)
    query_down = bell_draw(key_of[3], (D, QRANK), D ** -0.5, 0.125, ((0, 32),))
    query_gain = jnp.clip(1.0 + 0.18 * jax.random.normal(key_of[4], (QRANK,), jnp.float32), 0.099609375, 1.8984375).astype(jnp.bfloat16)
    query_up = bell_draw(key_of[5], (QRANK, HEADS * (NOPE + ROPE)), QRANK ** -0.5, 0.21875, ((0, 32),))
    latent_down = bell_draw(key_of[6], (D, KVRANK + ROPE), D ** -0.5, 0.125, ((0, 32),))
    latent_gain = jnp.clip(1.0 + 0.18 * jax.random.normal(key_of[7], (KVRANK,), jnp.float32), 0.099609375, 1.8984375).astype(jnp.bfloat16)
    latent_up = bell_draw(key_of[8], (KVRANK, HEADS * (NOPE + VDIM)), KVRANK ** -0.5, 0.375, ((0, 32),))
    output_weight = bell_draw(key_of[9], (HEADS * VDIM, D), 8 ** -0.5, 2.0, ((0, 32),))
    feed_gain = jnp.clip(1.0 + 0.18 * jax.random.normal(key_of[10], (D,), jnp.float32), 0.099609375, 1.8984375).astype(jnp.bfloat16)
    gate_weight = bell_draw(key_of[11], (D, FF), D ** -0.5, 0.125, ((0, 32),))
    up_weight = bell_draw(key_of[12], (D, FF), D ** -0.5, 0.125, ((0, 32),))
    down_weight = bell_draw(key_of[13], (FF, D), 64 ** -0.5, 0.75, ((0, 32),))
    cotangent = bell_draw(key_of[14], (MICRO, SEQS, SLOT, D), 1.0, 6.0, ((1, 32),))
    return dict(tokens=tokens, lengths=lengths, attn_gain=attn_gain, query_down=query_down, query_gain=query_gain, query_up=query_up, latent_down=latent_down, latent_gain=latent_gain, latent_up=latent_up, output_weight=output_weight, feed_gain=feed_gain, gate_weight=gate_weight, up_weight=up_weight, down_weight=down_weight, cotangent=cotangent)


@jax.custom_vjp
def low(v):
    return lax.optimization_barrier(v.astype(jnp.bfloat16)).astype(jnp.float32)

@jax.custom_vjp
def low_back(v):
    return v

def low_keep(v):
    return (low(v), None)

def low_pass(kept, grad):
    return (grad,)

def back_keep(v):
    return (v, None)

def back_low(kept, grad):
    return (low(grad),)
low.defvjp(low_keep, low_pass)
low_back.defvjp(back_keep, back_low)
epsilon = 1e-05
depth_scale = 1.4 / math.sqrt(62.0)
masked_score = -1e+30

def matmul(left, right):
    return jnp.dot(left, right, precision=lax.Precision.HIGHEST)

def rms_gain(values, gain):
    return values * lax.rsqrt(lax.optimization_barrier(jnp.mean(values * values, axis=-1, keepdims=True)) + epsilon) * gain

def rotate(values, cosines, sines):
    half = values.shape[-1] // 2
    first = values[..., :half]
    second = values[..., half:]
    return jnp.concatenate([first * cosines - second * sines, second * cosines + first * sines], axis=-1)

def attend(block):
    queries, keys, values, seq_lengths = block
    scale = 1.0 / math.sqrt(NOPE + ROPE)
    raw = jnp.einsum('gqhd,gkhd->ghqk', queries, keys, precision=lax.Precision.HIGHEST) * scale
    query_pos = lax.broadcasted_iota(jnp.int32, (1, 1, SLOT, SLOT), 2)
    key_pos = lax.broadcasted_iota(jnp.int32, (1, 1, SLOT, SLOT), 3)
    allowed = (key_pos <= query_pos) & (key_pos < seq_lengths[:, None, None, None])
    scores = low_back(jnp.where(allowed, raw, masked_score))
    top = lax.optimization_barrier(jnp.max(scores, axis=-1, keepdims=True))
    expo = jnp.exp(scores - top)
    probs = expo / lax.optimization_barrier(jnp.sum(expo, axis=-1, keepdims=True))
    return jnp.einsum('ghqk,gkhd->gqhd', low(probs), values, precision=lax.Precision.HIGHEST)

def layer(inputs, weights, seq_lengths, valid):
    gain_one, down_query, gain_query, up_query, down_latent, gain_latent, up_latent, weight_out, gain_two, weight_gate, weight_up, weight_down = weights
    count = inputs.shape[0]
    half = ROPE // 2
    freqs = 10000.0 ** (-(2.0 * jnp.arange(half, dtype=jnp.float32)) / ROPE)
    angles = jnp.arange(SLOT, dtype=jnp.float32)[:, None] * freqs[None, :]
    cosines = jnp.cos(angles)[:, None, :]
    sines = jnp.sin(angles)[:, None, :]
    h_one = low(rms_gain(inputs, gain_one))
    cq = low_back(matmul(h_one, down_query))
    cq_low = low(rms_gain(cq, gain_query))
    query_raw = low_back(matmul(cq_low, up_query)).reshape(count, SLOT, HEADS, NOPE + ROPE)
    kva = low_back(matmul(h_one, down_latent))
    kv_low = low(rms_gain(kva[..., :KVRANK], gain_latent))
    kv_raw = low_back(matmul(kv_low, up_latent)).reshape(count, SLOT, HEADS, NOPE + VDIM)
    queries = low(jnp.concatenate([query_raw[..., :NOPE], rotate(query_raw[..., NOPE:], cosines, sines)], axis=-1))
    key_rope = rotate(kva[..., KVRANK:].reshape(count, SLOT, 1, ROPE), cosines, sines)
    keys = low(jnp.concatenate([kv_raw[..., :NOPE], jnp.broadcast_to(key_rope, (count, SLOT, HEADS, ROPE))], axis=-1))
    values = low(kv_raw[..., NOPE:])
    group = math.gcd(count, max(1, 4096 // SLOT))
    blocks = (queries.reshape(count // group, group, SLOT, HEADS, NOPE + ROPE), keys.reshape(count // group, group, SLOT, HEADS, NOPE + ROPE), values.reshape(count // group, group, SLOT, HEADS, VDIM), seq_lengths.reshape(count // group, group))
    attended = lax.map(jax.checkpoint(attend), blocks).reshape(count, SLOT, HEADS * VDIM)
    attended = low_back(low(attended))
    middle = inputs + depth_scale * low_back(matmul(attended, weight_out))
    h_two = low(rms_gain(middle, gain_two))
    gate = low_back(matmul(h_two, weight_gate))
    upward = low_back(matmul(h_two, weight_up))
    hidden = low(jax.nn.silu(gate) * upward)
    result = middle + depth_scale * low_back(matmul(hidden, weight_down))
    return result * valid

def reference(tokens, lengths, attn_gain, query_down, query_gain, query_up, latent_down, latent_gain, latent_up, output_weight, feed_gain, gate_weight, up_weight, down_weight, cotangent):
    count = MICRO * SEQS
    inputs = tokens.astype(jnp.float32).reshape(count, SLOT, D)
    seq_lengths = lengths.reshape(count).astype(jnp.int32)
    positions = lax.broadcasted_iota(jnp.int32, (count, SLOT), 1)
    valid = (positions < seq_lengths[:, None]).astype(jnp.float32)[..., None]
    weights = tuple((w.astype(jnp.float32) for w in (attn_gain, query_down, query_gain, query_up, latent_down, latent_gain, latent_up, output_weight, feed_gain, gate_weight, up_weight, down_weight)))
    result, pullback = jax.vjp(lambda a, b: layer(a, b, seq_lengths, valid), inputs, weights)
    input_grad, weight_grads = pullback(cotangent.astype(jnp.float32).reshape(count, SLOT, D))
    output = result.astype(jnp.bfloat16).reshape(MICRO, SEQS, SLOT, D)
    return (output, input_grad.reshape(MICRO, SEQS, SLOT, D), weight_grads[0], weight_grads[1], weight_grads[2], weight_grads[3], weight_grads[4], weight_grads[5], weight_grads[6], weight_grads[7], weight_grads[8], weight_grads[9], weight_grads[10], weight_grads[11])
```

```python
import math

import jax
import jax.numpy as jnp
from jax import lax
from jax.sharding import PartitionSpec as P

HEADS = 40
NOPE = 64
ROPE = 32
VDIM = 64
KVRANK = 256


epsilon = 1e-05
depth_scale = 1.4 / math.sqrt(62.0)
masked_score = -1e30


def matmul(left, right):
    return jnp.dot(left, right, preferred_element_type=jnp.float32)


def rows_product(left, right):
    return lax.dot_general(
        left, right, (((0,), (0,)), ((), ())), preferred_element_type=jnp.float32
    )


def back_product(left, right):
    return lax.dot_general(
        left, right, (((1,), (1,)), ((), ())), preferred_element_type=jnp.float32
    )


def normalize(values):
    inverse = lax.rsqrt(jnp.mean(values * values, axis=-1, keepdims=True) + epsilon)
    return (values * inverse, inverse)


def norm_back(grad, normed, inverse, gain):
    scaled = grad * gain.astype(jnp.float32)
    gain_grad = jnp.sum(grad * normed, axis=0)
    inner = jnp.mean(scaled * normed, axis=-1, keepdims=True)
    return (gain_grad, inverse * (scaled - normed * inner))


def rotate(values, cosines, sines):
    half = values.shape[-1] // 2
    first = values[..., :half]
    second = values[..., half:]
    return jnp.concatenate(
        [first * cosines - second * sines, second * cosines + first * sines], axis=-1
    )


def rotate_back(grad, cosines, sines):
    half = grad.shape[-1] // 2
    first = grad[..., :half]
    second = grad[..., half:]
    return jnp.concatenate(
        [first * cosines + second * sines, second * cosines - first * sines], axis=-1
    )


def scatter_rows(term):
    return lax.psum_scatter(term, ("fsdp", "dp"), scatter_dimension=0, tiled=True)


def local(
    tokens,
    lengths,
    attn_gain,
    query_down,
    query_gain,
    query_up,
    latent_down,
    latent_gain,
    latent_up,
    output_weight,
    feed_gain,
    gate_weight,
    up_weight,
    down_weight,
    cotangent,
):
    micro, _, slot, width = tokens.shape
    rows = micro * slot
    devices = lax.axis_size(("fsdp", "dp"))
    attn_shards = (
        attn_gain,
        query_down,
        query_gain,
        query_up,
        latent_down,
        latent_gain,
        latent_up,
        output_weight,
    )
    feed_shards = (feed_gain, gate_weight, up_weight, down_weight)
    attn_full = (
        lax.all_gather(attn_shards[0], ("fsdp", "dp"), axis=0, tiled=True),
        lax.all_gather(attn_shards[1], ("fsdp", "dp"), axis=0, tiled=True),
        lax.all_gather(attn_shards[2], ("fsdp", "dp"), axis=0, tiled=True),
        lax.all_gather(attn_shards[3], ("fsdp", "dp"), axis=0, tiled=True),
        lax.all_gather(attn_shards[4], ("fsdp", "dp"), axis=0, tiled=True),
        lax.all_gather(attn_shards[5], ("fsdp", "dp"), axis=0, tiled=True),
        lax.all_gather(attn_shards[6], ("fsdp", "dp"), axis=0, tiled=True),
        lax.all_gather(attn_shards[7], ("fsdp", "dp"), axis=0, tiled=True),
    )
    feed_full = (
        lax.all_gather(feed_shards[0], ("fsdp", "dp"), axis=0, tiled=True),
        lax.all_gather(feed_shards[1], ("fsdp", "dp"), axis=0, tiled=True),
        lax.all_gather(feed_shards[2], ("fsdp", "dp"), axis=0, tiled=True),
        lax.all_gather(feed_shards[3], ("fsdp", "dp"), axis=0, tiled=True),
    )
    gain_one, down_query, gain_query, up_query, down_latent, gain_latent, up_latent, weight_out = (
        attn_full
    )
    gain_two, weight_gate, weight_up, weight_down = feed_full
    half = ROPE // 2
    freqs = 10000.0 ** (-(2.0 * jnp.arange(half, dtype=jnp.float32)) / ROPE)
    angles = jnp.arange(slot, dtype=jnp.float32)[:, None] * freqs[None, :]
    cosines = jnp.cos(angles)[:, None, :]
    sines = jnp.sin(angles)[:, None, :]
    positions = lax.broadcasted_iota(jnp.int32, (micro, slot), 1)
    valid_rows = (positions < lengths).astype(jnp.float32).reshape(rows, 1)
    query_pos = lax.broadcasted_iota(jnp.int32, (micro, 1, slot, slot), 2)
    key_pos = lax.broadcasted_iota(jnp.int32, (micro, 1, slot, slot), 3)
    allowed = (key_pos <= query_pos) & (key_pos < lengths[:, :, None, None])
    scale = 1.0 / math.sqrt(NOPE + ROPE)
    inputs = tokens.reshape(rows, width).astype(jnp.float32)
    normed_one, inverse_one = normalize(inputs)
    h_one = (normed_one * gain_one.astype(jnp.float32)).astype(jnp.bfloat16)
    latent_query = matmul(h_one, down_query)
    normed_query, inverse_query = normalize(latent_query)
    query_low = (normed_query * gain_query.astype(jnp.float32)).astype(jnp.bfloat16)
    query_raw = matmul(query_low, up_query).reshape(micro, slot, HEADS, NOPE + ROPE)
    queries = jnp.concatenate(
        [query_raw[..., :NOPE], rotate(query_raw[..., NOPE:], cosines, sines)], axis=-1
    ).astype(jnp.bfloat16)
    latent_all = matmul(h_one, down_latent)
    normed_latent, inverse_latent = normalize(latent_all[:, :KVRANK])
    latent_low = (normed_latent * gain_latent.astype(jnp.float32)).astype(jnp.bfloat16)
    kv_raw = matmul(latent_low, up_latent).reshape(micro, slot, HEADS, NOPE + VDIM)
    key_rope = rotate(latent_all[:, KVRANK:].reshape(micro, slot, 1, ROPE), cosines, sines)
    keys = jnp.concatenate(
        [kv_raw[..., :NOPE], jnp.broadcast_to(key_rope, (micro, slot, HEADS, ROPE))], axis=-1
    ).astype(jnp.bfloat16)
    values = kv_raw[..., NOPE:].astype(jnp.bfloat16)
    raw = jnp.einsum("mqhd,mkhd->mhqk", queries, keys, preferred_element_type=jnp.float32)
    scores = jnp.where(allowed, raw * scale, masked_score)
    top = jnp.max(scores, axis=-1, keepdims=True)
    expo = jnp.exp(scores - top)
    total = jnp.sum(expo, axis=-1, keepdims=True)
    probs = expo / total
    log_total = top + jnp.log(total)
    attended = jnp.einsum(
        "mhqk,mkhd->mqhd", probs.astype(jnp.bfloat16), values, preferred_element_type=jnp.float32
    )
    attended = attended.reshape(rows, HEADS * VDIM).astype(jnp.bfloat16)
    middle = inputs + depth_scale * matmul(attended, weight_out)
    normed_two, inverse_two = normalize(middle)
    h_two = (normed_two * gain_two.astype(jnp.float32)).astype(jnp.bfloat16)
    gate = matmul(h_two, weight_gate)
    upward = matmul(h_two, weight_up)
    sigma = jax.nn.sigmoid(gate)
    hidden = (gate * sigma * upward).astype(jnp.bfloat16)
    result = (middle + depth_scale * matmul(hidden, weight_down)) * valid_rows
    output = result.astype(jnp.bfloat16).reshape(tokens.shape)
    feed_back = (
        lax.all_gather(feed_shards[0], ("fsdp", "dp"), axis=0, tiled=True),
        lax.all_gather(feed_shards[1], ("fsdp", "dp"), axis=0, tiled=True),
        lax.all_gather(feed_shards[2], ("fsdp", "dp"), axis=0, tiled=True),
        lax.all_gather(feed_shards[3], ("fsdp", "dp"), axis=0, tiled=True),
    )
    attn_back = (
        lax.all_gather(attn_shards[0], ("fsdp", "dp"), axis=0, tiled=True),
        lax.all_gather(attn_shards[1], ("fsdp", "dp"), axis=0, tiled=True),
        lax.all_gather(attn_shards[2], ("fsdp", "dp"), axis=0, tiled=True),
        lax.all_gather(attn_shards[3], ("fsdp", "dp"), axis=0, tiled=True),
        lax.all_gather(attn_shards[4], ("fsdp", "dp"), axis=0, tiled=True),
        lax.all_gather(attn_shards[5], ("fsdp", "dp"), axis=0, tiled=True),
        lax.all_gather(attn_shards[6], ("fsdp", "dp"), axis=0, tiled=True),
        lax.all_gather(attn_shards[7], ("fsdp", "dp"), axis=0, tiled=True),
    )
    grad_out = cotangent.reshape(rows, width).astype(jnp.float32) * valid_rows
    grad_feed = (depth_scale * grad_out).astype(jnp.bfloat16)
    grad_hidden = back_product(grad_feed, feed_back[3])
    grad_gate = (grad_hidden * upward * sigma * (1.0 + gate * (1.0 - sigma))).astype(jnp.bfloat16)
    grad_up = (grad_hidden * gate * sigma).astype(jnp.bfloat16)
    grad_h_two = back_product(grad_gate, feed_back[1]) + back_product(grad_up, feed_back[2])
    gain_two_term, grad_middle_norm = norm_back(grad_h_two, normed_two, inverse_two, feed_back[0])
    feed_sums = [
        scatter_rows(gain_two_term),
        scatter_rows(rows_product(h_two, grad_gate)),
        scatter_rows(rows_product(h_two, grad_up)),
        scatter_rows(rows_product(hidden, grad_feed)),
    ]
    grad_middle = grad_out + grad_middle_norm
    grad_attn = (depth_scale * grad_middle).astype(jnp.bfloat16)
    grad_heads = (
        back_product(grad_attn, attn_back[7]).astype(jnp.bfloat16).reshape(micro, slot, HEADS, VDIM)
    )
    probs_again = jnp.exp(scores - log_total)
    grad_values = jnp.einsum(
        "mhqk,mqhd->mkhd",
        probs_again.astype(jnp.bfloat16),
        grad_heads,
        preferred_element_type=jnp.float32,
    )
    grad_probs = jnp.einsum(
        "mqhd,mkhd->mhqk", grad_heads, values, preferred_element_type=jnp.float32
    )
    inner = jnp.sum(probs_again * grad_probs, axis=-1, keepdims=True)
    grad_scores = (probs_again * (grad_probs - inner)).astype(jnp.bfloat16)
    grad_queries = scale * jnp.einsum(
        "mhqk,mkhd->mqhd", grad_scores, keys, preferred_element_type=jnp.float32
    )
    grad_keys = scale * jnp.einsum(
        "mhqk,mqhd->mkhd", grad_scores, queries, preferred_element_type=jnp.float32
    )
    grad_query_raw = jnp.concatenate(
        [grad_queries[..., :NOPE], rotate_back(grad_queries[..., NOPE:], cosines, sines)], axis=-1
    )
    grad_query_raw = grad_query_raw.reshape(rows, HEADS * (NOPE + ROPE)).astype(jnp.bfloat16)
    grad_query_low = back_product(grad_query_raw, attn_back[3])
    grad_kv = (
        jnp.concatenate([grad_keys[..., :NOPE], grad_values], axis=-1)
        .reshape(rows, HEADS * (NOPE + VDIM))
        .astype(jnp.bfloat16)
    )
    grad_latent_low = back_product(grad_kv, attn_back[6])
    latent_gain_term, grad_latent = norm_back(
        grad_latent_low, normed_latent, inverse_latent, attn_back[5]
    )
    grad_key_rope = rotate_back(
        jnp.sum(grad_keys[..., NOPE:], axis=2, keepdims=True), cosines, sines
    ).reshape(rows, ROPE)
    grad_latent_all = jnp.concatenate([grad_latent, grad_key_rope], axis=-1).astype(jnp.bfloat16)
    query_gain_term, grad_latent_query = norm_back(
        grad_query_low, normed_query, inverse_query, attn_back[2]
    )
    grad_latent_query = grad_latent_query.astype(jnp.bfloat16)
    grad_h_one = back_product(grad_latent_all, attn_back[4]) + back_product(
        grad_latent_query, attn_back[1]
    )
    gain_one_term, grad_input_norm = norm_back(grad_h_one, normed_one, inverse_one, attn_back[0])
    input_grad = (grad_middle + grad_input_norm).reshape(tokens.shape)
    attn_sums = [
        scatter_rows(gain_one_term),
        scatter_rows(rows_product(h_one, grad_latent_query)),
        scatter_rows(query_gain_term),
        scatter_rows(rows_product(query_low, grad_query_raw)),
        scatter_rows(rows_product(h_one, grad_latent_all)),
        scatter_rows(latent_gain_term),
        scatter_rows(rows_product(latent_low, grad_kv)),
        scatter_rows(rows_product(attended, grad_attn)),
    ]
    return (
        output,
        input_grad,
        attn_sums[0],
        attn_sums[1],
        attn_sums[2],
        attn_sums[3],
        attn_sums[4],
        attn_sums[5],
        attn_sums[6],
        attn_sums[7],
        feed_sums[0],
        feed_sums[1],
        feed_sums[2],
        feed_sums[3],
    )


def solution(mesh):
    placed = (
        P(None, ("fsdp", "dp"), None, None),
        P(None, ("fsdp", "dp")),
        P(("fsdp", "dp")),
        P(("fsdp", "dp"), None),
        P(("fsdp", "dp")),
        P(("fsdp", "dp"), None),
        P(("fsdp", "dp"), None),
        P(("fsdp", "dp")),
        P(("fsdp", "dp"), None),
        P(("fsdp", "dp"), None),
        P(("fsdp", "dp")),
        P(("fsdp", "dp"), None),
        P(("fsdp", "dp"), None),
        P(("fsdp", "dp"), None),
        P(None, ("fsdp", "dp"), None, None),
    )
    return jax.shard_map(
        local,
        mesh=mesh,
        in_specs=placed,
        out_specs=(
            P(None, ("fsdp", "dp"), None, None),
            P(None, ("fsdp", "dp"), None, None),
            P(("fsdp", "dp")),
            P(("fsdp", "dp"), None),
            P(("fsdp", "dp")),
            P(("fsdp", "dp"), None),
            P(("fsdp", "dp"), None),
            P(("fsdp", "dp")),
            P(("fsdp", "dp"), None),
            P(("fsdp", "dp"), None),
            P(("fsdp", "dp")),
            P(("fsdp", "dp"), None),
            P(("fsdp", "dp"), None),
            P(("fsdp", "dp"), None),
        ),
        check_vma=False,
    )
```

```python
import math

import jax
import jax.numpy as jnp
from jax import lax
from jax.sharding import PartitionSpec as P

HEADS = 40
NOPE = 64
ROPE = 32
VDIM = 64
KVRANK = 256


epsilon = 1e-05
depth_scale = 1.4 / math.sqrt(62.0)
masked_score = -1e30


def matmul(left, right):
    return jnp.dot(left, right, preferred_element_type=jnp.float32)


def rows_product(left, right):
    return lax.dot_general(
        left, right, (((0,), (0,)), ((), ())), preferred_element_type=jnp.float32
    )


def back_product(left, right):
    return lax.dot_general(
        left, right, (((1,), (1,)), ((), ())), preferred_element_type=jnp.float32
    )


def normalize(values):
    inverse = lax.rsqrt(jnp.mean(values * values, axis=-1, keepdims=True) + epsilon)
    return (values * inverse, inverse)


def norm_back(grad, normed, inverse, gain):
    scaled = grad * gain.astype(jnp.float32)
    gain_grad = jnp.sum(grad * normed, axis=0)
    inner = jnp.mean(scaled * normed, axis=-1, keepdims=True)
    return (gain_grad, inverse * (scaled - normed * inner))


def rotate(values, cosines, sines):
    half = values.shape[-1] // 2
    first = values[..., :half]
    second = values[..., half:]
    return jnp.concatenate(
        [first * cosines - second * sines, second * cosines + first * sines], axis=-1
    )


def rotate_back(grad, cosines, sines):
    half = grad.shape[-1] // 2
    first = grad[..., :half]
    second = grad[..., half:]
    return jnp.concatenate(
        [first * cosines + second * sines, second * cosines - first * sines], axis=-1
    )


AXES = ("fsdp", "dp")


def scatter_rows(term):
    return lax.psum_scatter(term, AXES, scatter_dimension=0, tiled=True)


def gather_tokens(values):
    return lax.all_gather(values, AXES, axis=0, tiled=True)


def column_share(values):
    return lax.all_to_all(values, AXES, 1, 0, tiled=True)


def rows_from_columns(grad):
    return lax.all_to_all(grad, AXES, 0, 1, tiled=True)


def local(
    tokens,
    lengths,
    attn_gain,
    query_down,
    query_gain,
    query_up,
    latent_down,
    latent_gain,
    latent_up,
    output_weight,
    feed_gain,
    gate_weight,
    up_weight,
    down_weight,
    cotangent,
):
    micro, _, slot, width = tokens.shape
    rows = micro * slot
    attn_shards = (
        attn_gain,
        query_down,
        query_gain,
        query_up,
        latent_down,
        latent_gain,
        latent_up,
        output_weight,
    )
    feed_shards = (feed_gain, gate_weight, up_weight, down_weight)
    attn_full = (
        lax.all_gather(attn_shards[0], ("fsdp", "dp"), axis=0, tiled=True),
        lax.all_gather(attn_shards[1], ("fsdp", "dp"), axis=0, tiled=True),
        lax.all_gather(attn_shards[2], ("fsdp", "dp"), axis=0, tiled=True),
        lax.all_gather(attn_shards[3], ("fsdp", "dp"), axis=0, tiled=True),
        lax.all_gather(attn_shards[4], ("fsdp", "dp"), axis=0, tiled=True),
        lax.all_gather(attn_shards[5], ("fsdp", "dp"), axis=0, tiled=True),
        lax.all_gather(attn_shards[6], ("fsdp", "dp"), axis=0, tiled=True),
        lax.all_gather(attn_shards[7], ("fsdp", "dp"), axis=0, tiled=True),
    )
    feed_full = (
        lax.all_gather(feed_shards[0], ("fsdp", "dp"), axis=0, tiled=True),
        lax.all_gather(feed_shards[1], ("fsdp", "dp"), axis=0, tiled=True),
        lax.all_gather(feed_shards[2], ("fsdp", "dp"), axis=0, tiled=True),
        lax.all_gather(feed_shards[3], ("fsdp", "dp"), axis=0, tiled=True),
    )
    gain_one, down_query, gain_query, up_query, down_latent, gain_latent, up_latent, weight_out = (
        attn_full
    )
    gain_two, weight_gate, weight_up, weight_down = feed_full
    half = ROPE // 2
    freqs = 10000.0 ** (-(2.0 * jnp.arange(half, dtype=jnp.float32)) / ROPE)
    angles = jnp.arange(slot, dtype=jnp.float32)[:, None] * freqs[None, :]
    cosines = jnp.cos(angles)[:, None, :]
    sines = jnp.sin(angles)[:, None, :]
    positions = lax.broadcasted_iota(jnp.int32, (micro, slot), 1)
    valid_rows = (positions < lengths).astype(jnp.float32).reshape(rows, 1)
    query_pos = lax.broadcasted_iota(jnp.int32, (micro, 1, slot, slot), 2)
    key_pos = lax.broadcasted_iota(jnp.int32, (micro, 1, slot, slot), 3)
    allowed = (key_pos <= query_pos) & (key_pos < lengths[:, :, None, None])
    scale = 1.0 / math.sqrt(NOPE + ROPE)
    inputs = tokens.reshape(rows, width).astype(jnp.float32)
    normed_one, inverse_one = normalize(inputs)
    h_one = (normed_one * gain_one.astype(jnp.float32)).astype(jnp.bfloat16)
    latent_query = matmul(h_one, down_query)
    normed_query, inverse_query = normalize(latent_query)
    query_low = (normed_query * gain_query.astype(jnp.float32)).astype(jnp.bfloat16)
    query_raw = matmul(query_low, up_query).reshape(micro, slot, HEADS, NOPE + ROPE)
    queries = jnp.concatenate(
        [query_raw[..., :NOPE], rotate(query_raw[..., NOPE:], cosines, sines)], axis=-1
    ).astype(jnp.bfloat16)
    latent_all = matmul(h_one, down_latent)
    normed_latent, inverse_latent = normalize(latent_all[:, :KVRANK])
    latent_low = (normed_latent * gain_latent.astype(jnp.float32)).astype(jnp.bfloat16)
    kv_raw = matmul(latent_low, up_latent).reshape(micro, slot, HEADS, NOPE + VDIM)
    key_rope = rotate(latent_all[:, KVRANK:].reshape(micro, slot, 1, ROPE), cosines, sines)
    keys = jnp.concatenate(
        [kv_raw[..., :NOPE], jnp.broadcast_to(key_rope, (micro, slot, HEADS, ROPE))], axis=-1
    ).astype(jnp.bfloat16)
    values = kv_raw[..., NOPE:].astype(jnp.bfloat16)
    raw = jnp.einsum("mqhd,mkhd->mhqk", queries, keys, preferred_element_type=jnp.float32)
    scores = jnp.where(allowed, raw * scale, masked_score)
    top = jnp.max(scores, axis=-1, keepdims=True)
    expo = jnp.exp(scores - top)
    total = jnp.sum(expo, axis=-1, keepdims=True)
    probs = expo / total
    log_total = top + jnp.log(total)
    attended = jnp.einsum(
        "mhqk,mkhd->mqhd", probs.astype(jnp.bfloat16), values, preferred_element_type=jnp.float32
    )
    attended = attended.reshape(rows, HEADS * VDIM).astype(jnp.bfloat16)
    middle = inputs + depth_scale * matmul(attended, weight_out)
    normed_two, inverse_two = normalize(middle)
    h_two = (normed_two * gain_two.astype(jnp.float32)).astype(jnp.bfloat16)
    gate = matmul(h_two, weight_gate)
    upward = matmul(h_two, weight_up)
    sigma = jax.nn.sigmoid(gate)
    hidden = (gate * sigma * upward).astype(jnp.bfloat16)
    result = (middle + depth_scale * matmul(hidden, weight_down)) * valid_rows
    output = result.astype(jnp.bfloat16).reshape(tokens.shape)
    feed_back = (
        lax.all_gather(feed_shards[0], ("fsdp", "dp"), axis=0, tiled=True),
        lax.all_gather(feed_shards[1], ("fsdp", "dp"), axis=0, tiled=True),
        lax.all_gather(feed_shards[2], ("fsdp", "dp"), axis=0, tiled=True),
        lax.all_gather(feed_shards[3], ("fsdp", "dp"), axis=0, tiled=True),
    )
    attn_back = (
        lax.all_gather(attn_shards[0], ("fsdp", "dp"), axis=0, tiled=True),
        lax.all_gather(attn_shards[1], ("fsdp", "dp"), axis=0, tiled=True),
        lax.all_gather(attn_shards[2], ("fsdp", "dp"), axis=0, tiled=True),
        lax.all_gather(attn_shards[3], ("fsdp", "dp"), axis=0, tiled=True),
        lax.all_gather(attn_shards[4], ("fsdp", "dp"), axis=0, tiled=True),
        lax.all_gather(attn_shards[5], ("fsdp", "dp"), axis=0, tiled=True),
        lax.all_gather(attn_shards[6], ("fsdp", "dp"), axis=0, tiled=True),
        lax.all_gather(attn_shards[7], ("fsdp", "dp"), axis=0, tiled=True),
    )
    grad_out = cotangent.reshape(rows, width).astype(jnp.float32) * valid_rows
    grad_feed = (depth_scale * grad_out).astype(jnp.bfloat16)
    grad_hidden = back_product(grad_feed, feed_back[3])
    grad_gate = (grad_hidden * upward * sigma * (1.0 + gate * (1.0 - sigma))).astype(jnp.bfloat16)
    grad_up = (grad_hidden * gate * sigma).astype(jnp.bfloat16)
    grad_h_two = back_product(grad_gate, feed_back[1]) + back_product(grad_up, feed_back[2])
    gain_two_term, grad_middle_norm = norm_back(grad_h_two, normed_two, inverse_two, feed_back[0])
    h_two_all = gather_tokens(h_two)
    feed_sums = [
        scatter_rows(gain_two_term),
        rows_from_columns(rows_product(h_two_all, column_share(grad_gate))),
        rows_from_columns(rows_product(h_two_all, column_share(grad_up))),
        rows_product(column_share(hidden), gather_tokens(grad_feed)),
    ]
    grad_middle = grad_out + grad_middle_norm
    grad_attn = (depth_scale * grad_middle).astype(jnp.bfloat16)
    grad_heads = (
        back_product(grad_attn, attn_back[7]).astype(jnp.bfloat16).reshape(micro, slot, HEADS, VDIM)
    )
    probs_again = jnp.exp(scores - log_total)
    grad_values = jnp.einsum(
        "mhqk,mqhd->mkhd",
        probs_again.astype(jnp.bfloat16),
        grad_heads,
        preferred_element_type=jnp.float32,
    )
    grad_probs = jnp.einsum(
        "mqhd,mkhd->mhqk", grad_heads, values, preferred_element_type=jnp.float32
    )
    inner = jnp.sum(probs_again * grad_probs, axis=-1, keepdims=True)
    grad_scores = (probs_again * (grad_probs - inner)).astype(jnp.bfloat16)
    grad_queries = scale * jnp.einsum(
        "mhqk,mkhd->mqhd", grad_scores, keys, preferred_element_type=jnp.float32
    )
    grad_keys = scale * jnp.einsum(
        "mhqk,mqhd->mkhd", grad_scores, queries, preferred_element_type=jnp.float32
    )
    grad_query_raw = jnp.concatenate(
        [grad_queries[..., :NOPE], rotate_back(grad_queries[..., NOPE:], cosines, sines)], axis=-1
    )
    grad_query_raw = grad_query_raw.reshape(rows, HEADS * (NOPE + ROPE)).astype(jnp.bfloat16)
    grad_query_low = back_product(grad_query_raw, attn_back[3])
    grad_kv = (
        jnp.concatenate([grad_keys[..., :NOPE], grad_values], axis=-1)
        .reshape(rows, HEADS * (NOPE + VDIM))
        .astype(jnp.bfloat16)
    )
    grad_latent_low = back_product(grad_kv, attn_back[6])
    latent_gain_term, grad_latent = norm_back(
        grad_latent_low, normed_latent, inverse_latent, attn_back[5]
    )
    grad_key_rope = rotate_back(
        jnp.sum(grad_keys[..., NOPE:], axis=2, keepdims=True), cosines, sines
    ).reshape(rows, ROPE)
    grad_latent_all = jnp.concatenate([grad_latent, grad_key_rope], axis=-1).astype(jnp.bfloat16)
    query_gain_term, grad_latent_query = norm_back(
        grad_query_low, normed_query, inverse_query, attn_back[2]
    )
    grad_latent_query = grad_latent_query.astype(jnp.bfloat16)
    grad_h_one = back_product(grad_latent_all, attn_back[4]) + back_product(
        grad_latent_query, attn_back[1]
    )
    gain_one_term, grad_input_norm = norm_back(grad_h_one, normed_one, inverse_one, attn_back[0])
    input_grad = (grad_middle + grad_input_norm).reshape(tokens.shape)
    h_one_cols = column_share(h_one)
    attn_sums = [
        scatter_rows(gain_one_term),
        rows_product(h_one_cols, gather_tokens(grad_latent_query)),
        scatter_rows(query_gain_term),
        rows_from_columns(rows_product(gather_tokens(query_low), column_share(grad_query_raw))),
        rows_product(h_one_cols, gather_tokens(grad_latent_all)),
        scatter_rows(latent_gain_term),
        rows_from_columns(rows_product(gather_tokens(latent_low), column_share(grad_kv))),
        rows_product(column_share(attended), gather_tokens(grad_attn)),
    ]
    return (
        output,
        input_grad,
        attn_sums[0],
        attn_sums[1],
        attn_sums[2],
        attn_sums[3],
        attn_sums[4],
        attn_sums[5],
        attn_sums[6],
        attn_sums[7],
        feed_sums[0],
        feed_sums[1],
        feed_sums[2],
        feed_sums[3],
    )


def solution(mesh):
    placed = (
        P(None, ("fsdp", "dp"), None, None),
        P(None, ("fsdp", "dp")),
        P(("fsdp", "dp")),
        P(("fsdp", "dp"), None),
        P(("fsdp", "dp")),
        P(("fsdp", "dp"), None),
        P(("fsdp", "dp"), None),
        P(("fsdp", "dp")),
        P(("fsdp", "dp"), None),
        P(("fsdp", "dp"), None),
        P(("fsdp", "dp")),
        P(("fsdp", "dp"), None),
        P(("fsdp", "dp"), None),
        P(("fsdp", "dp"), None),
        P(None, ("fsdp", "dp"), None, None),
    )
    return jax.shard_map(
        local,
        mesh=mesh,
        in_specs=placed,
        out_specs=(
            P(None, ("fsdp", "dp"), None, None),
            P(None, ("fsdp", "dp"), None, None),
            P(("fsdp", "dp")),
            P(("fsdp", "dp"), None),
            P(("fsdp", "dp")),
            P(("fsdp", "dp"), None),
            P(("fsdp", "dp"), None),
            P(("fsdp", "dp")),
            P(("fsdp", "dp"), None),
            P(("fsdp", "dp"), None),
            P(("fsdp", "dp")),
            P(("fsdp", "dp"), None),
            P(("fsdp", "dp"), None),
            P(("fsdp", "dp"), None),
        ),
        check_vma=False,
    )
```

```python
import math

import jax
import jax.numpy as jnp
from jax import lax
from jax.sharding import PartitionSpec as P

HEADS = 40
NOPE = 64
ROPE = 32
VDIM = 64
KVRANK = 256


epsilon = 1e-05
depth_scale = 1.4 / math.sqrt(62.0)
masked_score = -1e30
AXES = ("fsdp", "dp")
LANES = 128


def matmul(left, right):
    return jnp.dot(left, right, preferred_element_type=jnp.float32)


def rows_product(left, right):
    return lax.dot_general(
        left, right, (((0,), (0,)), ((), ())), preferred_element_type=jnp.float32
    )


def back_product(left, right):
    return lax.dot_general(
        left, right, (((1,), (1,)), ((), ())), preferred_element_type=jnp.float32
    )


def normalize(values):
    inverse = lax.rsqrt(jnp.mean(values * values, axis=-1, keepdims=True) + epsilon)
    return (values * inverse, inverse)


def norm_back(grad, normed, inverse, gain):
    scaled = grad * gain.astype(jnp.float32)
    gain_grad = jnp.sum(grad * normed, axis=0)
    inner = jnp.mean(scaled * normed, axis=-1, keepdims=True)
    return (gain_grad, inverse * (scaled - normed * inner))


def rotate(values, cosines, sines):
    half = values.shape[-1] // 2
    first = values[..., :half]
    second = values[..., half:]
    return jnp.concatenate(
        [first * cosines - second * sines, second * cosines + first * sines], axis=-1
    )


def rotate_back(grad, cosines, sines):
    half = grad.shape[-1] // 2
    first = grad[..., :half]
    second = grad[..., half:]
    return jnp.concatenate(
        [first * cosines + second * sines, second * cosines - first * sines], axis=-1
    )


def padded(size):
    return -(-size // LANES) * LANES


def gather_packed(shards):
    flat = []
    for shard in shards:
        piece = shard.reshape(-1)
        flat.append(jnp.pad(piece, (0, padded(piece.size) - piece.size)))
    gathered = lax.all_gather(jnp.concatenate(flat), AXES, axis=0, tiled=False)
    devices = gathered.shape[0]
    results = []
    offset = 0
    for shard in shards:
        piece = gathered[:, offset : offset + shard.size]
        results.append(piece.reshape((devices * shard.shape[0],) + shard.shape[1:]))
        offset = offset + padded(shard.size)
    return results


def gather_tokens(values):
    return lax.all_gather(values, AXES, axis=0, tiled=True)


def column_shares(stacked, devices):
    tokens, count, width = stacked.shape
    blocks = stacked.reshape(tokens, count, devices, width // devices)
    moved = lax.all_to_all(blocks, AXES, 2, 0, tiled=True)
    return moved.reshape(devices * tokens, count, width // devices)


def rows_from_columns(grad, devices):
    rows, count, share = grad.shape
    moved = lax.all_to_all(grad, AXES, 0, 2, tiled=True)
    return moved.reshape(rows // devices, count, devices, share).reshape(
        rows // devices, count, devices * share
    )


def split_exact(values):
    high = lax.reduce_precision(values, exponent_bits=8, mantissa_bits=7)
    return (high.astype(jnp.bfloat16), (values - high).astype(jnp.bfloat16))


def local(
    tokens,
    lengths,
    attn_gain,
    query_down,
    query_gain,
    query_up,
    latent_down,
    latent_gain,
    latent_up,
    output_weight,
    feed_gain,
    gate_weight,
    up_weight,
    down_weight,
    cotangent,
):
    micro, _, slot, width = tokens.shape
    rows = micro * slot
    devices = lax.axis_size(AXES)
    me = lax.axis_index(AXES)
    ffn = gate_weight.shape[1]
    attn_shards = (
        query_down,
        query_up,
        latent_down,
        latent_up,
        output_weight,
        attn_gain,
        query_gain,
        latent_gain,
        feed_gain,
    )
    (
        down_query,
        up_query,
        down_latent,
        up_latent,
        weight_out,
        gain_one,
        gain_query,
        gain_latent,
        gain_two,
    ) = gather_packed(attn_shards)
    weight_gate_up = lax.all_gather(
        jnp.concatenate([gate_weight, up_weight], axis=1), AXES, axis=0, tiled=True
    )
    weight_down = lax.all_gather(down_weight, AXES, axis=0, tiled=True)
    half = ROPE // 2
    freqs = 10000.0 ** (-(2.0 * jnp.arange(half, dtype=jnp.float32)) / ROPE)
    angles = jnp.arange(slot, dtype=jnp.float32)[:, None] * freqs[None, :]
    cosines = jnp.cos(angles)[:, None, :]
    sines = jnp.sin(angles)[:, None, :]
    positions = lax.broadcasted_iota(jnp.int32, (micro, slot), 1)
    valid_rows = (positions < lengths).astype(jnp.float32).reshape(rows, 1)
    query_pos = lax.broadcasted_iota(jnp.int32, (micro, 1, slot, slot), 2)
    key_pos = lax.broadcasted_iota(jnp.int32, (micro, 1, slot, slot), 3)
    allowed = (key_pos <= query_pos) & (key_pos < lengths[:, :, None, None])
    scale = 1.0 / math.sqrt(NOPE + ROPE)
    inputs = tokens.reshape(rows, width).astype(jnp.float32)
    normed_one, inverse_one = normalize(inputs)
    h_one = (normed_one * gain_one.astype(jnp.float32)).astype(jnp.bfloat16)
    latent_query = matmul(h_one, down_query)
    normed_query, inverse_query = normalize(latent_query)
    query_low = (normed_query * gain_query.astype(jnp.float32)).astype(jnp.bfloat16)
    query_raw = matmul(query_low, up_query).reshape(micro, slot, HEADS, NOPE + ROPE)
    queries = jnp.concatenate(
        [query_raw[..., :NOPE], rotate(query_raw[..., NOPE:], cosines, sines)], axis=-1
    ).astype(jnp.bfloat16)
    latent_all = matmul(h_one, down_latent)
    normed_latent, inverse_latent = normalize(latent_all[:, :KVRANK])
    latent_low = (normed_latent * gain_latent.astype(jnp.float32)).astype(jnp.bfloat16)
    kv_raw = matmul(latent_low, up_latent).reshape(micro, slot, HEADS, NOPE + VDIM)
    key_rope = rotate(latent_all[:, KVRANK:].reshape(micro, slot, 1, ROPE), cosines, sines)
    keys = jnp.concatenate(
        [kv_raw[..., :NOPE], jnp.broadcast_to(key_rope, (micro, slot, HEADS, ROPE))], axis=-1
    ).astype(jnp.bfloat16)
    values = kv_raw[..., NOPE:].astype(jnp.bfloat16)
    raw = jnp.einsum("mqhd,mkhd->mhqk", queries, keys, preferred_element_type=jnp.float32)
    scores = jnp.where(allowed, raw * scale, masked_score)
    top = jnp.max(scores, axis=-1, keepdims=True)
    expo = jnp.exp(scores - top)
    total = jnp.sum(expo, axis=-1, keepdims=True)
    probs = expo / total
    log_total = top + jnp.log(total)
    attended = jnp.einsum(
        "mhqk,mkhd->mqhd", probs.astype(jnp.bfloat16), values, preferred_element_type=jnp.float32
    )
    attended = attended.reshape(rows, HEADS * VDIM).astype(jnp.bfloat16)
    q_rank = query_low.shape[1]
    kv_rank = latent_low.shape[1]
    latents_all = gather_tokens(jnp.concatenate([query_low, latent_low, attended], axis=1))
    query_low_all = latents_all[:, :q_rank]
    latent_low_all = latents_all[:, q_rank : q_rank + kv_rank]
    attended_all = latents_all[:, q_rank + kv_rank :]
    h_one_cols = column_shares(h_one[:, None, :], devices)[:, 0]
    middle = inputs + depth_scale * matmul(attended, weight_out)
    normed_two, inverse_two = normalize(middle)
    h_two = (normed_two * gain_two.astype(jnp.float32)).astype(jnp.bfloat16)
    gate_up = matmul(h_two, weight_gate_up)
    gate = gate_up[:, :ffn]
    upward = gate_up[:, ffn:]
    sigma = jax.nn.sigmoid(gate)
    hidden = (gate * sigma * upward).astype(jnp.bfloat16)
    result = (middle + depth_scale * matmul(hidden, weight_down)) * valid_rows
    output = result.astype(jnp.bfloat16).reshape(tokens.shape)
    grad_out = cotangent.reshape(rows, width).astype(jnp.float32) * valid_rows
    grad_feed = (depth_scale * grad_out).astype(jnp.bfloat16)
    feed_all = lax.all_gather(jnp.stack([h_two, grad_feed]), AXES, axis=1, tiled=True)
    h_two_all = feed_all[0]
    grad_feed_all = feed_all[1]
    grad_hidden = back_product(grad_feed, weight_down)
    grad_gate = (grad_hidden * upward * sigma * (1.0 + gate * (1.0 - sigma))).astype(jnp.bfloat16)
    grad_up = (grad_hidden * gate * sigma).astype(jnp.bfloat16)
    grad_h_two = back_product(jnp.concatenate([grad_gate, grad_up], axis=1), weight_gate_up)
    gain_two_term, grad_middle_norm = norm_back(grad_h_two, normed_two, inverse_two, gain_two)
    grad_middle = grad_out + grad_middle_norm
    grad_attn = (depth_scale * grad_middle).astype(jnp.bfloat16)
    ff_share = ffn // devices
    attn_share = width // devices
    feed_cols = column_shares(
        jnp.concatenate(
            [
                jnp.stack([hidden, grad_gate, grad_up], axis=1)
                .reshape(rows, 3, devices, ff_share)
                .transpose(0, 2, 1, 3)
                .reshape(rows, devices, 3 * ff_share),
                grad_attn.reshape(rows, devices, attn_share),
            ],
            axis=2,
        ).reshape(rows, 1, devices * (3 * ff_share + attn_share)),
        devices,
    )[:, 0]
    down_grad = rows_product(feed_cols[:, :ff_share], grad_feed_all)
    gate_up_cols = rows_product(h_two_all, feed_cols[:, ff_share : 3 * ff_share])
    out_cols = rows_product(attended_all, feed_cols[:, 3 * ff_share :])
    wide_rows = rows_from_columns(
        jnp.concatenate([gate_up_cols, out_cols], axis=1)[:, None, :], devices
    ).reshape(width // devices, devices, 2 * ff_share + attn_share)
    gate_grad = wide_rows[:, :, :ff_share].reshape(width // devices, ffn)
    up_grad = wide_rows[:, :, ff_share : 2 * ff_share].reshape(width // devices, ffn)
    output_weight_grad = wide_rows[:, :, 2 * ff_share :].reshape(width // devices, width)
    grad_heads = (
        back_product(grad_attn, weight_out).astype(jnp.bfloat16).reshape(micro, slot, HEADS, VDIM)
    )
    probs_again = jnp.exp(scores - log_total)
    grad_values = jnp.einsum(
        "mhqk,mqhd->mkhd",
        probs_again.astype(jnp.bfloat16),
        grad_heads,
        preferred_element_type=jnp.float32,
    )
    grad_probs = jnp.einsum(
        "mqhd,mkhd->mhqk", grad_heads, values, preferred_element_type=jnp.float32
    )
    inner = jnp.sum(probs_again * grad_probs, axis=-1, keepdims=True)
    grad_scores = (probs_again * (grad_probs - inner)).astype(jnp.bfloat16)
    grad_queries = scale * jnp.einsum(
        "mhqk,mkhd->mqhd", grad_scores, keys, preferred_element_type=jnp.float32
    )
    grad_keys = scale * jnp.einsum(
        "mhqk,mqhd->mkhd", grad_scores, queries, preferred_element_type=jnp.float32
    )
    grad_query_raw = jnp.concatenate(
        [grad_queries[..., :NOPE], rotate_back(grad_queries[..., NOPE:], cosines, sines)], axis=-1
    )
    grad_query_raw = grad_query_raw.reshape(rows, HEADS * (NOPE + ROPE)).astype(jnp.bfloat16)
    grad_query_low = back_product(grad_query_raw, up_query)
    grad_kv = (
        jnp.concatenate([grad_keys[..., :NOPE], grad_values], axis=-1)
        .reshape(rows, HEADS * (NOPE + VDIM))
        .astype(jnp.bfloat16)
    )
    grad_latent_low = back_product(grad_kv, up_latent)
    latent_gain_term, grad_latent = norm_back(
        grad_latent_low, normed_latent, inverse_latent, gain_latent
    )
    grad_key_rope = rotate_back(
        jnp.sum(grad_keys[..., NOPE:], axis=2, keepdims=True), cosines, sines
    ).reshape(rows, ROPE)
    grad_latent_all = jnp.concatenate([grad_latent, grad_key_rope], axis=-1).astype(jnp.bfloat16)
    query_gain_term, grad_latent_query = norm_back(
        grad_query_low, normed_query, inverse_query, gain_query
    )
    grad_latent_query = grad_latent_query.astype(jnp.bfloat16)
    query_width = up_query.shape[1]
    kv_width = up_latent.shape[1]
    up_cols = column_shares(
        jnp.concatenate(
            [
                grad_query_raw.reshape(rows, devices, query_width // devices),
                grad_kv.reshape(rows, devices, kv_width // devices),
            ],
            axis=2,
        ).reshape(rows, 1, query_width + kv_width),
        devices,
    )[:, 0]
    query_cols = query_width // devices
    query_up_cols = rows_product(query_low_all, up_cols[:, :query_cols])
    latent_up_cols = rows_product(latent_low_all, up_cols[:, query_cols:])
    grad_h_one = back_product(grad_latent_all, down_latent) + back_product(
        grad_latent_query, down_query
    )
    gain_one_term, grad_input_norm = norm_back(grad_h_one, normed_one, inverse_one, gain_one)
    input_grad = (grad_middle + grad_input_norm).reshape(tokens.shape)
    gain_terms = jnp.concatenate([gain_one_term, query_gain_term, latent_gain_term, gain_two_term])
    high, low = split_exact(gain_terms)
    down_grads = jnp.concatenate([grad_latent_all, grad_latent_query], axis=1)
    grad_width = down_grads.shape[1]
    gain_rows = -(-(2 * gain_terms.size) // grad_width)
    gain_block = jnp.pad(
        jnp.concatenate([high, low]), (0, gain_rows * grad_width - 2 * gain_terms.size)
    ).reshape(gain_rows, grad_width)
    last_all = lax.all_gather(
        jnp.concatenate([down_grads, gain_block], axis=0), AXES, axis=0, tiled=False
    )
    down_grads_all = last_all[:, :rows].reshape(devices * rows, grad_width)
    gain_parts = last_all[:, rows:].reshape(devices, gain_rows * grad_width)[:, : 2 * gain_terms.size]
    gain_sums = jnp.sum(
        gain_parts[:, : gain_terms.size].astype(jnp.float32)
        + gain_parts[:, gain_terms.size :].astype(jnp.float32),
        axis=0,
    )
    latent_width = grad_latent_all.shape[1]
    latent_down_grad = rows_product(h_one_cols, down_grads_all[:, :latent_width])
    query_down_grad = rows_product(h_one_cols, down_grads_all[:, latent_width:])
    up_rows = rows_from_columns(
        jnp.concatenate(
            [
                query_up_cols.reshape(devices, -1),
                latent_up_cols.reshape(devices, -1),
            ],
            axis=1,
        ).reshape(devices, 1, -1),
        devices,
    )
    q_rows = up_query.shape[0] // devices
    kv_rows = up_latent.shape[0] // devices
    kv_cols = kv_width // devices
    up_rows = up_rows.reshape(devices, -1)
    query_up_grad = (
        up_rows[:, : q_rows * query_cols]
        .reshape(devices, q_rows, query_cols)
        .transpose(1, 0, 2)
        .reshape(q_rows, query_width)
    )
    latent_up_grad = (
        up_rows[:, q_rows * query_cols :]
        .reshape(devices, kv_rows, kv_cols)
        .transpose(1, 0, 2)
        .reshape(kv_rows, kv_width)
    )

    def own(vector, offset, size):
        share = size // devices
        return lax.dynamic_slice(vector, (offset + me * share,), (share,))

    d_model = gain_one_term.size
    attn_gain_grad = own(gain_sums, 0, d_model)
    query_gain_grad = own(gain_sums, d_model, q_rank)
    latent_gain_grad = own(gain_sums, d_model + q_rank, kv_rank)
    feed_gain_grad = own(gain_sums, d_model + q_rank + kv_rank, d_model)
    return (
        output,
        input_grad,
        attn_gain_grad,
        query_down_grad,
        query_gain_grad,
        query_up_grad,
        latent_down_grad,
        latent_gain_grad,
        latent_up_grad,
        output_weight_grad,
        feed_gain_grad,
        gate_grad,
        up_grad,
        down_grad,
    )


def solution(mesh):
    placed = (
        P(None, ("fsdp", "dp"), None, None),
        P(None, ("fsdp", "dp")),
        P(("fsdp", "dp")),
        P(("fsdp", "dp"), None),
        P(("fsdp", "dp")),
        P(("fsdp", "dp"), None),
        P(("fsdp", "dp"), None),
        P(("fsdp", "dp")),
        P(("fsdp", "dp"), None),
        P(("fsdp", "dp"), None),
        P(("fsdp", "dp")),
        P(("fsdp", "dp"), None),
        P(("fsdp", "dp"), None),
        P(("fsdp", "dp"), None),
        P(None, ("fsdp", "dp"), None, None),
    )
    return jax.shard_map(
        local,
        mesh=mesh,
        in_specs=placed,
        out_specs=(
            P(None, ("fsdp", "dp"), None, None),
            P(None, ("fsdp", "dp"), None, None),
            P(("fsdp", "dp")),
            P(("fsdp", "dp"), None),
            P(("fsdp", "dp")),
            P(("fsdp", "dp"), None),
            P(("fsdp", "dp"), None),
            P(("fsdp", "dp")),
            P(("fsdp", "dp"), None),
            P(("fsdp", "dp"), None),
            P(("fsdp", "dp")),
            P(("fsdp", "dp"), None),
            P(("fsdp", "dp"), None),
            P(("fsdp", "dp"), None),
        ),
        check_vma=False,
    )
```

```python
import math

import jax
import jax.numpy as jnp
from jax import lax
from jax.sharding import PartitionSpec as P

HEADS = 40
NOPE = 64
ROPE = 32
VDIM = 64
KVRANK = 256


epsilon = 1e-05
depth_scale = 1.4 / math.sqrt(62.0)
masked_score = -1e30
AXES = ("fsdp", "dp")
LANES = 128


def matmul(left, right):
    return jnp.dot(left, right, preferred_element_type=jnp.float32)


def rows_product(left, right):
    return lax.dot_general(
        left, right, (((0,), (0,)), ((), ())), preferred_element_type=jnp.float32
    )


def back_product(left, right):
    return lax.dot_general(
        left, right, (((1,), (1,)), ((), ())), preferred_element_type=jnp.float32
    )


def normalize(values):
    inverse = lax.rsqrt(jnp.mean(values * values, axis=-1, keepdims=True) + epsilon)
    return (values * inverse, inverse)


def norm_back(grad, normed, inverse, gain):
    scaled = grad * gain.astype(jnp.float32)
    gain_grad = jnp.sum(grad * normed, axis=0)
    inner = jnp.mean(scaled * normed, axis=-1, keepdims=True)
    return (gain_grad, inverse * (scaled - normed * inner))


def rotate(values, cosines, sines):
    half = values.shape[-1] // 2
    first = values[..., :half]
    second = values[..., half:]
    return jnp.concatenate(
        [first * cosines - second * sines, second * cosines + first * sines], axis=-1
    )


def rotate_back(grad, cosines, sines):
    half = grad.shape[-1] // 2
    first = grad[..., :half]
    second = grad[..., half:]
    return jnp.concatenate(
        [first * cosines + second * sines, second * cosines - first * sines], axis=-1
    )


def padded(size):
    return -(-size // LANES) * LANES


def gather_packed(shards):
    flat = []
    for shard in shards:
        piece = shard.reshape(-1)
        flat.append(jnp.pad(piece, (0, padded(piece.size) - piece.size)))
    gathered = lax.all_gather(jnp.concatenate(flat), AXES, axis=0, tiled=False)
    devices = gathered.shape[0]
    results = []
    offset = 0
    for shard in shards:
        piece = gathered[:, offset : offset + shard.size]
        results.append(piece.reshape((devices * shard.shape[0],) + shard.shape[1:]))
        offset = offset + padded(shard.size)
    return results


def gather_tokens(values):
    return lax.all_gather(values, AXES, axis=0, tiled=True)


def column_shares(stacked, devices):
    tokens, count, width = stacked.shape
    blocks = stacked.reshape(tokens, count, devices, width // devices)
    moved = lax.all_to_all(blocks, AXES, 2, 0, tiled=True)
    return moved.reshape(devices * tokens, count, width // devices)


def rows_from_columns(grad, devices):
    rows, count, share = grad.shape
    moved = lax.all_to_all(grad, AXES, 0, 2, tiled=True)
    return moved.reshape(rows // devices, count, devices, share).reshape(
        rows // devices, count, devices * share
    )


def split_exact(values):
    high = lax.reduce_precision(values, exponent_bits=8, mantissa_bits=7)
    return (high.astype(jnp.bfloat16), (values - high).astype(jnp.bfloat16))


def local(
    tokens,
    lengths,
    attn_gain,
    query_down,
    query_gain,
    query_up,
    latent_down,
    latent_gain,
    latent_up,
    output_weight,
    feed_gain,
    gate_weight,
    up_weight,
    down_weight,
    cotangent,
):
    micro, _, slot, width = tokens.shape
    rows = micro * slot
    devices = lax.axis_size(AXES)
    me = lax.axis_index(AXES)
    ffn = gate_weight.shape[1]
    attn_shards = (
        query_down,
        query_up,
        latent_down,
        latent_up,
        output_weight,
        attn_gain,
        query_gain,
        latent_gain,
        feed_gain,
    )
    (
        down_query,
        up_query,
        down_latent,
        up_latent,
        weight_out,
        gain_one,
        gain_query,
        gain_latent,
        gain_two,
    ) = gather_packed(attn_shards)
    weight_gate_up = lax.all_gather(
        jnp.concatenate([gate_weight, up_weight], axis=1), AXES, axis=0, tiled=True
    )
    weight_down = lax.all_gather(down_weight, AXES, axis=0, tiled=True)
    half = ROPE // 2
    freqs = 10000.0 ** (-(2.0 * jnp.arange(half, dtype=jnp.float32)) / ROPE)
    angles = jnp.arange(slot, dtype=jnp.float32)[:, None] * freqs[None, :]
    cosines = jnp.cos(angles)[:, None, :]
    sines = jnp.sin(angles)[:, None, :]
    positions = lax.broadcasted_iota(jnp.int32, (micro, slot), 1)
    valid_rows = (positions < lengths).astype(jnp.float32).reshape(rows, 1)
    query_pos = lax.broadcasted_iota(jnp.int32, (micro, 1, slot, slot), 2)
    key_pos = lax.broadcasted_iota(jnp.int32, (micro, 1, slot, slot), 3)
    allowed = (key_pos <= query_pos) & (key_pos < lengths[:, :, None, None])
    scale = 1.0 / math.sqrt(NOPE + ROPE)
    inputs = tokens.reshape(rows, width).astype(jnp.float32)
    normed_one, inverse_one = normalize(inputs)
    h_one = (normed_one * gain_one.astype(jnp.float32)).astype(jnp.bfloat16)
    latent_query = matmul(h_one, down_query)
    normed_query, inverse_query = normalize(latent_query)
    query_low = (normed_query * gain_query.astype(jnp.float32)).astype(jnp.bfloat16)
    query_raw = matmul(query_low, up_query).reshape(micro, slot, HEADS, NOPE + ROPE)
    queries = jnp.concatenate(
        [query_raw[..., :NOPE], rotate(query_raw[..., NOPE:], cosines, sines)], axis=-1
    ).astype(jnp.bfloat16)
    latent_all = matmul(h_one, down_latent)
    normed_latent, inverse_latent = normalize(latent_all[:, :KVRANK])
    latent_low = (normed_latent * gain_latent.astype(jnp.float32)).astype(jnp.bfloat16)
    kv_raw = matmul(latent_low, up_latent).reshape(micro, slot, HEADS, NOPE + VDIM)
    key_rope = rotate(latent_all[:, KVRANK:].reshape(micro, slot, 1, ROPE), cosines, sines)
    keys = jnp.concatenate(
        [kv_raw[..., :NOPE], jnp.broadcast_to(key_rope, (micro, slot, HEADS, ROPE))], axis=-1
    ).astype(jnp.bfloat16)
    values = kv_raw[..., NOPE:].astype(jnp.bfloat16)
    raw = jnp.einsum("mqhd,mkhd->mhqk", queries, keys, preferred_element_type=jnp.float32)
    scores = jnp.where(allowed, raw * scale, masked_score)
    top = jnp.max(scores, axis=-1, keepdims=True)
    expo = jnp.exp(scores - top)
    total = jnp.sum(expo, axis=-1, keepdims=True)
    probs = expo / total
    log_total = top + jnp.log(total)
    attended = jnp.einsum(
        "mhqk,mkhd->mqhd", probs.astype(jnp.bfloat16), values, preferred_element_type=jnp.float32
    )
    attended = attended.reshape(rows, HEADS * VDIM).astype(jnp.bfloat16)
    q_rank = query_low.shape[1]
    kv_rank = latent_low.shape[1]
    latents_all = gather_tokens(jnp.concatenate([query_low, latent_low, attended], axis=1))
    query_low_all = latents_all[:, :q_rank]
    latent_low_all = latents_all[:, q_rank : q_rank + kv_rank]
    attended_all = latents_all[:, q_rank + kv_rank :]
    middle = inputs + depth_scale * matmul(attended, weight_out)
    normed_two, inverse_two = normalize(middle)
    h_two = (normed_two * gain_two.astype(jnp.float32)).astype(jnp.bfloat16)
    gate_up = matmul(h_two, weight_gate_up)
    gate = gate_up[:, :ffn]
    upward = gate_up[:, ffn:]
    sigma = jax.nn.sigmoid(gate)
    hidden = (gate * sigma * upward).astype(jnp.bfloat16)
    result = (middle + depth_scale * matmul(hidden, weight_down)) * valid_rows
    output = result.astype(jnp.bfloat16).reshape(tokens.shape)
    grad_out = cotangent.reshape(rows, width).astype(jnp.float32) * valid_rows
    grad_feed = (depth_scale * grad_out).astype(jnp.bfloat16)
    feed_all = lax.all_gather(jnp.stack([h_two, grad_feed]), AXES, axis=1, tiled=True)
    h_two_all = feed_all[0]
    grad_feed_all = feed_all[1]
    grad_hidden = back_product(grad_feed, weight_down)
    grad_gate = (grad_hidden * upward * sigma * (1.0 + gate * (1.0 - sigma))).astype(jnp.bfloat16)
    grad_up = (grad_hidden * gate * sigma).astype(jnp.bfloat16)
    grad_h_two = back_product(jnp.concatenate([grad_gate, grad_up], axis=1), weight_gate_up)
    gain_two_term, grad_middle_norm = norm_back(grad_h_two, normed_two, inverse_two, gain_two)
    grad_middle = grad_out + grad_middle_norm
    grad_attn = (depth_scale * grad_middle).astype(jnp.bfloat16)
    ff_share = ffn // devices
    attn_share = width // devices
    gate_c = matmul(h_two_all, lax.dynamic_slice_in_dim(weight_gate_up, me * ff_share, ff_share, 1))
    up_c = matmul(
        h_two_all, lax.dynamic_slice_in_dim(weight_gate_up, ffn + me * ff_share, ff_share, 1)
    )
    sigma_c = jax.nn.sigmoid(gate_c)
    hidden_c = (gate_c * sigma_c * up_c).astype(jnp.bfloat16)
    grad_hidden_c = back_product(grad_feed_all, down_weight)
    grad_gate_c = (grad_hidden_c * up_c * sigma_c * (1.0 + gate_c * (1.0 - sigma_c))).astype(
        jnp.bfloat16
    )
    grad_up_c = (grad_hidden_c * gate_c * sigma_c).astype(jnp.bfloat16)
    down_grad = rows_product(hidden_c, grad_feed_all)
    gate_up_cols = rows_product(h_two_all, jnp.concatenate([grad_gate_c, grad_up_c], axis=1))
    inner_cols = column_shares(jnp.stack([h_one, grad_attn], axis=1), devices)
    h_one_cols = inner_cols[:, 0]
    out_cols = rows_product(attended_all, inner_cols[:, 1])
    wide_rows = rows_from_columns(
        jnp.concatenate([gate_up_cols, out_cols], axis=1)[:, None, :], devices
    ).reshape(width // devices, devices, 2 * ff_share + attn_share)
    gate_grad = wide_rows[:, :, :ff_share].reshape(width // devices, ffn)
    up_grad = wide_rows[:, :, ff_share : 2 * ff_share].reshape(width // devices, ffn)
    output_weight_grad = wide_rows[:, :, 2 * ff_share :].reshape(width // devices, width)
    grad_heads = (
        back_product(grad_attn, weight_out).astype(jnp.bfloat16).reshape(micro, slot, HEADS, VDIM)
    )
    probs_again = jnp.exp(scores - log_total)
    grad_values = jnp.einsum(
        "mhqk,mqhd->mkhd",
        probs_again.astype(jnp.bfloat16),
        grad_heads,
        preferred_element_type=jnp.float32,
    )
    grad_probs = jnp.einsum(
        "mqhd,mkhd->mhqk", grad_heads, values, preferred_element_type=jnp.float32
    )
    inner = jnp.sum(probs_again * grad_probs, axis=-1, keepdims=True)
    grad_scores = (probs_again * (grad_probs - inner)).astype(jnp.bfloat16)
    grad_queries = scale * jnp.einsum(
        "mhqk,mkhd->mqhd", grad_scores, keys, preferred_element_type=jnp.float32
    )
    grad_keys = scale * jnp.einsum(
        "mhqk,mqhd->mkhd", grad_scores, queries, preferred_element_type=jnp.float32
    )
    grad_query_raw = jnp.concatenate(
        [grad_queries[..., :NOPE], rotate_back(grad_queries[..., NOPE:], cosines, sines)], axis=-1
    )
    grad_query_raw = grad_query_raw.reshape(rows, HEADS * (NOPE + ROPE)).astype(jnp.bfloat16)
    grad_query_low = back_product(grad_query_raw, up_query)
    grad_kv = (
        jnp.concatenate([grad_keys[..., :NOPE], grad_values], axis=-1)
        .reshape(rows, HEADS * (NOPE + VDIM))
        .astype(jnp.bfloat16)
    )
    grad_latent_low = back_product(grad_kv, up_latent)
    latent_gain_term, grad_latent = norm_back(
        grad_latent_low, normed_latent, inverse_latent, gain_latent
    )
    grad_key_rope = rotate_back(
        jnp.sum(grad_keys[..., NOPE:], axis=2, keepdims=True), cosines, sines
    ).reshape(rows, ROPE)
    grad_latent_all = jnp.concatenate([grad_latent, grad_key_rope], axis=-1).astype(jnp.bfloat16)
    query_gain_term, grad_latent_query = norm_back(
        grad_query_low, normed_query, inverse_query, gain_query
    )
    grad_latent_query = grad_latent_query.astype(jnp.bfloat16)
    query_width = up_query.shape[1]
    kv_width = up_latent.shape[1]
    up_cols = column_shares(
        jnp.concatenate(
            [
                grad_query_raw.reshape(rows, devices, query_width // devices),
                grad_kv.reshape(rows, devices, kv_width // devices),
            ],
            axis=2,
        ).reshape(rows, 1, query_width + kv_width),
        devices,
    )[:, 0]
    query_cols = query_width // devices
    query_up_cols = rows_product(query_low_all, up_cols[:, :query_cols])
    latent_up_cols = rows_product(latent_low_all, up_cols[:, query_cols:])
    grad_h_one = back_product(grad_latent_all, down_latent) + back_product(
        grad_latent_query, down_query
    )
    gain_one_term, grad_input_norm = norm_back(grad_h_one, normed_one, inverse_one, gain_one)
    input_grad = (grad_middle + grad_input_norm).reshape(tokens.shape)
    gain_terms = jnp.concatenate([gain_one_term, query_gain_term, latent_gain_term, gain_two_term])
    high, low = split_exact(gain_terms)
    down_grads = jnp.concatenate([grad_latent_all, grad_latent_query], axis=1)
    grad_width = down_grads.shape[1]
    gain_rows = -(-(2 * gain_terms.size) // grad_width)
    gain_block = jnp.pad(
        jnp.concatenate([high, low]), (0, gain_rows * grad_width - 2 * gain_terms.size)
    ).reshape(gain_rows, grad_width)
    last_all = lax.all_gather(
        jnp.concatenate([down_grads, gain_block], axis=0), AXES, axis=0, tiled=False
    )
    down_grads_all = last_all[:, :rows].reshape(devices * rows, grad_width)
    gain_parts = last_all[:, rows:].reshape(devices, gain_rows * grad_width)[:, : 2 * gain_terms.size]
    gain_sums = jnp.sum(
        gain_parts[:, : gain_terms.size].astype(jnp.float32)
        + gain_parts[:, gain_terms.size :].astype(jnp.float32),
        axis=0,
    )
    latent_width = grad_latent_all.shape[1]
    latent_down_grad = rows_product(h_one_cols, down_grads_all[:, :latent_width])
    query_down_grad = rows_product(h_one_cols, down_grads_all[:, latent_width:])
    up_rows = rows_from_columns(
        jnp.concatenate(
            [
                query_up_cols.reshape(devices, -1),
                latent_up_cols.reshape(devices, -1),
            ],
            axis=1,
        ).reshape(devices, 1, -1),
        devices,
    )
    q_rows = up_query.shape[0] // devices
    kv_rows = up_latent.shape[0] // devices
    kv_cols = kv_width // devices
    up_rows = up_rows.reshape(devices, -1)
    query_up_grad = (
        up_rows[:, : q_rows * query_cols]
        .reshape(devices, q_rows, query_cols)
        .transpose(1, 0, 2)
        .reshape(q_rows, query_width)
    )
    latent_up_grad = (
        up_rows[:, q_rows * query_cols :]
        .reshape(devices, kv_rows, kv_cols)
        .transpose(1, 0, 2)
        .reshape(kv_rows, kv_width)
    )

    def own(vector, offset, size):
        share = size // devices
        return lax.dynamic_slice(vector, (offset + me * share,), (share,))

    d_model = gain_one_term.size
    attn_gain_grad = own(gain_sums, 0, d_model)
    query_gain_grad = own(gain_sums, d_model, q_rank)
    latent_gain_grad = own(gain_sums, d_model + q_rank, kv_rank)
    feed_gain_grad = own(gain_sums, d_model + q_rank + kv_rank, d_model)
    return (
        output,
        input_grad,
        attn_gain_grad,
        query_down_grad,
        query_gain_grad,
        query_up_grad,
        latent_down_grad,
        latent_gain_grad,
        latent_up_grad,
        output_weight_grad,
        feed_gain_grad,
        gate_grad,
        up_grad,
        down_grad,
    )


def solution(mesh):
    placed = (
        P(None, ("fsdp", "dp"), None, None),
        P(None, ("fsdp", "dp")),
        P(("fsdp", "dp")),
        P(("fsdp", "dp"), None),
        P(("fsdp", "dp")),
        P(("fsdp", "dp"), None),
        P(("fsdp", "dp"), None),
        P(("fsdp", "dp")),
        P(("fsdp", "dp"), None),
        P(("fsdp", "dp"), None),
        P(("fsdp", "dp")),
        P(("fsdp", "dp"), None),
        P(("fsdp", "dp"), None),
        P(("fsdp", "dp"), None),
        P(None, ("fsdp", "dp"), None, None),
    )
    return jax.shard_map(
        local,
        mesh=mesh,
        in_specs=placed,
        out_specs=(
            P(None, ("fsdp", "dp"), None, None),
            P(None, ("fsdp", "dp"), None, None),
            P(("fsdp", "dp")),
            P(("fsdp", "dp"), None),
            P(("fsdp", "dp")),
            P(("fsdp", "dp"), None),
            P(("fsdp", "dp"), None),
            P(("fsdp", "dp")),
            P(("fsdp", "dp"), None),
            P(("fsdp", "dp"), None),
            P(("fsdp", "dp")),
            P(("fsdp", "dp"), None),
            P(("fsdp", "dp"), None),
            P(("fsdp", "dp"), None),
        ),
        check_vma=False,
    )
```

```python
import math

import jax
import jax.numpy as jnp
from jax import lax
from jax.sharding import PartitionSpec as P

HEADS = 40
NOPE = 64
ROPE = 32
VDIM = 64
KVRANK = 256


epsilon = 1e-05
depth_scale = 1.4 / math.sqrt(62.0)
masked_score = -1e30
AXES = ("fsdp", "dp")
LANES = 128


def matmul(left, right):
    return jnp.dot(left, right, preferred_element_type=jnp.float32)


def rows_product(left, right):
    return lax.dot_general(
        left, right, (((0,), (0,)), ((), ())), preferred_element_type=jnp.float32
    )


def back_product(left, right):
    return lax.dot_general(
        left, right, (((1,), (1,)), ((), ())), preferred_element_type=jnp.float32
    )


def normalize(values):
    inverse = lax.rsqrt(jnp.mean(values * values, axis=-1, keepdims=True) + epsilon)
    return (values * inverse, inverse)


def norm_back(grad, normed, inverse, gain):
    scaled = grad * gain.astype(jnp.float32)
    gain_grad = jnp.sum(grad * normed, axis=0)
    inner = jnp.mean(scaled * normed, axis=-1, keepdims=True)
    return (gain_grad, inverse * (scaled - normed * inner))


def rotate(values, cosines, sines):
    half = values.shape[-1] // 2
    first = values[..., :half]
    second = values[..., half:]
    return jnp.concatenate(
        [first * cosines - second * sines, second * cosines + first * sines], axis=-1
    )


def rotate_back(grad, cosines, sines):
    half = grad.shape[-1] // 2
    first = grad[..., :half]
    second = grad[..., half:]
    return jnp.concatenate(
        [first * cosines + second * sines, second * cosines - first * sines], axis=-1
    )


def padded(size):
    return -(-size // LANES) * LANES


def gather_packed(shards):
    flat = []
    for shard in shards:
        piece = shard.reshape(-1)
        flat.append(jnp.pad(piece, (0, padded(piece.size) - piece.size)))
    gathered = lax.all_gather(jnp.concatenate(flat), AXES, axis=0, tiled=False)
    devices = gathered.shape[0]
    results = []
    offset = 0
    for shard in shards:
        piece = gathered[:, offset : offset + shard.size]
        results.append(piece.reshape((devices * shard.shape[0],) + shard.shape[1:]))
        offset = offset + padded(shard.size)
    return results


def gather_tokens(values):
    return lax.all_gather(values, AXES, axis=0, tiled=True)


def column_shares(stacked, devices):
    tokens, count, width = stacked.shape
    blocks = stacked.reshape(tokens, count, devices, width // devices)
    moved = lax.all_to_all(blocks, AXES, 2, 0, tiled=True)
    return moved.reshape(devices * tokens, count, width // devices)


def rows_from_columns(grad, devices):
    rows, count, share = grad.shape
    moved = lax.all_to_all(grad, AXES, 0, 2, tiled=True)
    return moved.reshape(rows // devices, count, devices, share).reshape(
        rows // devices, count, devices * share
    )


def split_exact(values):
    high = lax.reduce_precision(values, exponent_bits=8, mantissa_bits=7)
    return (high.astype(jnp.bfloat16), (values - high).astype(jnp.bfloat16))


def local(
    tokens,
    lengths,
    attn_gain,
    query_down,
    query_gain,
    query_up,
    latent_down,
    latent_gain,
    latent_up,
    output_weight,
    feed_gain,
    gate_weight,
    up_weight,
    down_weight,
    cotangent,
):
    micro, _, slot, width = tokens.shape
    rows = micro * slot
    devices = lax.axis_size(AXES)
    me = lax.axis_index(AXES)
    ffn = gate_weight.shape[1]
    attn_shards = (
        query_down,
        query_up,
        latent_down,
        latent_up,
        output_weight,
        attn_gain,
        query_gain,
        latent_gain,
        feed_gain,
    )
    (
        down_query,
        up_query,
        down_latent,
        up_latent,
        weight_out,
        gain_one,
        gain_query,
        gain_latent,
        gain_two,
    ) = gather_packed(attn_shards)
    weight_gate_up = lax.all_gather(
        jnp.concatenate([gate_weight, up_weight], axis=1), AXES, axis=0, tiled=True
    )
    weight_down = lax.all_gather(down_weight, AXES, axis=0, tiled=True)
    half = ROPE // 2
    freqs = 10000.0 ** (-(2.0 * jnp.arange(half, dtype=jnp.float32)) / ROPE)
    angles = jnp.arange(slot, dtype=jnp.float32)[:, None] * freqs[None, :]
    cosines = jnp.cos(angles)[:, None, :]
    sines = jnp.sin(angles)[:, None, :]
    positions = lax.broadcasted_iota(jnp.int32, (micro, slot), 1)
    valid_rows = (positions < lengths).astype(jnp.float32).reshape(rows, 1)
    query_pos = lax.broadcasted_iota(jnp.int32, (micro, 1, slot, slot), 2)
    key_pos = lax.broadcasted_iota(jnp.int32, (micro, 1, slot, slot), 3)
    allowed = (key_pos <= query_pos) & (key_pos < lengths[:, :, None, None])
    scale = 1.0 / math.sqrt(NOPE + ROPE)
    inputs = tokens.reshape(rows, width).astype(jnp.float32)
    normed_one, inverse_one = normalize(inputs)
    h_one = (normed_one * gain_one.astype(jnp.float32)).astype(jnp.bfloat16)
    latent_query = matmul(h_one, down_query)
    normed_query, inverse_query = normalize(latent_query)
    query_low = (normed_query * gain_query.astype(jnp.float32)).astype(jnp.bfloat16)
    query_raw = matmul(query_low, up_query).reshape(micro, slot, HEADS, NOPE + ROPE)
    queries = jnp.concatenate(
        [query_raw[..., :NOPE], rotate(query_raw[..., NOPE:], cosines, sines)], axis=-1
    ).astype(jnp.bfloat16)
    latent_all = matmul(h_one, down_latent)
    normed_latent, inverse_latent = normalize(latent_all[:, :KVRANK])
    latent_low = (normed_latent * gain_latent.astype(jnp.float32)).astype(jnp.bfloat16)
    kv_raw = matmul(latent_low, up_latent).reshape(micro, slot, HEADS, NOPE + VDIM)
    key_rope = rotate(latent_all[:, KVRANK:].reshape(micro, slot, 1, ROPE), cosines, sines)
    keys = jnp.concatenate(
        [kv_raw[..., :NOPE], jnp.broadcast_to(key_rope, (micro, slot, HEADS, ROPE))], axis=-1
    ).astype(jnp.bfloat16)
    values = kv_raw[..., NOPE:].astype(jnp.bfloat16)
    raw = jnp.einsum("mqhd,mkhd->mhqk", queries, keys, preferred_element_type=jnp.float32)
    scores = jnp.where(allowed, raw * scale, masked_score)
    top = jnp.max(scores, axis=-1, keepdims=True)
    expo = jnp.exp(scores - top)
    total = jnp.sum(expo, axis=-1, keepdims=True)
    probs = expo / total
    log_total = top + jnp.log(total)
    attended = jnp.einsum(
        "mhqk,mkhd->mqhd", probs.astype(jnp.bfloat16), values, preferred_element_type=jnp.float32
    )
    attended = attended.reshape(rows, HEADS * VDIM).astype(jnp.bfloat16)
    q_rank = query_low.shape[1]
    kv_rank = latent_low.shape[1]
    latent_src = jnp.concatenate([query_low, latent_low, attended], axis=1)
    middle = inputs + depth_scale * matmul(attended, weight_out)
    normed_two, inverse_two = normalize(middle)
    h_two = (normed_two * gain_two.astype(jnp.float32)).astype(jnp.bfloat16)
    gate_up = matmul(h_two, weight_gate_up)
    gate = gate_up[:, :ffn]
    upward = gate_up[:, ffn:]
    sigma = jax.nn.sigmoid(gate)
    hidden = (gate * sigma * upward).astype(jnp.bfloat16)
    result = (middle + depth_scale * matmul(hidden, weight_down)) * valid_rows
    output = result.astype(jnp.bfloat16).reshape(tokens.shape)
    grad_out = cotangent.reshape(rows, width).astype(jnp.float32) * valid_rows
    grad_feed = (depth_scale * grad_out).astype(jnp.bfloat16)
    feed_all = lax.all_gather(jnp.stack([h_two, grad_feed]), AXES, axis=1, tiled=True)
    latent_src, feed_all = lax.optimization_barrier((latent_src, feed_all))
    latents_all = gather_tokens(latent_src)
    query_low_all = latents_all[:, :q_rank]
    latent_low_all = latents_all[:, q_rank : q_rank + kv_rank]
    attended_all = latents_all[:, q_rank + kv_rank :]
    h_two_all = feed_all[0]
    grad_feed_all = feed_all[1]
    grad_hidden = back_product(grad_feed, weight_down)
    grad_gate = (grad_hidden * upward * sigma * (1.0 + gate * (1.0 - sigma))).astype(jnp.bfloat16)
    grad_up = (grad_hidden * gate * sigma).astype(jnp.bfloat16)
    grad_h_two = back_product(jnp.concatenate([grad_gate, grad_up], axis=1), weight_gate_up)
    gain_two_term, grad_middle_norm = norm_back(grad_h_two, normed_two, inverse_two, gain_two)
    grad_middle = grad_out + grad_middle_norm
    grad_attn = (depth_scale * grad_middle).astype(jnp.bfloat16)
    ff_share = ffn // devices
    attn_share = width // devices
    gate_c = matmul(h_two_all, lax.dynamic_slice_in_dim(weight_gate_up, me * ff_share, ff_share, 1))
    up_c = matmul(
        h_two_all, lax.dynamic_slice_in_dim(weight_gate_up, ffn + me * ff_share, ff_share, 1)
    )
    sigma_c = jax.nn.sigmoid(gate_c)
    hidden_c = (gate_c * sigma_c * up_c).astype(jnp.bfloat16)
    grad_hidden_c = back_product(grad_feed_all, down_weight)
    grad_gate_c = (grad_hidden_c * up_c * sigma_c * (1.0 + gate_c * (1.0 - sigma_c))).astype(
        jnp.bfloat16
    )
    grad_up_c = (grad_hidden_c * gate_c * sigma_c).astype(jnp.bfloat16)
    down_grad = rows_product(hidden_c, grad_feed_all)
    gate_up_cols = rows_product(h_two_all, jnp.concatenate([grad_gate_c, grad_up_c], axis=1))
    inner_cols = column_shares(jnp.stack([h_one, grad_attn], axis=1), devices)
    h_one_cols = inner_cols[:, 0]
    out_cols = rows_product(attended_all, inner_cols[:, 1])
    wide_rows = rows_from_columns(
        jnp.concatenate([gate_up_cols, out_cols], axis=1)[:, None, :], devices
    ).reshape(width // devices, devices, 2 * ff_share + attn_share)
    gate_grad = wide_rows[:, :, :ff_share].reshape(width // devices, ffn)
    up_grad = wide_rows[:, :, ff_share : 2 * ff_share].reshape(width // devices, ffn)
    output_weight_grad = wide_rows[:, :, 2 * ff_share :].reshape(width // devices, width)
    grad_heads = (
        back_product(grad_attn, weight_out).astype(jnp.bfloat16).reshape(micro, slot, HEADS, VDIM)
    )
    probs_again = jnp.exp(scores - log_total)
    grad_values = jnp.einsum(
        "mhqk,mqhd->mkhd",
        probs_again.astype(jnp.bfloat16),
        grad_heads,
        preferred_element_type=jnp.float32,
    )
    grad_probs = jnp.einsum(
        "mqhd,mkhd->mhqk", grad_heads, values, preferred_element_type=jnp.float32
    )
    inner = jnp.sum(probs_again * grad_probs, axis=-1, keepdims=True)
    grad_scores = (probs_again * (grad_probs - inner)).astype(jnp.bfloat16)
    grad_queries = scale * jnp.einsum(
        "mhqk,mkhd->mqhd", grad_scores, keys, preferred_element_type=jnp.float32
    )
    grad_keys = scale * jnp.einsum(
        "mhqk,mqhd->mkhd", grad_scores, queries, preferred_element_type=jnp.float32
    )
    grad_query_raw = jnp.concatenate(
        [grad_queries[..., :NOPE], rotate_back(grad_queries[..., NOPE:], cosines, sines)], axis=-1
    )
    grad_query_raw = grad_query_raw.reshape(rows, HEADS * (NOPE + ROPE)).astype(jnp.bfloat16)
    grad_query_low = back_product(grad_query_raw, up_query)
    grad_kv = (
        jnp.concatenate([grad_keys[..., :NOPE], grad_values], axis=-1)
        .reshape(rows, HEADS * (NOPE + VDIM))
        .astype(jnp.bfloat16)
    )
    grad_latent_low = back_product(grad_kv, up_latent)
    latent_gain_term, grad_latent = norm_back(
        grad_latent_low, normed_latent, inverse_latent, gain_latent
    )
    grad_key_rope = rotate_back(
        jnp.sum(grad_keys[..., NOPE:], axis=2, keepdims=True), cosines, sines
    ).reshape(rows, ROPE)
    grad_latent_all = jnp.concatenate([grad_latent, grad_key_rope], axis=-1).astype(jnp.bfloat16)
    query_gain_term, grad_latent_query = norm_back(
        grad_query_low, normed_query, inverse_query, gain_query
    )
    grad_latent_query = grad_latent_query.astype(jnp.bfloat16)
    query_width = up_query.shape[1]
    kv_width = up_latent.shape[1]
    up_cols = column_shares(
        jnp.concatenate(
            [
                grad_query_raw.reshape(rows, devices, query_width // devices),
                grad_kv.reshape(rows, devices, kv_width // devices),
            ],
            axis=2,
        ).reshape(rows, 1, query_width + kv_width),
        devices,
    )[:, 0]
    query_cols = query_width // devices
    query_up_cols = rows_product(query_low_all, up_cols[:, :query_cols])
    latent_up_cols = rows_product(latent_low_all, up_cols[:, query_cols:])
    grad_h_one = back_product(grad_latent_all, down_latent) + back_product(
        grad_latent_query, down_query
    )
    gain_one_term, grad_input_norm = norm_back(grad_h_one, normed_one, inverse_one, gain_one)
    input_grad = (grad_middle + grad_input_norm).reshape(tokens.shape)
    gain_terms = jnp.concatenate([gain_one_term, query_gain_term, latent_gain_term, gain_two_term])
    high, low = split_exact(gain_terms)
    down_grads = jnp.concatenate([grad_latent_all, grad_latent_query], axis=1)
    grad_width = down_grads.shape[1]
    gain_rows = -(-(2 * gain_terms.size) // grad_width)
    gain_block = jnp.pad(
        jnp.concatenate([high, low]), (0, gain_rows * grad_width - 2 * gain_terms.size)
    ).reshape(gain_rows, grad_width)
    last_all = lax.all_gather(
        jnp.concatenate([down_grads, gain_block], axis=0), AXES, axis=0, tiled=False
    )
    down_grads_all = last_all[:, :rows].reshape(devices * rows, grad_width)
    gain_parts = last_all[:, rows:].reshape(devices, gain_rows * grad_width)[:, : 2 * gain_terms.size]
    gain_sums = jnp.sum(
        gain_parts[:, : gain_terms.size].astype(jnp.float32)
        + gain_parts[:, gain_terms.size :].astype(jnp.float32),
        axis=0,
    )
    latent_width = grad_latent_all.shape[1]
    latent_down_grad = rows_product(h_one_cols, down_grads_all[:, :latent_width])
    query_down_grad = rows_product(h_one_cols, down_grads_all[:, latent_width:])
    up_rows = rows_from_columns(
        jnp.concatenate(
            [
                query_up_cols.reshape(devices, -1),
                latent_up_cols.reshape(devices, -1),
            ],
            axis=1,
        ).reshape(devices, 1, -1),
        devices,
    )
    q_rows = up_query.shape[0] // devices
    kv_rows = up_latent.shape[0] // devices
    kv_cols = kv_width // devices
    up_rows = up_rows.reshape(devices, -1)
    query_up_grad = (
        up_rows[:, : q_rows * query_cols]
        .reshape(devices, q_rows, query_cols)
        .transpose(1, 0, 2)
        .reshape(q_rows, query_width)
    )
    latent_up_grad = (
        up_rows[:, q_rows * query_cols :]
        .reshape(devices, kv_rows, kv_cols)
        .transpose(1, 0, 2)
        .reshape(kv_rows, kv_width)
    )

    def own(vector, offset, size):
        share = size // devices
        return lax.dynamic_slice(vector, (offset + me * share,), (share,))

    d_model = gain_one_term.size
    attn_gain_grad = own(gain_sums, 0, d_model)
    query_gain_grad = own(gain_sums, d_model, q_rank)
    latent_gain_grad = own(gain_sums, d_model + q_rank, kv_rank)
    feed_gain_grad = own(gain_sums, d_model + q_rank + kv_rank, d_model)
    return (
        output,
        input_grad,
        attn_gain_grad,
        query_down_grad,
        query_gain_grad,
        query_up_grad,
        latent_down_grad,
        latent_gain_grad,
        latent_up_grad,
        output_weight_grad,
        feed_gain_grad,
        gate_grad,
        up_grad,
        down_grad,
    )


def solution(mesh):
    placed = (
        P(None, ("fsdp", "dp"), None, None),
        P(None, ("fsdp", "dp")),
        P(("fsdp", "dp")),
        P(("fsdp", "dp"), None),
        P(("fsdp", "dp")),
        P(("fsdp", "dp"), None),
        P(("fsdp", "dp"), None),
        P(("fsdp", "dp")),
        P(("fsdp", "dp"), None),
        P(("fsdp", "dp"), None),
        P(("fsdp", "dp")),
        P(("fsdp", "dp"), None),
        P(("fsdp", "dp"), None),
        P(("fsdp", "dp"), None),
        P(None, ("fsdp", "dp"), None, None),
    )
    return jax.shard_map(
        local,
        mesh=mesh,
        in_specs=placed,
        out_specs=(
            P(None, ("fsdp", "dp"), None, None),
            P(None, ("fsdp", "dp"), None, None),
            P(("fsdp", "dp")),
            P(("fsdp", "dp"), None),
            P(("fsdp", "dp")),
            P(("fsdp", "dp"), None),
            P(("fsdp", "dp"), None),
            P(("fsdp", "dp")),
            P(("fsdp", "dp"), None),
            P(("fsdp", "dp"), None),
            P(("fsdp", "dp")),
            P(("fsdp", "dp"), None),
            P(("fsdp", "dp"), None),
            P(("fsdp", "dp"), None),
        ),
        check_vma=False,
    )
```

```python
import math

import jax
import jax.numpy as jnp
from jax import lax
from jax.sharding import PartitionSpec as P

HEADS = 40
NOPE = 64
ROPE = 32
VDIM = 64
KVRANK = 256


epsilon = 1e-05
depth_scale = 1.4 / math.sqrt(62.0)
masked_score = -1e30
AXES = ("fsdp", "dp")
LANES = 128


def matmul(left, right):
    return jnp.dot(left, right, preferred_element_type=jnp.float32)


def rows_product(left, right):
    return lax.dot_general(
        left, right, (((0,), (0,)), ((), ())), preferred_element_type=jnp.float32
    )


def back_product(left, right):
    return lax.dot_general(
        left, right, (((1,), (1,)), ((), ())), preferred_element_type=jnp.float32
    )


def normalize(values):
    inverse = lax.rsqrt(jnp.mean(values * values, axis=-1, keepdims=True) + epsilon)
    return (values * inverse, inverse)


def norm_back(grad, normed, inverse, gain):
    scaled = grad * gain.astype(jnp.float32)
    gain_grad = jnp.sum(grad * normed, axis=0)
    inner = jnp.mean(scaled * normed, axis=-1, keepdims=True)
    return (gain_grad, inverse * (scaled - normed * inner))


def rotate(values, cosines, sines):
    half = values.shape[-1] // 2
    first = values[..., :half]
    second = values[..., half:]
    return jnp.concatenate(
        [first * cosines - second * sines, second * cosines + first * sines], axis=-1
    )


def rotate_back(grad, cosines, sines):
    half = grad.shape[-1] // 2
    first = grad[..., :half]
    second = grad[..., half:]
    return jnp.concatenate(
        [first * cosines + second * sines, second * cosines - first * sines], axis=-1
    )


def padded(size):
    return -(-size // LANES) * LANES


def gather_packed(shards):
    flat = []
    for shard in shards:
        piece = shard.reshape(-1)
        flat.append(jnp.pad(piece, (0, padded(piece.size) - piece.size)))
    gathered = lax.all_gather(jnp.concatenate(flat), AXES, axis=0, tiled=False)
    devices = gathered.shape[0]
    results = []
    offset = 0
    for shard in shards:
        piece = gathered[:, offset : offset + shard.size]
        results.append(piece.reshape((devices * shard.shape[0],) + shard.shape[1:]))
        offset = offset + padded(shard.size)
    return results


def gather_tokens(values):
    return lax.all_gather(values, AXES, axis=0, tiled=True)


def column_shares(stacked, devices):
    tokens, count, width = stacked.shape
    blocks = stacked.reshape(tokens, count, devices, width // devices)
    moved = lax.all_to_all(blocks, AXES, 2, 0, tiled=True)
    return moved.reshape(devices * tokens, count, width // devices)


def rows_from_columns(grad, devices):
    rows, count, share = grad.shape
    moved = lax.all_to_all(grad, AXES, 0, 2, tiled=True)
    return moved.reshape(rows // devices, count, devices, share).reshape(
        rows // devices, count, devices * share
    )


def split_exact(values):
    high = lax.reduce_precision(values, exponent_bits=8, mantissa_bits=7)
    return (high.astype(jnp.bfloat16), (values - high).astype(jnp.bfloat16))


def local(
    tokens,
    lengths,
    attn_gain,
    query_down,
    query_gain,
    query_up,
    latent_down,
    latent_gain,
    latent_up,
    output_weight,
    feed_gain,
    gate_weight,
    up_weight,
    down_weight,
    cotangent,
):
    micro, _, slot, width = tokens.shape
    rows = micro * slot
    devices = lax.axis_size(AXES)
    me = lax.axis_index(AXES)
    ffn = gate_weight.shape[1]
    attn_shards = (
        query_down,
        query_up,
        latent_down,
        latent_up,
        output_weight,
        attn_gain,
        query_gain,
        latent_gain,
        feed_gain,
    )
    (
        down_query,
        up_query,
        down_latent,
        up_latent,
        weight_out,
        gain_one,
        gain_query,
        gain_latent,
        gain_two,
    ) = gather_packed(attn_shards)
    weight_gate_up, weight_down = gather_packed(
        (jnp.concatenate([gate_weight, up_weight], axis=1), down_weight)
    )
    half = ROPE // 2
    freqs = 10000.0 ** (-(2.0 * jnp.arange(half, dtype=jnp.float32)) / ROPE)
    angles = jnp.arange(slot, dtype=jnp.float32)[:, None] * freqs[None, :]
    cosines = jnp.cos(angles)[:, None, :]
    sines = jnp.sin(angles)[:, None, :]
    positions = lax.broadcasted_iota(jnp.int32, (micro, slot), 1)
    valid_rows = (positions < lengths).astype(jnp.float32).reshape(rows, 1)
    query_pos = lax.broadcasted_iota(jnp.int32, (micro, 1, slot, slot), 2)
    key_pos = lax.broadcasted_iota(jnp.int32, (micro, 1, slot, slot), 3)
    allowed = (key_pos <= query_pos) & (key_pos < lengths[:, :, None, None])
    scale = 1.0 / math.sqrt(NOPE + ROPE)
    inputs = tokens.reshape(rows, width).astype(jnp.float32)
    normed_one, inverse_one = normalize(inputs)
    h_one = (normed_one * gain_one.astype(jnp.float32)).astype(jnp.bfloat16)
    latent_query = matmul(h_one, down_query)
    normed_query, inverse_query = normalize(latent_query)
    query_low = (normed_query * gain_query.astype(jnp.float32)).astype(jnp.bfloat16)
    query_raw = matmul(query_low, up_query).reshape(micro, slot, HEADS, NOPE + ROPE)
    queries = jnp.concatenate(
        [query_raw[..., :NOPE], rotate(query_raw[..., NOPE:], cosines, sines)], axis=-1
    ).astype(jnp.bfloat16)
    latent_all = matmul(h_one, down_latent)
    normed_latent, inverse_latent = normalize(latent_all[:, :KVRANK])
    latent_low = (normed_latent * gain_latent.astype(jnp.float32)).astype(jnp.bfloat16)
    kv_raw = matmul(latent_low, up_latent).reshape(micro, slot, HEADS, NOPE + VDIM)
    key_rope = rotate(latent_all[:, KVRANK:].reshape(micro, slot, 1, ROPE), cosines, sines)
    keys = jnp.concatenate(
        [kv_raw[..., :NOPE], jnp.broadcast_to(key_rope, (micro, slot, HEADS, ROPE))], axis=-1
    ).astype(jnp.bfloat16)
    values = kv_raw[..., NOPE:].astype(jnp.bfloat16)
    raw = jnp.einsum("mqhd,mkhd->mhqk", queries, keys, preferred_element_type=jnp.float32)
    scores = jnp.where(allowed, raw * scale, masked_score)
    top = jnp.max(scores, axis=-1, keepdims=True)
    expo = jnp.exp(scores - top)
    total = jnp.sum(expo, axis=-1, keepdims=True)
    probs = expo / total
    log_total = top + jnp.log(total)
    attended = jnp.einsum(
        "mhqk,mkhd->mqhd", probs.astype(jnp.bfloat16), values, preferred_element_type=jnp.float32
    )
    attended = attended.reshape(rows, HEADS * VDIM).astype(jnp.bfloat16)
    q_rank = query_low.shape[1]
    kv_rank = latent_low.shape[1]
    middle = inputs + depth_scale * matmul(attended, weight_out)
    normed_two, inverse_two = normalize(middle)
    h_two = (normed_two * gain_two.astype(jnp.float32)).astype(jnp.bfloat16)
    gate_up = matmul(h_two, weight_gate_up)
    gate = gate_up[:, :ffn]
    upward = gate_up[:, ffn:]
    sigma = jax.nn.sigmoid(gate)
    hidden = (gate * sigma * upward).astype(jnp.bfloat16)
    result = (middle + depth_scale * matmul(hidden, weight_down)) * valid_rows
    output = result.astype(jnp.bfloat16).reshape(tokens.shape)
    grad_out = cotangent.reshape(rows, width).astype(jnp.float32) * valid_rows
    grad_feed = (depth_scale * grad_out).astype(jnp.bfloat16)
    latents_all = gather_tokens(
        jnp.concatenate([query_low, latent_low, attended, h_two], axis=1)
    )
    query_low_all = latents_all[:, :q_rank]
    latent_low_all = latents_all[:, q_rank : q_rank + kv_rank]
    attended_all = latents_all[:, q_rank + kv_rank : q_rank + kv_rank + width]
    h_two_all = latents_all[:, q_rank + kv_rank + width :]
    grad_feed_late, latents_all = lax.optimization_barrier((grad_feed, latents_all))
    grad_feed_all = gather_tokens(grad_feed_late)
    grad_hidden = back_product(grad_feed, weight_down)
    grad_gate = (grad_hidden * upward * sigma * (1.0 + gate * (1.0 - sigma))).astype(jnp.bfloat16)
    grad_up = (grad_hidden * gate * sigma).astype(jnp.bfloat16)
    grad_h_two = back_product(jnp.concatenate([grad_gate, grad_up], axis=1), weight_gate_up)
    gain_two_term, grad_middle_norm = norm_back(grad_h_two, normed_two, inverse_two, gain_two)
    grad_middle = grad_out + grad_middle_norm
    grad_attn = (depth_scale * grad_middle).astype(jnp.bfloat16)
    ff_share = ffn // devices
    attn_share = width // devices
    gate_c = matmul(h_two_all, lax.dynamic_slice_in_dim(weight_gate_up, me * ff_share, ff_share, 1))
    up_c = matmul(
        h_two_all, lax.dynamic_slice_in_dim(weight_gate_up, ffn + me * ff_share, ff_share, 1)
    )
    sigma_c = jax.nn.sigmoid(gate_c)
    hidden_c = (gate_c * sigma_c * up_c).astype(jnp.bfloat16)
    grad_hidden_c = back_product(grad_feed_all, down_weight)
    grad_gate_c = (grad_hidden_c * up_c * sigma_c * (1.0 + gate_c * (1.0 - sigma_c))).astype(
        jnp.bfloat16
    )
    grad_up_c = (grad_hidden_c * gate_c * sigma_c).astype(jnp.bfloat16)
    down_grad = rows_product(hidden_c, grad_feed_all)
    gate_up_cols = rows_product(h_two_all, jnp.concatenate([grad_gate_c, grad_up_c], axis=1))
    inner_cols = column_shares(jnp.stack([h_one, grad_attn], axis=1), devices)
    h_one_cols = inner_cols[:, 0]
    out_cols = rows_product(attended_all, inner_cols[:, 1])
    wide_rows = rows_from_columns(
        jnp.concatenate([gate_up_cols, out_cols], axis=1)[:, None, :], devices
    ).reshape(width // devices, devices, 2 * ff_share + attn_share)
    gate_grad = wide_rows[:, :, :ff_share].reshape(width // devices, ffn)
    up_grad = wide_rows[:, :, ff_share : 2 * ff_share].reshape(width // devices, ffn)
    output_weight_grad = wide_rows[:, :, 2 * ff_share :].reshape(width // devices, width)
    grad_heads = (
        back_product(grad_attn, weight_out).astype(jnp.bfloat16).reshape(micro, slot, HEADS, VDIM)
    )
    probs_again = jnp.exp(scores - log_total)
    grad_values = jnp.einsum(
        "mhqk,mqhd->mkhd",
        probs_again.astype(jnp.bfloat16),
        grad_heads,
        preferred_element_type=jnp.float32,
    )
    grad_probs = jnp.einsum(
        "mqhd,mkhd->mhqk", grad_heads, values, preferred_element_type=jnp.float32
    )
    inner = jnp.sum(probs_again * grad_probs, axis=-1, keepdims=True)
    grad_scores = (probs_again * (grad_probs - inner)).astype(jnp.bfloat16)
    grad_queries = scale * jnp.einsum(
        "mhqk,mkhd->mqhd", grad_scores, keys, preferred_element_type=jnp.float32
    )
    grad_keys = scale * jnp.einsum(
        "mhqk,mqhd->mkhd", grad_scores, queries, preferred_element_type=jnp.float32
    )
    grad_query_raw = jnp.concatenate(
        [grad_queries[..., :NOPE], rotate_back(grad_queries[..., NOPE:], cosines, sines)], axis=-1
    )
    grad_query_raw = grad_query_raw.reshape(rows, HEADS * (NOPE + ROPE)).astype(jnp.bfloat16)
    grad_query_low = back_product(grad_query_raw, up_query)
    grad_kv = (
        jnp.concatenate([grad_keys[..., :NOPE], grad_values], axis=-1)
        .reshape(rows, HEADS * (NOPE + VDIM))
        .astype(jnp.bfloat16)
    )
    grad_latent_low = back_product(grad_kv, up_latent)
    latent_gain_term, grad_latent = norm_back(
        grad_latent_low, normed_latent, inverse_latent, gain_latent
    )
    grad_key_rope = rotate_back(
        jnp.sum(grad_keys[..., NOPE:], axis=2, keepdims=True), cosines, sines
    ).reshape(rows, ROPE)
    grad_latent_all = jnp.concatenate([grad_latent, grad_key_rope], axis=-1).astype(jnp.bfloat16)
    query_gain_term, grad_latent_query = norm_back(
        grad_query_low, normed_query, inverse_query, gain_query
    )
    grad_latent_query = grad_latent_query.astype(jnp.bfloat16)
    query_width = up_query.shape[1]
    kv_width = up_latent.shape[1]
    up_cols = column_shares(
        jnp.concatenate(
            [
                grad_query_raw.reshape(rows, devices, query_width // devices),
                grad_kv.reshape(rows, devices, kv_width // devices),
            ],
            axis=2,
        ).reshape(rows, 1, query_width + kv_width),
        devices,
    )[:, 0]
    query_cols = query_width // devices
    query_up_cols = rows_product(query_low_all, up_cols[:, :query_cols])
    latent_up_cols = rows_product(latent_low_all, up_cols[:, query_cols:])
    grad_h_one = back_product(grad_latent_all, down_latent) + back_product(
        grad_latent_query, down_query
    )
    gain_one_term, grad_input_norm = norm_back(grad_h_one, normed_one, inverse_one, gain_one)
    input_grad = (grad_middle + grad_input_norm).reshape(tokens.shape)
    gain_terms = jnp.concatenate([gain_one_term, query_gain_term, latent_gain_term, gain_two_term])
    high, low = split_exact(gain_terms)
    down_grads = jnp.concatenate([grad_latent_all, grad_latent_query], axis=1)
    grad_width = down_grads.shape[1]
    gain_rows = -(-(2 * gain_terms.size) // grad_width)
    gain_block = jnp.pad(
        jnp.concatenate([high, low]), (0, gain_rows * grad_width - 2 * gain_terms.size)
    ).reshape(gain_rows, grad_width)
    last_all = lax.all_gather(
        jnp.concatenate([down_grads, gain_block], axis=0), AXES, axis=0, tiled=False
    )
    down_grads_all = last_all[:, :rows].reshape(devices * rows, grad_width)
    gain_parts = last_all[:, rows:].reshape(devices, gain_rows * grad_width)[:, : 2 * gain_terms.size]
    gain_sums = jnp.sum(
        gain_parts[:, : gain_terms.size].astype(jnp.float32)
        + gain_parts[:, gain_terms.size :].astype(jnp.float32),
        axis=0,
    )
    latent_width = grad_latent_all.shape[1]
    latent_down_grad = rows_product(h_one_cols, down_grads_all[:, :latent_width])
    query_down_grad = rows_product(h_one_cols, down_grads_all[:, latent_width:])
    up_rows = rows_from_columns(
        jnp.concatenate(
            [
                query_up_cols.reshape(devices, -1),
                latent_up_cols.reshape(devices, -1),
            ],
            axis=1,
        ).reshape(devices, 1, -1),
        devices,
    )
    q_rows = up_query.shape[0] // devices
    kv_rows = up_latent.shape[0] // devices
    kv_cols = kv_width // devices
    up_rows = up_rows.reshape(devices, -1)
    query_up_grad = (
        up_rows[:, : q_rows * query_cols]
        .reshape(devices, q_rows, query_cols)
        .transpose(1, 0, 2)
        .reshape(q_rows, query_width)
    )
    latent_up_grad = (
        up_rows[:, q_rows * query_cols :]
        .reshape(devices, kv_rows, kv_cols)
        .transpose(1, 0, 2)
        .reshape(kv_rows, kv_width)
    )

    def own(vector, offset, size):
        share = size // devices
        return lax.dynamic_slice(vector, (offset + me * share,), (share,))

    d_model = gain_one_term.size
    attn_gain_grad = own(gain_sums, 0, d_model)
    query_gain_grad = own(gain_sums, d_model, q_rank)
    latent_gain_grad = own(gain_sums, d_model + q_rank, kv_rank)
    feed_gain_grad = own(gain_sums, d_model + q_rank + kv_rank, d_model)
    return (
        output,
        input_grad,
        attn_gain_grad,
        query_down_grad,
        query_gain_grad,
        query_up_grad,
        latent_down_grad,
        latent_gain_grad,
        latent_up_grad,
        output_weight_grad,
        feed_gain_grad,
        gate_grad,
        up_grad,
        down_grad,
    )


def solution(mesh):
    placed = (
        P(None, ("fsdp", "dp"), None, None),
        P(None, ("fsdp", "dp")),
        P(("fsdp", "dp")),
        P(("fsdp", "dp"), None),
        P(("fsdp", "dp")),
        P(("fsdp", "dp"), None),
        P(("fsdp", "dp"), None),
        P(("fsdp", "dp")),
        P(("fsdp", "dp"), None),
        P(("fsdp", "dp"), None),
        P(("fsdp", "dp")),
        P(("fsdp", "dp"), None),
        P(("fsdp", "dp"), None),
        P(("fsdp", "dp"), None),
        P(None, ("fsdp", "dp"), None, None),
    )
    return jax.shard_map(
        local,
        mesh=mesh,
        in_specs=placed,
        out_specs=(
            P(None, ("fsdp", "dp"), None, None),
            P(None, ("fsdp", "dp"), None, None),
            P(("fsdp", "dp")),
            P(("fsdp", "dp"), None),
            P(("fsdp", "dp")),
            P(("fsdp", "dp"), None),
            P(("fsdp", "dp"), None),
            P(("fsdp", "dp")),
            P(("fsdp", "dp"), None),
            P(("fsdp", "dp"), None),
            P(("fsdp", "dp")),
            P(("fsdp", "dp"), None),
            P(("fsdp", "dp"), None),
            P(("fsdp", "dp"), None),
        ),
        check_vma=False,
    )
```

```python
import math

import jax
import jax.numpy as jnp
from jax import lax
from jax.sharding import PartitionSpec as P

HEADS = 40
NOPE = 64
ROPE = 32
VDIM = 64
KVRANK = 256


epsilon = 1e-05
depth_scale = 1.4 / math.sqrt(62.0)
masked_score = -1e30
AXES = ("fsdp", "dp")
LANES = 128


def matmul(left, right):
    return jnp.dot(left, right, preferred_element_type=jnp.float32)


def rows_product(left, right):
    return lax.dot_general(
        left, right, (((0,), (0,)), ((), ())), preferred_element_type=jnp.float32
    )


def back_product(left, right):
    return lax.dot_general(
        left, right, (((1,), (1,)), ((), ())), preferred_element_type=jnp.float32
    )


def normalize(values):
    inverse = lax.rsqrt(jnp.mean(values * values, axis=-1, keepdims=True) + epsilon)
    return (values * inverse, inverse)


def norm_back(grad, normed, inverse, gain):
    scaled = grad * gain.astype(jnp.float32)
    gain_grad = jnp.sum(grad * normed, axis=0)
    inner = jnp.mean(scaled * normed, axis=-1, keepdims=True)
    return (gain_grad, inverse * (scaled - normed * inner))


def rotate(values, cosines, sines):
    half = values.shape[-1] // 2
    first = values[..., :half]
    second = values[..., half:]
    return jnp.concatenate(
        [first * cosines - second * sines, second * cosines + first * sines], axis=-1
    )


def rotate_back(grad, cosines, sines):
    half = grad.shape[-1] // 2
    first = grad[..., :half]
    second = grad[..., half:]
    return jnp.concatenate(
        [first * cosines + second * sines, second * cosines - first * sines], axis=-1
    )


def padded(size):
    return -(-size // LANES) * LANES


def gather_packed(shards):
    flat = []
    for shard in shards:
        piece = shard.reshape(-1)
        flat.append(jnp.pad(piece, (0, padded(piece.size) - piece.size)))
    gathered = lax.all_gather(jnp.concatenate(flat), AXES, axis=0, tiled=False)
    devices = gathered.shape[0]
    results = []
    offset = 0
    for shard in shards:
        piece = gathered[:, offset : offset + shard.size]
        results.append(piece.reshape((devices * shard.shape[0],) + shard.shape[1:]))
        offset = offset + padded(shard.size)
    return results


def gather_tokens(values):
    return lax.all_gather(values, AXES, axis=0, tiled=True)


def column_shares(stacked, devices):
    tokens, count, width = stacked.shape
    blocks = stacked.reshape(tokens, count, devices, width // devices)
    moved = lax.all_to_all(blocks, AXES, 2, 0, tiled=True)
    return moved.reshape(devices * tokens, count, width // devices)


def rows_from_columns(grad, devices):
    rows, count, share = grad.shape
    moved = lax.all_to_all(grad, AXES, 0, 2, tiled=True)
    return moved.reshape(rows // devices, count, devices, share).reshape(
        rows // devices, count, devices * share
    )


def split_exact(values):
    high = lax.reduce_precision(values, exponent_bits=8, mantissa_bits=7)
    return (high.astype(jnp.bfloat16), (values - high).astype(jnp.bfloat16))


def local(
    tokens,
    lengths,
    attn_gain,
    query_down,
    query_gain,
    query_up,
    latent_down,
    latent_gain,
    latent_up,
    output_weight,
    feed_gain,
    gate_weight,
    up_weight,
    down_weight,
    cotangent,
):
    micro, _, slot, width = tokens.shape
    rows = micro * slot
    devices = lax.axis_size(AXES)
    me = lax.axis_index(AXES)
    ffn = gate_weight.shape[1]
    attn_shards = (
        query_down,
        query_up,
        latent_down,
        latent_up,
        output_weight,
        attn_gain,
        query_gain,
        latent_gain,
        feed_gain,
    )
    (
        down_query,
        up_query,
        down_latent,
        up_latent,
        weight_out,
        gain_one,
        gain_query,
        gain_latent,
        gain_two,
    ) = gather_packed(attn_shards)
    weight_gate_up = lax.all_gather(
        jnp.concatenate([gate_weight, up_weight], axis=1), AXES, axis=0, tiled=True
    )
    weight_down = lax.all_gather(down_weight, AXES, axis=0, tiled=True)
    half = ROPE // 2
    freqs = 10000.0 ** (-(2.0 * jnp.arange(half, dtype=jnp.float32)) / ROPE)
    angles = jnp.arange(slot, dtype=jnp.float32)[:, None] * freqs[None, :]
    cosines = jnp.cos(angles)[:, None, :]
    sines = jnp.sin(angles)[:, None, :]
    positions = lax.broadcasted_iota(jnp.int32, (micro, slot), 1)
    valid_rows = (positions < lengths).astype(jnp.float32).reshape(rows, 1)
    query_pos = lax.broadcasted_iota(jnp.int32, (micro, 1, slot, slot), 2)
    key_pos = lax.broadcasted_iota(jnp.int32, (micro, 1, slot, slot), 3)
    allowed = (key_pos <= query_pos) & (key_pos < lengths[:, :, None, None])
    scale = 1.0 / math.sqrt(NOPE + ROPE)
    inputs = tokens.reshape(rows, width).astype(jnp.float32)
    normed_one, inverse_one = normalize(inputs)
    h_one = (normed_one * gain_one.astype(jnp.float32)).astype(jnp.bfloat16)
    latent_query = matmul(h_one, down_query)
    normed_query, inverse_query = normalize(latent_query)
    query_low = (normed_query * gain_query.astype(jnp.float32)).astype(jnp.bfloat16)
    query_raw = matmul(query_low, up_query).reshape(micro, slot, HEADS, NOPE + ROPE)
    queries = jnp.concatenate(
        [query_raw[..., :NOPE], rotate(query_raw[..., NOPE:], cosines, sines)], axis=-1
    ).astype(jnp.bfloat16)
    latent_all = matmul(h_one, down_latent)
    normed_latent, inverse_latent = normalize(latent_all[:, :KVRANK])
    latent_low = (normed_latent * gain_latent.astype(jnp.float32)).astype(jnp.bfloat16)
    kv_raw = matmul(latent_low, up_latent).reshape(micro, slot, HEADS, NOPE + VDIM)
    key_rope = rotate(latent_all[:, KVRANK:].reshape(micro, slot, 1, ROPE), cosines, sines)
    keys = jnp.concatenate(
        [kv_raw[..., :NOPE], jnp.broadcast_to(key_rope, (micro, slot, HEADS, ROPE))], axis=-1
    ).astype(jnp.bfloat16)
    values = kv_raw[..., NOPE:].astype(jnp.bfloat16)
    raw = jnp.einsum("mqhd,mkhd->mhqk", queries, keys, preferred_element_type=jnp.float32)
    scores = jnp.where(allowed, raw * scale, masked_score)
    top = jnp.max(scores, axis=-1, keepdims=True)
    expo = jnp.exp(scores - top)
    total = jnp.sum(expo, axis=-1, keepdims=True)
    probs = expo / total
    log_total = top + jnp.log(total)
    attended = jnp.einsum(
        "mhqk,mkhd->mqhd", probs.astype(jnp.bfloat16), values, preferred_element_type=jnp.float32
    )
    attended = attended.reshape(rows, HEADS * VDIM).astype(jnp.bfloat16)
    q_rank = query_low.shape[1]
    kv_rank = latent_low.shape[1]
    middle = inputs + depth_scale * matmul(attended, weight_out)
    normed_two, inverse_two = normalize(middle)
    h_two = (normed_two * gain_two.astype(jnp.float32)).astype(jnp.bfloat16)
    gate_up = matmul(h_two, weight_gate_up)
    gate = gate_up[:, :ffn]
    upward = gate_up[:, ffn:]
    sigma = jax.nn.sigmoid(gate)
    hidden = (gate * sigma * upward).astype(jnp.bfloat16)
    result = (middle + depth_scale * matmul(hidden, weight_down)) * valid_rows
    output = result.astype(jnp.bfloat16).reshape(tokens.shape)
    grad_out = cotangent.reshape(rows, width).astype(jnp.float32) * valid_rows
    grad_feed = (depth_scale * grad_out).astype(jnp.bfloat16)
    latents_all = gather_tokens(
        jnp.concatenate([query_low, latent_low, attended, h_two, grad_feed], axis=1)
    )
    query_low_all = latents_all[:, :q_rank]
    latent_low_all = latents_all[:, q_rank : q_rank + kv_rank]
    attended_all = latents_all[:, q_rank + kv_rank : q_rank + kv_rank + width]
    h_two_all = latents_all[:, q_rank + kv_rank + width : q_rank + kv_rank + 2 * width]
    grad_feed_all = latents_all[:, q_rank + kv_rank + 2 * width :]
    grad_hidden = back_product(grad_feed, weight_down)
    grad_gate = (grad_hidden * upward * sigma * (1.0 + gate * (1.0 - sigma))).astype(jnp.bfloat16)
    grad_up = (grad_hidden * gate * sigma).astype(jnp.bfloat16)
    grad_h_two = back_product(jnp.concatenate([grad_gate, grad_up], axis=1), weight_gate_up)
    gain_two_term, grad_middle_norm = norm_back(grad_h_two, normed_two, inverse_two, gain_two)
    grad_middle = grad_out + grad_middle_norm
    grad_attn = (depth_scale * grad_middle).astype(jnp.bfloat16)
    ff_share = ffn // devices
    attn_share = width // devices
    gate_c = matmul(h_two_all, lax.dynamic_slice_in_dim(weight_gate_up, me * ff_share, ff_share, 1))
    up_c = matmul(
        h_two_all, lax.dynamic_slice_in_dim(weight_gate_up, ffn + me * ff_share, ff_share, 1)
    )
    sigma_c = jax.nn.sigmoid(gate_c)
    hidden_c = (gate_c * sigma_c * up_c).astype(jnp.bfloat16)
    grad_hidden_c = back_product(grad_feed_all, down_weight)
    grad_gate_c = (grad_hidden_c * up_c * sigma_c * (1.0 + gate_c * (1.0 - sigma_c))).astype(
        jnp.bfloat16
    )
    grad_up_c = (grad_hidden_c * gate_c * sigma_c).astype(jnp.bfloat16)
    down_grad = rows_product(hidden_c, grad_feed_all)
    gate_up_cols = rows_product(h_two_all, jnp.concatenate([grad_gate_c, grad_up_c], axis=1))
    inner_cols = column_shares(jnp.stack([h_one, grad_attn], axis=1), devices)
    h_one_cols = inner_cols[:, 0]
    out_cols = rows_product(attended_all, inner_cols[:, 1])
    wide_rows = rows_from_columns(
        jnp.concatenate([gate_up_cols, out_cols], axis=1)[:, None, :], devices
    ).reshape(width // devices, devices, 2 * ff_share + attn_share)
    gate_grad = wide_rows[:, :, :ff_share].reshape(width // devices, ffn)
    up_grad = wide_rows[:, :, ff_share : 2 * ff_share].reshape(width // devices, ffn)
    output_weight_grad = wide_rows[:, :, 2 * ff_share :].reshape(width // devices, width)
    grad_heads = (
        back_product(grad_attn, weight_out).astype(jnp.bfloat16).reshape(micro, slot, HEADS, VDIM)
    )
    probs_again = jnp.exp(scores - log_total)
    grad_values = jnp.einsum(
        "mhqk,mqhd->mkhd",
        probs_again.astype(jnp.bfloat16),
        grad_heads,
        preferred_element_type=jnp.float32,
    )
    grad_probs = jnp.einsum(
        "mqhd,mkhd->mhqk", grad_heads, values, preferred_element_type=jnp.float32
    )
    inner = jnp.sum(probs_again * grad_probs, axis=-1, keepdims=True)
    grad_scores = (probs_again * (grad_probs - inner)).astype(jnp.bfloat16)
    grad_queries = scale * jnp.einsum(
        "mhqk,mkhd->mqhd", grad_scores, keys, preferred_element_type=jnp.float32
    )
    grad_keys = scale * jnp.einsum(
        "mhqk,mqhd->mkhd", grad_scores, queries, preferred_element_type=jnp.float32
    )
    grad_query_raw = jnp.concatenate(
        [grad_queries[..., :NOPE], rotate_back(grad_queries[..., NOPE:], cosines, sines)], axis=-1
    )
    grad_query_raw = grad_query_raw.reshape(rows, HEADS * (NOPE + ROPE)).astype(jnp.bfloat16)
    grad_query_low = back_product(grad_query_raw, up_query)
    grad_kv = (
        jnp.concatenate([grad_keys[..., :NOPE], grad_values], axis=-1)
        .reshape(rows, HEADS * (NOPE + VDIM))
        .astype(jnp.bfloat16)
    )
    grad_latent_low = back_product(grad_kv, up_latent)
    latent_gain_term, grad_latent = norm_back(
        grad_latent_low, normed_latent, inverse_latent, gain_latent
    )
    grad_key_rope = rotate_back(
        jnp.sum(grad_keys[..., NOPE:], axis=2, keepdims=True), cosines, sines
    ).reshape(rows, ROPE)
    grad_latent_all = jnp.concatenate([grad_latent, grad_key_rope], axis=-1).astype(jnp.bfloat16)
    query_gain_term, grad_latent_query = norm_back(
        grad_query_low, normed_query, inverse_query, gain_query
    )
    grad_latent_query = grad_latent_query.astype(jnp.bfloat16)
    query_width = up_query.shape[1]
    kv_width = up_latent.shape[1]
    up_cols = column_shares(
        jnp.concatenate(
            [
                grad_query_raw.reshape(rows, devices, query_width // devices),
                grad_kv.reshape(rows, devices, kv_width // devices),
            ],
            axis=2,
        ).reshape(rows, 1, query_width + kv_width),
        devices,
    )[:, 0]
    query_cols = query_width // devices
    query_up_cols = rows_product(query_low_all, up_cols[:, :query_cols])
    latent_up_cols = rows_product(latent_low_all, up_cols[:, query_cols:])
    grad_h_one = back_product(grad_latent_all, down_latent) + back_product(
        grad_latent_query, down_query
    )
    gain_one_term, grad_input_norm = norm_back(grad_h_one, normed_one, inverse_one, gain_one)
    input_grad = (grad_middle + grad_input_norm).reshape(tokens.shape)
    gain_terms = jnp.concatenate([gain_one_term, query_gain_term, latent_gain_term, gain_two_term])
    high, low = split_exact(gain_terms)
    down_grads = jnp.concatenate([grad_latent_all, grad_latent_query], axis=1)
    grad_width = down_grads.shape[1]
    gain_rows = -(-(2 * gain_terms.size) // grad_width)
    gain_block = jnp.pad(
        jnp.concatenate([high, low]), (0, gain_rows * grad_width - 2 * gain_terms.size)
    ).reshape(gain_rows, grad_width)
    last_all = lax.all_gather(
        jnp.concatenate([down_grads, gain_block], axis=0), AXES, axis=0, tiled=False
    )
    down_grads_all = last_all[:, :rows].reshape(devices * rows, grad_width)
    gain_parts = last_all[:, rows:].reshape(devices, gain_rows * grad_width)[:, : 2 * gain_terms.size]
    gain_sums = jnp.sum(
        gain_parts[:, : gain_terms.size].astype(jnp.float32)
        + gain_parts[:, gain_terms.size :].astype(jnp.float32),
        axis=0,
    )
    latent_width = grad_latent_all.shape[1]
    latent_down_grad = rows_product(h_one_cols, down_grads_all[:, :latent_width])
    query_down_grad = rows_product(h_one_cols, down_grads_all[:, latent_width:])
    up_rows = rows_from_columns(
        jnp.concatenate(
            [
                query_up_cols.reshape(devices, -1),
                latent_up_cols.reshape(devices, -1),
            ],
            axis=1,
        ).reshape(devices, 1, -1),
        devices,
    )
    q_rows = up_query.shape[0] // devices
    kv_rows = up_latent.shape[0] // devices
    kv_cols = kv_width // devices
    up_rows = up_rows.reshape(devices, -1)
    query_up_grad = (
        up_rows[:, : q_rows * query_cols]
        .reshape(devices, q_rows, query_cols)
        .transpose(1, 0, 2)
        .reshape(q_rows, query_width)
    )
    latent_up_grad = (
        up_rows[:, q_rows * query_cols :]
        .reshape(devices, kv_rows, kv_cols)
        .transpose(1, 0, 2)
        .reshape(kv_rows, kv_width)
    )

    def own(vector, offset, size):
        share = size // devices
        return lax.dynamic_slice(vector, (offset + me * share,), (share,))

    d_model = gain_one_term.size
    attn_gain_grad = own(gain_sums, 0, d_model)
    query_gain_grad = own(gain_sums, d_model, q_rank)
    latent_gain_grad = own(gain_sums, d_model + q_rank, kv_rank)
    feed_gain_grad = own(gain_sums, d_model + q_rank + kv_rank, d_model)
    return (
        output,
        input_grad,
        attn_gain_grad,
        query_down_grad,
        query_gain_grad,
        query_up_grad,
        latent_down_grad,
        latent_gain_grad,
        latent_up_grad,
        output_weight_grad,
        feed_gain_grad,
        gate_grad,
        up_grad,
        down_grad,
    )


def solution(mesh):
    placed = (
        P(None, ("fsdp", "dp"), None, None),
        P(None, ("fsdp", "dp")),
        P(("fsdp", "dp")),
        P(("fsdp", "dp"), None),
        P(("fsdp", "dp")),
        P(("fsdp", "dp"), None),
        P(("fsdp", "dp"), None),
        P(("fsdp", "dp")),
        P(("fsdp", "dp"), None),
        P(("fsdp", "dp"), None),
        P(("fsdp", "dp")),
        P(("fsdp", "dp"), None),
        P(("fsdp", "dp"), None),
        P(("fsdp", "dp"), None),
        P(None, ("fsdp", "dp"), None, None),
    )
    return jax.shard_map(
        local,
        mesh=mesh,
        in_specs=placed,
        out_specs=(
            P(None, ("fsdp", "dp"), None, None),
            P(None, ("fsdp", "dp"), None, None),
            P(("fsdp", "dp")),
            P(("fsdp", "dp"), None),
            P(("fsdp", "dp")),
            P(("fsdp", "dp"), None),
            P(("fsdp", "dp"), None),
            P(("fsdp", "dp")),
            P(("fsdp", "dp"), None),
            P(("fsdp", "dp"), None),
            P(("fsdp", "dp")),
            P(("fsdp", "dp"), None),
            P(("fsdp", "dp"), None),
            P(("fsdp", "dp"), None),
        ),
        check_vma=False,
    )
```

```python
import math

import jax
import jax.numpy as jnp
from jax import lax
from jax.sharding import PartitionSpec as P

HEADS = 40
NOPE = 64
ROPE = 32
VDIM = 64
KVRANK = 256


epsilon = 1e-05
depth_scale = 1.4 / math.sqrt(62.0)
masked_score = -1e30
AXES = ("fsdp", "dp")
LANES = 128


def matmul(left, right):
    return jnp.dot(left, right, preferred_element_type=jnp.float32)


def rows_product(left, right):
    return lax.dot_general(
        left, right, (((0,), (0,)), ((), ())), preferred_element_type=jnp.float32
    )


def back_product(left, right):
    return lax.dot_general(
        left, right, (((1,), (1,)), ((), ())), preferred_element_type=jnp.float32
    )


def normalize(values):
    inverse = lax.rsqrt(jnp.mean(values * values, axis=-1, keepdims=True) + epsilon)
    return (values * inverse, inverse)


def norm_back(grad, normed, inverse, gain):
    scaled = grad * gain.astype(jnp.float32)
    gain_grad = jnp.sum(grad * normed, axis=0)
    inner = jnp.mean(scaled * normed, axis=-1, keepdims=True)
    return (gain_grad, inverse * (scaled - normed * inner))


def rotate(values, cosines, sines):
    half = values.shape[-1] // 2
    first = values[..., :half]
    second = values[..., half:]
    return jnp.concatenate(
        [first * cosines - second * sines, second * cosines + first * sines], axis=-1
    )


def rotate_back(grad, cosines, sines):
    half = grad.shape[-1] // 2
    first = grad[..., :half]
    second = grad[..., half:]
    return jnp.concatenate(
        [first * cosines + second * sines, second * cosines - first * sines], axis=-1
    )


def padded(size):
    return -(-size // LANES) * LANES


def gather_packed(shards):
    flat = []
    for shard in shards:
        piece = shard.reshape(-1)
        flat.append(jnp.pad(piece, (0, padded(piece.size) - piece.size)))
    gathered = lax.all_gather(jnp.concatenate(flat), AXES, axis=0, tiled=False)
    devices = gathered.shape[0]
    results = []
    offset = 0
    for shard in shards:
        piece = gathered[:, offset : offset + shard.size]
        results.append(piece.reshape((devices * shard.shape[0],) + shard.shape[1:]))
        offset = offset + padded(shard.size)
    return results


def gather_tokens(values):
    return lax.all_gather(values, AXES, axis=0, tiled=True)


def column_shares(stacked, devices):
    tokens, count, width = stacked.shape
    blocks = stacked.reshape(tokens, count, devices, width // devices)
    moved = lax.all_to_all(blocks, AXES, 2, 0, tiled=True)
    return moved.reshape(devices * tokens, count, width // devices)


def rows_from_columns(grad, devices):
    rows, count, share = grad.shape
    moved = lax.all_to_all(grad, AXES, 0, 2, tiled=True)
    return moved.reshape(rows // devices, count, devices, share).reshape(
        rows // devices, count, devices * share
    )


def interleave(first, second, devices):
    rows, width = first.shape
    share = width // devices
    return jnp.stack(
        [first.reshape(rows, devices, share), second.reshape(rows, devices, share)], axis=2
    ).reshape(rows, 2 * width)


def split_exact(values):
    high = lax.reduce_precision(values, exponent_bits=8, mantissa_bits=7)
    return (high.astype(jnp.bfloat16), (values - high).astype(jnp.bfloat16))


def local(
    tokens,
    lengths,
    attn_gain,
    query_down,
    query_gain,
    query_up,
    latent_down,
    latent_gain,
    latent_up,
    output_weight,
    feed_gain,
    gate_weight,
    up_weight,
    down_weight,
    cotangent,
):
    micro, _, slot, width = tokens.shape
    rows = micro * slot
    devices = lax.axis_size(AXES)
    me = lax.axis_index(AXES)
    ffn = gate_weight.shape[1]
    attn_shards = (
        query_down,
        query_up,
        latent_down,
        latent_up,
        output_weight,
        attn_gain,
        query_gain,
        latent_gain,
        feed_gain,
    )
    (
        down_query,
        up_query,
        down_latent,
        up_latent,
        weight_out,
        gain_one,
        gain_query,
        gain_latent,
        gain_two,
    ) = gather_packed(attn_shards)
    ff_share = ffn // devices
    weight_gate_up = lax.all_gather(
        interleave(gate_weight, up_weight, devices), AXES, axis=0, tiled=True
    )
    weight_down = lax.all_gather(down_weight, AXES, axis=0, tiled=True)
    half = ROPE // 2
    freqs = 10000.0 ** (-(2.0 * jnp.arange(half, dtype=jnp.float32)) / ROPE)
    angles = jnp.arange(slot, dtype=jnp.float32)[:, None] * freqs[None, :]
    cosines = jnp.cos(angles)[:, None, :]
    sines = jnp.sin(angles)[:, None, :]
    positions = lax.broadcasted_iota(jnp.int32, (micro, slot), 1)
    valid_rows = (positions < lengths).astype(jnp.float32).reshape(rows, 1)
    query_pos = lax.broadcasted_iota(jnp.int32, (micro, 1, slot, slot), 2)
    key_pos = lax.broadcasted_iota(jnp.int32, (micro, 1, slot, slot), 3)
    allowed = (key_pos <= query_pos) & (key_pos < lengths[:, :, None, None])
    scale = 1.0 / math.sqrt(NOPE + ROPE)
    inputs = tokens.reshape(rows, width).astype(jnp.float32)
    normed_one, inverse_one = normalize(inputs)
    h_one = (normed_one * gain_one.astype(jnp.float32)).astype(jnp.bfloat16)
    latent_query = matmul(h_one, down_query)
    normed_query, inverse_query = normalize(latent_query)
    query_low = (normed_query * gain_query.astype(jnp.float32)).astype(jnp.bfloat16)
    query_raw = matmul(query_low, up_query).reshape(micro, slot, HEADS, NOPE + ROPE)
    queries = jnp.concatenate(
        [query_raw[..., :NOPE], rotate(query_raw[..., NOPE:], cosines, sines)], axis=-1
    ).astype(jnp.bfloat16)
    latent_all = matmul(h_one, down_latent)
    normed_latent, inverse_latent = normalize(latent_all[:, :KVRANK])
    latent_low = (normed_latent * gain_latent.astype(jnp.float32)).astype(jnp.bfloat16)
    kv_raw = matmul(latent_low, up_latent).reshape(micro, slot, HEADS, NOPE + VDIM)
    key_rope = rotate(latent_all[:, KVRANK:].reshape(micro, slot, 1, ROPE), cosines, sines)
    keys = jnp.concatenate(
        [kv_raw[..., :NOPE], jnp.broadcast_to(key_rope, (micro, slot, HEADS, ROPE))], axis=-1
    ).astype(jnp.bfloat16)
    values = kv_raw[..., NOPE:].astype(jnp.bfloat16)
    raw = jnp.einsum("mqhd,mkhd->mhqk", queries, keys, preferred_element_type=jnp.float32)
    scores = jnp.where(allowed, raw * scale, masked_score)
    top = jnp.max(scores, axis=-1, keepdims=True)
    expo = jnp.exp(scores - top)
    total = jnp.sum(expo, axis=-1, keepdims=True)
    probs = expo / total
    log_total = top + jnp.log(total)
    attended = jnp.einsum(
        "mhqk,mkhd->mqhd", probs.astype(jnp.bfloat16), values, preferred_element_type=jnp.float32
    )
    attended = attended.reshape(rows, HEADS * VDIM).astype(jnp.bfloat16)
    q_rank = query_low.shape[1]
    kv_rank = latent_low.shape[1]
    middle = inputs + depth_scale * matmul(attended, weight_out)
    normed_two, inverse_two = normalize(middle)
    h_two = (normed_two * gain_two.astype(jnp.float32)).astype(jnp.bfloat16)
    gate_up = matmul(h_two, weight_gate_up).reshape(rows, devices, 2, ff_share)
    gate = gate_up[:, :, 0].reshape(rows, ffn)
    upward = gate_up[:, :, 1].reshape(rows, ffn)
    sigma = jax.nn.sigmoid(gate)
    hidden = (gate * sigma * upward).astype(jnp.bfloat16)
    result = (middle + depth_scale * matmul(hidden, weight_down)) * valid_rows
    output = result.astype(jnp.bfloat16).reshape(tokens.shape)
    grad_out = cotangent.reshape(rows, width).astype(jnp.float32) * valid_rows
    grad_feed = (depth_scale * grad_out).astype(jnp.bfloat16)
    latents_all = gather_tokens(
        jnp.concatenate([query_low, latent_low, attended, h_two, grad_feed], axis=1)
    )
    query_low_all = latents_all[:, :q_rank]
    latent_low_all = latents_all[:, q_rank : q_rank + kv_rank]
    attended_all = latents_all[:, q_rank + kv_rank : q_rank + kv_rank + width]
    h_two_all = latents_all[:, q_rank + kv_rank + width : q_rank + kv_rank + 2 * width]
    grad_feed_all = latents_all[:, q_rank + kv_rank + 2 * width :]
    grad_hidden = back_product(grad_feed, weight_down)
    grad_gate = (grad_hidden * upward * sigma * (1.0 + gate * (1.0 - sigma))).astype(jnp.bfloat16)
    grad_up = (grad_hidden * gate * sigma).astype(jnp.bfloat16)
    grad_h_two = back_product(interleave(grad_gate, grad_up, devices), weight_gate_up)
    gain_two_term, grad_middle_norm = norm_back(grad_h_two, normed_two, inverse_two, gain_two)
    grad_middle = grad_out + grad_middle_norm
    grad_attn = (depth_scale * grad_middle).astype(jnp.bfloat16)
    attn_share = width // devices
    gate_up_c = matmul(
        h_two_all, lax.dynamic_slice_in_dim(weight_gate_up, me * 2 * ff_share, 2 * ff_share, 1)
    )
    gate_c = gate_up_c[:, :ff_share]
    up_c = gate_up_c[:, ff_share:]
    sigma_c = jax.nn.sigmoid(gate_c)
    hidden_c = (gate_c * sigma_c * up_c).astype(jnp.bfloat16)
    grad_hidden_c = back_product(grad_feed_all, down_weight)
    grad_gate_c = (grad_hidden_c * up_c * sigma_c * (1.0 + gate_c * (1.0 - sigma_c))).astype(
        jnp.bfloat16
    )
    grad_up_c = (grad_hidden_c * gate_c * sigma_c).astype(jnp.bfloat16)
    down_grad = rows_product(hidden_c, grad_feed_all)
    gate_up_cols = rows_product(h_two_all, jnp.concatenate([grad_gate_c, grad_up_c], axis=1))
    inner_cols = column_shares(jnp.stack([h_one, grad_attn], axis=1), devices)
    h_one_cols = inner_cols[:, 0]
    out_cols = rows_product(attended_all, inner_cols[:, 1])
    wide_rows = rows_from_columns(
        jnp.concatenate([gate_up_cols, out_cols], axis=1)[:, None, :], devices
    ).reshape(width // devices, devices, 2 * ff_share + attn_share)
    gate_grad = wide_rows[:, :, :ff_share].reshape(width // devices, ffn)
    up_grad = wide_rows[:, :, ff_share : 2 * ff_share].reshape(width // devices, ffn)
    output_weight_grad = wide_rows[:, :, 2 * ff_share :].reshape(width // devices, width)
    grad_heads = (
        back_product(grad_attn, weight_out).astype(jnp.bfloat16).reshape(micro, slot, HEADS, VDIM)
    )
    probs_again = jnp.exp(scores - log_total)
    grad_values = jnp.einsum(
        "mhqk,mqhd->mkhd",
        probs_again.astype(jnp.bfloat16),
        grad_heads,
        preferred_element_type=jnp.float32,
    )
    grad_probs = jnp.einsum(
        "mqhd,mkhd->mhqk", grad_heads, values, preferred_element_type=jnp.float32
    )
    inner = jnp.sum(probs_again * grad_probs, axis=-1, keepdims=True)
    grad_scores = (probs_again * (grad_probs - inner)).astype(jnp.bfloat16)
    grad_queries = scale * jnp.einsum(
        "mhqk,mkhd->mqhd", grad_scores, keys, preferred_element_type=jnp.float32
    )
    grad_keys = scale * jnp.einsum(
        "mhqk,mqhd->mkhd", grad_scores, queries, preferred_element_type=jnp.float32
    )
    grad_query_raw = jnp.concatenate(
        [grad_queries[..., :NOPE], rotate_back(grad_queries[..., NOPE:], cosines, sines)], axis=-1
    )
    grad_query_raw = grad_query_raw.reshape(rows, HEADS * (NOPE + ROPE)).astype(jnp.bfloat16)
    grad_query_low = back_product(grad_query_raw, up_query)
    grad_kv = (
        jnp.concatenate([grad_keys[..., :NOPE], grad_values], axis=-1)
        .reshape(rows, HEADS * (NOPE + VDIM))
        .astype(jnp.bfloat16)
    )
    grad_latent_low = back_product(grad_kv, up_latent)
    latent_gain_term, grad_latent = norm_back(
        grad_latent_low, normed_latent, inverse_latent, gain_latent
    )
    grad_key_rope = rotate_back(
        jnp.sum(grad_keys[..., NOPE:], axis=2, keepdims=True), cosines, sines
    ).reshape(rows, ROPE)
    grad_latent_all = jnp.concatenate([grad_latent, grad_key_rope], axis=-1).astype(jnp.bfloat16)
    query_gain_term, grad_latent_query = norm_back(
        grad_query_low, normed_query, inverse_query, gain_query
    )
    grad_latent_query = grad_latent_query.astype(jnp.bfloat16)
    query_width = up_query.shape[1]
    kv_width = up_latent.shape[1]
    up_cols = column_shares(
        jnp.concatenate(
            [
                grad_query_raw.reshape(rows, devices, query_width // devices),
                grad_kv.reshape(rows, devices, kv_width // devices),
            ],
            axis=2,
        ).reshape(rows, 1, query_width + kv_width),
        devices,
    )[:, 0]
    query_cols = query_width // devices
    query_up_cols = rows_product(query_low_all, up_cols[:, :query_cols])
    latent_up_cols = rows_product(latent_low_all, up_cols[:, query_cols:])
    grad_h_one = back_product(grad_latent_all, down_latent) + back_product(
        grad_latent_query, down_query
    )
    gain_one_term, grad_input_norm = norm_back(grad_h_one, normed_one, inverse_one, gain_one)
    input_grad = (grad_middle + grad_input_norm).reshape(tokens.shape)
    gain_terms = jnp.concatenate([gain_one_term, query_gain_term, latent_gain_term, gain_two_term])
    high, low = split_exact(gain_terms)
    down_grads = jnp.concatenate([grad_latent_all, grad_latent_query], axis=1)
    grad_width = down_grads.shape[1]
    gain_rows = -(-(2 * gain_terms.size) // grad_width)
    gain_block = jnp.pad(
        jnp.concatenate([high, low]), (0, gain_rows * grad_width - 2 * gain_terms.size)
    ).reshape(gain_rows, grad_width)
    last_all = lax.all_gather(
        jnp.concatenate([down_grads, gain_block], axis=0), AXES, axis=0, tiled=False
    )
    down_grads_all = last_all[:, :rows].reshape(devices * rows, grad_width)
    gain_parts = last_all[:, rows:].reshape(devices, gain_rows * grad_width)[:, : 2 * gain_terms.size]
    gain_sums = jnp.sum(
        gain_parts[:, : gain_terms.size].astype(jnp.float32)
        + gain_parts[:, gain_terms.size :].astype(jnp.float32),
        axis=0,
    )
    latent_width = grad_latent_all.shape[1]
    latent_down_grad = rows_product(h_one_cols, down_grads_all[:, :latent_width])
    query_down_grad = rows_product(h_one_cols, down_grads_all[:, latent_width:])
    up_rows = rows_from_columns(
        jnp.concatenate(
            [
                query_up_cols.reshape(devices, -1),
                latent_up_cols.reshape(devices, -1),
            ],
            axis=1,
        ).reshape(devices, 1, -1),
        devices,
    )
    q_rows = up_query.shape[0] // devices
    kv_rows = up_latent.shape[0] // devices
    kv_cols = kv_width // devices
    up_rows = up_rows.reshape(devices, -1)
    query_up_grad = (
        up_rows[:, : q_rows * query_cols]
        .reshape(devices, q_rows, query_cols)
        .transpose(1, 0, 2)
        .reshape(q_rows, query_width)
    )
    latent_up_grad = (
        up_rows[:, q_rows * query_cols :]
        .reshape(devices, kv_rows, kv_cols)
        .transpose(1, 0, 2)
        .reshape(kv_rows, kv_width)
    )

    def own(vector, offset, size):
        share = size // devices
        return lax.dynamic_slice(vector, (offset + me * share,), (share,))

    d_model = gain_one_term.size
    attn_gain_grad = own(gain_sums, 0, d_model)
    query_gain_grad = own(gain_sums, d_model, q_rank)
    latent_gain_grad = own(gain_sums, d_model + q_rank, kv_rank)
    feed_gain_grad = own(gain_sums, d_model + q_rank + kv_rank, d_model)
    return (
        output,
        input_grad,
        attn_gain_grad,
        query_down_grad,
        query_gain_grad,
        query_up_grad,
        latent_down_grad,
        latent_gain_grad,
        latent_up_grad,
        output_weight_grad,
        feed_gain_grad,
        gate_grad,
        up_grad,
        down_grad,
    )


def solution(mesh):
    placed = (
        P(None, ("fsdp", "dp"), None, None),
        P(None, ("fsdp", "dp")),
        P(("fsdp", "dp")),
        P(("fsdp", "dp"), None),
        P(("fsdp", "dp")),
        P(("fsdp", "dp"), None),
        P(("fsdp", "dp"), None),
        P(("fsdp", "dp")),
        P(("fsdp", "dp"), None),
        P(("fsdp", "dp"), None),
        P(("fsdp", "dp")),
        P(("fsdp", "dp"), None),
        P(("fsdp", "dp"), None),
        P(("fsdp", "dp"), None),
        P(None, ("fsdp", "dp"), None, None),
    )
    return jax.shard_map(
        local,
        mesh=mesh,
        in_specs=placed,
        out_specs=(
            P(None, ("fsdp", "dp"), None, None),
            P(None, ("fsdp", "dp"), None, None),
            P(("fsdp", "dp")),
            P(("fsdp", "dp"), None),
            P(("fsdp", "dp")),
            P(("fsdp", "dp"), None),
            P(("fsdp", "dp"), None),
            P(("fsdp", "dp")),
            P(("fsdp", "dp"), None),
            P(("fsdp", "dp"), None),
            P(("fsdp", "dp")),
            P(("fsdp", "dp"), None),
            P(("fsdp", "dp"), None),
            P(("fsdp", "dp"), None),
        ),
        check_vma=False,
    )
```

```python
import math

import jax
import jax.numpy as jnp
from jax import lax
from jax.sharding import PartitionSpec as P

HEADS = 40
NOPE = 64
ROPE = 32
VDIM = 64
KVRANK = 256


epsilon = 1e-05
depth_scale = 1.4 / math.sqrt(62.0)
masked_score = -1e30
AXES = ("fsdp", "dp")
LANES = 128


def matmul(left, right):
    return jnp.dot(left, right, preferred_element_type=jnp.float32)


def rows_product(left, right):
    return lax.dot_general(
        left, right, (((0,), (0,)), ((), ())), preferred_element_type=jnp.float32
    )


def back_product(left, right):
    return lax.dot_general(
        left, right, (((1,), (1,)), ((), ())), preferred_element_type=jnp.float32
    )


def normalize(values):
    inverse = lax.rsqrt(jnp.mean(values * values, axis=-1, keepdims=True) + epsilon)
    return (values * inverse, inverse)


def norm_back(grad, normed, inverse, gain):
    scaled = grad * gain.astype(jnp.float32)
    gain_grad = jnp.sum(grad * normed, axis=0)
    inner = jnp.mean(scaled * normed, axis=-1, keepdims=True)
    return (gain_grad, inverse * (scaled - normed * inner))


def rotate(values, cosines, sines):
    half = values.shape[-1] // 2
    first = values[..., :half]
    second = values[..., half:]
    return jnp.concatenate(
        [first * cosines - second * sines, second * cosines + first * sines], axis=-1
    )


def rotate_back(grad, cosines, sines):
    half = grad.shape[-1] // 2
    first = grad[..., :half]
    second = grad[..., half:]
    return jnp.concatenate(
        [first * cosines + second * sines, second * cosines - first * sines], axis=-1
    )


def padded(size):
    return -(-size // LANES) * LANES


def gather_packed(shards):
    flat = []
    for shard in shards:
        piece = shard.reshape(-1)
        flat.append(jnp.pad(piece, (0, padded(piece.size) - piece.size)))
    gathered = lax.all_gather(jnp.concatenate(flat), AXES, axis=0, tiled=False)
    devices = gathered.shape[0]
    results = []
    offset = 0
    for shard in shards:
        piece = gathered[:, offset : offset + shard.size]
        results.append(piece.reshape((devices * shard.shape[0],) + shard.shape[1:]))
        offset = offset + padded(shard.size)
    return results


def gather_tokens(values):
    return lax.all_gather(values, AXES, axis=0, tiled=True)


def column_shares(stacked, devices):
    tokens, count, width = stacked.shape
    blocks = stacked.reshape(tokens, count, devices, width // devices)
    moved = lax.all_to_all(blocks, AXES, 2, 0, tiled=True)
    return moved.reshape(devices * tokens, count, width // devices)


def rows_from_columns(grad, devices):
    rows, count, share = grad.shape
    moved = lax.all_to_all(grad, AXES, 0, 2, tiled=True)
    return moved.reshape(rows // devices, count, devices, share).reshape(
        rows // devices, count, devices * share
    )


def interleave(first, second, devices):
    rows, width = first.shape
    share = width // devices
    return jnp.stack(
        [first.reshape(rows, devices, share), second.reshape(rows, devices, share)], axis=2
    ).reshape(rows, 2 * width)


def split_exact(values):
    high = lax.reduce_precision(values, exponent_bits=8, mantissa_bits=7)
    return (high.astype(jnp.bfloat16), (values - high).astype(jnp.bfloat16))


def local(
    tokens,
    lengths,
    attn_gain,
    query_down,
    query_gain,
    query_up,
    latent_down,
    latent_gain,
    latent_up,
    output_weight,
    feed_gain,
    gate_weight,
    up_weight,
    down_weight,
    cotangent,
):
    micro, _, slot, width = tokens.shape
    rows = micro * slot
    devices = lax.axis_size(AXES)
    me = lax.axis_index(AXES)
    ffn = gate_weight.shape[1]
    attn_shards = (
        query_down,
        query_up,
        latent_down,
        latent_up,
        output_weight,
        attn_gain,
        query_gain,
        latent_gain,
        feed_gain,
    )
    (
        down_query,
        up_query,
        down_latent,
        up_latent,
        weight_out,
        gain_one,
        gain_query,
        gain_latent,
        gain_two,
    ) = gather_packed(attn_shards)
    ff_share = ffn // devices
    weight_gate_up = lax.all_gather(
        interleave(gate_weight, up_weight, devices), AXES, axis=0, tiled=True
    )
    weight_down = lax.all_gather(down_weight, AXES, axis=0, tiled=True)
    half = ROPE // 2
    freqs = 10000.0 ** (-(2.0 * jnp.arange(half, dtype=jnp.float32)) / ROPE)
    angles = jnp.arange(slot, dtype=jnp.float32)[:, None] * freqs[None, :]
    cosines = jnp.cos(angles)[:, None, :]
    sines = jnp.sin(angles)[:, None, :]
    positions = lax.broadcasted_iota(jnp.int32, (micro, slot), 1)
    valid_rows = (positions < lengths).astype(jnp.float32).reshape(rows, 1)
    query_pos = lax.broadcasted_iota(jnp.int32, (micro, 1, slot, slot), 2)
    key_pos = lax.broadcasted_iota(jnp.int32, (micro, 1, slot, slot), 3)
    allowed = (key_pos <= query_pos) & (key_pos < lengths[:, :, None, None])
    scale = 1.0 / math.sqrt(NOPE + ROPE)
    inputs = tokens.reshape(rows, width).astype(jnp.float32)
    normed_one, inverse_one = normalize(inputs)
    h_one = (normed_one * gain_one.astype(jnp.float32)).astype(jnp.bfloat16)
    latent_query = matmul(h_one, down_query)
    normed_query, inverse_query = normalize(latent_query)
    query_low = (normed_query * gain_query.astype(jnp.float32)).astype(jnp.bfloat16)
    query_raw = matmul(query_low, up_query).reshape(micro, slot, HEADS, NOPE + ROPE)
    queries = jnp.concatenate(
        [query_raw[..., :NOPE], rotate(query_raw[..., NOPE:], cosines, sines)], axis=-1
    ).astype(jnp.bfloat16)
    latent_all = matmul(h_one, down_latent)
    normed_latent, inverse_latent = normalize(latent_all[:, :KVRANK])
    latent_low = (normed_latent * gain_latent.astype(jnp.float32)).astype(jnp.bfloat16)
    kv_raw = matmul(latent_low, up_latent).reshape(micro, slot, HEADS, NOPE + VDIM)
    key_rope = rotate(latent_all[:, KVRANK:].reshape(micro, slot, 1, ROPE), cosines, sines)
    keys = jnp.concatenate(
        [kv_raw[..., :NOPE], jnp.broadcast_to(key_rope, (micro, slot, HEADS, ROPE))], axis=-1
    ).astype(jnp.bfloat16)
    values = kv_raw[..., NOPE:].astype(jnp.bfloat16)
    raw = jnp.einsum("mqhd,mkhd->mhqk", queries, keys, preferred_element_type=jnp.float32)
    scores = jnp.where(allowed, raw * scale, masked_score)
    top = jnp.max(scores, axis=-1, keepdims=True)
    expo = jnp.exp(scores - top)
    total = jnp.sum(expo, axis=-1, keepdims=True)
    probs = expo / total
    log_total = top + jnp.log(total)
    attended = jnp.einsum(
        "mhqk,mkhd->mqhd", probs.astype(jnp.bfloat16), values, preferred_element_type=jnp.float32
    )
    attended = attended.reshape(rows, HEADS * VDIM).astype(jnp.bfloat16)
    q_rank = query_low.shape[1]
    kv_rank = latent_low.shape[1]
    middle = inputs + depth_scale * matmul(attended, weight_out)
    normed_two, inverse_two = normalize(middle)
    h_two = (normed_two * gain_two.astype(jnp.float32)).astype(jnp.bfloat16)
    gate_up = matmul(h_two, weight_gate_up).reshape(rows, devices, 2, ff_share)
    gate = gate_up[:, :, 0].reshape(rows, ffn)
    upward = gate_up[:, :, 1].reshape(rows, ffn)
    sigma = jax.nn.sigmoid(gate)
    hidden = (gate * sigma * upward).astype(jnp.bfloat16)
    result = (middle + depth_scale * matmul(hidden, weight_down)) * valid_rows
    output = result.astype(jnp.bfloat16).reshape(tokens.shape)
    grad_out = cotangent.reshape(rows, width).astype(jnp.float32) * valid_rows
    grad_feed = (depth_scale * grad_out).astype(jnp.bfloat16)
    latents_all = gather_tokens(
        jnp.concatenate([query_low, latent_low, attended, h_two, grad_feed], axis=1)
    )
    query_low_all = latents_all[:, :q_rank]
    latent_low_all = latents_all[:, q_rank : q_rank + kv_rank]
    attended_all = latents_all[:, q_rank + kv_rank : q_rank + kv_rank + width]
    h_two_all = latents_all[:, q_rank + kv_rank + width : q_rank + kv_rank + 2 * width]
    grad_feed_all = latents_all[:, q_rank + kv_rank + 2 * width :]
    grad_hidden = back_product(grad_feed, weight_down)
    grad_gate = (grad_hidden * upward * sigma * (1.0 + gate * (1.0 - sigma))).astype(jnp.bfloat16)
    grad_up = (grad_hidden * gate * sigma).astype(jnp.bfloat16)
    grad_h_two = back_product(interleave(grad_gate, grad_up, devices), weight_gate_up)
    gain_two_term, grad_middle_norm = norm_back(grad_h_two, normed_two, inverse_two, gain_two)
    grad_middle = grad_out + grad_middle_norm
    grad_attn = (depth_scale * grad_middle).astype(jnp.bfloat16)
    attn_share = width // devices
    gate_up_c = matmul(
        h_two_all, lax.dynamic_slice_in_dim(weight_gate_up, me * 2 * ff_share, 2 * ff_share, 1)
    )
    gate_c = gate_up_c[:, :ff_share]
    up_c = gate_up_c[:, ff_share:]
    sigma_c = jax.nn.sigmoid(gate_c)
    hidden_c = (gate_c * sigma_c * up_c).astype(jnp.bfloat16)
    grad_hidden_c = back_product(grad_feed_all, down_weight)
    grad_gate_c = (grad_hidden_c * up_c * sigma_c * (1.0 + gate_c * (1.0 - sigma_c))).astype(
        jnp.bfloat16
    )
    grad_up_c = (grad_hidden_c * gate_c * sigma_c).astype(jnp.bfloat16)
    down_grad = rows_product(hidden_c, grad_feed_all)
    gate_up_cols = rows_product(h_two_all, jnp.concatenate([grad_gate_c, grad_up_c], axis=1))
    wide_rows = rows_from_columns(gate_up_cols[:, None, :], devices).reshape(
        width // devices, devices, 2 * ff_share
    )
    gate_grad = wide_rows[:, :, :ff_share].reshape(width // devices, ffn)
    up_grad = wide_rows[:, :, ff_share:].reshape(width // devices, ffn)
    grad_heads = (
        back_product(grad_attn, weight_out).astype(jnp.bfloat16).reshape(micro, slot, HEADS, VDIM)
    )
    probs_again = jnp.exp(scores - log_total)
    grad_values = jnp.einsum(
        "mhqk,mqhd->mkhd",
        probs_again.astype(jnp.bfloat16),
        grad_heads,
        preferred_element_type=jnp.float32,
    )
    grad_probs = jnp.einsum(
        "mqhd,mkhd->mhqk", grad_heads, values, preferred_element_type=jnp.float32
    )
    inner = jnp.sum(probs_again * grad_probs, axis=-1, keepdims=True)
    grad_scores = (probs_again * (grad_probs - inner)).astype(jnp.bfloat16)
    grad_queries = scale * jnp.einsum(
        "mhqk,mkhd->mqhd", grad_scores, keys, preferred_element_type=jnp.float32
    )
    grad_keys = scale * jnp.einsum(
        "mhqk,mqhd->mkhd", grad_scores, queries, preferred_element_type=jnp.float32
    )
    grad_query_raw = jnp.concatenate(
        [grad_queries[..., :NOPE], rotate_back(grad_queries[..., NOPE:], cosines, sines)], axis=-1
    )
    grad_query_raw = grad_query_raw.reshape(rows, HEADS * (NOPE + ROPE)).astype(jnp.bfloat16)
    grad_query_low = back_product(grad_query_raw, up_query)
    grad_kv = (
        jnp.concatenate([grad_keys[..., :NOPE], grad_values], axis=-1)
        .reshape(rows, HEADS * (NOPE + VDIM))
        .astype(jnp.bfloat16)
    )
    grad_latent_low = back_product(grad_kv, up_latent)
    latent_gain_term, grad_latent = norm_back(
        grad_latent_low, normed_latent, inverse_latent, gain_latent
    )
    grad_key_rope = rotate_back(
        jnp.sum(grad_keys[..., NOPE:], axis=2, keepdims=True), cosines, sines
    ).reshape(rows, ROPE)
    grad_latent_all = jnp.concatenate([grad_latent, grad_key_rope], axis=-1).astype(jnp.bfloat16)
    query_gain_term, grad_latent_query = norm_back(
        grad_query_low, normed_query, inverse_query, gain_query
    )
    grad_latent_query = grad_latent_query.astype(jnp.bfloat16)
    query_width = up_query.shape[1]
    kv_width = up_latent.shape[1]
    up_cols = column_shares(
        jnp.concatenate(
            [
                grad_query_raw.reshape(rows, devices, query_width // devices),
                grad_kv.reshape(rows, devices, kv_width // devices),
                h_one.reshape(rows, devices, attn_share),
                grad_attn.reshape(rows, devices, attn_share),
            ],
            axis=2,
        ).reshape(rows, 1, query_width + kv_width + 2 * width),
        devices,
    )[:, 0]
    inner_at = (query_width + kv_width) // devices
    h_one_cols = up_cols[:, inner_at : inner_at + attn_share]
    out_cols = rows_product(attended_all, up_cols[:, inner_at + attn_share :])
    query_cols = query_width // devices
    query_up_cols = rows_product(query_low_all, up_cols[:, :query_cols])
    latent_up_cols = rows_product(latent_low_all, up_cols[:, query_cols:inner_at])
    grad_h_one = back_product(grad_latent_all, down_latent) + back_product(
        grad_latent_query, down_query
    )
    gain_one_term, grad_input_norm = norm_back(grad_h_one, normed_one, inverse_one, gain_one)
    input_grad = (grad_middle + grad_input_norm).reshape(tokens.shape)
    gain_terms = jnp.concatenate([gain_one_term, query_gain_term, latent_gain_term, gain_two_term])
    high, low = split_exact(gain_terms)
    down_grads = jnp.concatenate([grad_latent_all, grad_latent_query], axis=1)
    grad_width = down_grads.shape[1]
    gain_rows = -(-(2 * gain_terms.size) // grad_width)
    gain_block = jnp.pad(
        jnp.concatenate([high, low]), (0, gain_rows * grad_width - 2 * gain_terms.size)
    ).reshape(gain_rows, grad_width)
    last_all = lax.all_gather(
        jnp.concatenate([down_grads, gain_block], axis=0), AXES, axis=0, tiled=False
    )
    down_grads_all = last_all[:, :rows].reshape(devices * rows, grad_width)
    gain_parts = last_all[:, rows:].reshape(devices, gain_rows * grad_width)[:, : 2 * gain_terms.size]
    gain_sums = jnp.sum(
        gain_parts[:, : gain_terms.size].astype(jnp.float32)
        + gain_parts[:, gain_terms.size :].astype(jnp.float32),
        axis=0,
    )
    latent_width = grad_latent_all.shape[1]
    latent_down_grad = rows_product(h_one_cols, down_grads_all[:, :latent_width])
    query_down_grad = rows_product(h_one_cols, down_grads_all[:, latent_width:])
    up_rows = rows_from_columns(
        jnp.concatenate(
            [
                query_up_cols.reshape(devices, -1),
                latent_up_cols.reshape(devices, -1),
                out_cols.reshape(devices, -1),
            ],
            axis=1,
        ).reshape(devices, 1, -1),
        devices,
    )
    q_rows = up_query.shape[0] // devices
    kv_rows = up_latent.shape[0] // devices
    kv_cols = kv_width // devices
    up_rows = up_rows.reshape(devices, -1)
    query_up_grad = (
        up_rows[:, : q_rows * query_cols]
        .reshape(devices, q_rows, query_cols)
        .transpose(1, 0, 2)
        .reshape(q_rows, query_width)
    )
    kv_end = q_rows * query_cols + kv_rows * kv_cols
    latent_up_grad = (
        up_rows[:, q_rows * query_cols : kv_end]
        .reshape(devices, kv_rows, kv_cols)
        .transpose(1, 0, 2)
        .reshape(kv_rows, kv_width)
    )
    output_weight_grad = (
        up_rows[:, kv_end:]
        .reshape(devices, width // devices, attn_share)
        .transpose(1, 0, 2)
        .reshape(width // devices, width)
    )

    def own(vector, offset, size):
        share = size // devices
        return lax.dynamic_slice(vector, (offset + me * share,), (share,))

    d_model = gain_one_term.size
    attn_gain_grad = own(gain_sums, 0, d_model)
    query_gain_grad = own(gain_sums, d_model, q_rank)
    latent_gain_grad = own(gain_sums, d_model + q_rank, kv_rank)
    feed_gain_grad = own(gain_sums, d_model + q_rank + kv_rank, d_model)
    return (
        output,
        input_grad,
        attn_gain_grad,
        query_down_grad,
        query_gain_grad,
        query_up_grad,
        latent_down_grad,
        latent_gain_grad,
        latent_up_grad,
        output_weight_grad,
        feed_gain_grad,
        gate_grad,
        up_grad,
        down_grad,
    )


def solution(mesh):
    placed = (
        P(None, ("fsdp", "dp"), None, None),
        P(None, ("fsdp", "dp")),
        P(("fsdp", "dp")),
        P(("fsdp", "dp"), None),
        P(("fsdp", "dp")),
        P(("fsdp", "dp"), None),
        P(("fsdp", "dp"), None),
        P(("fsdp", "dp")),
        P(("fsdp", "dp"), None),
        P(("fsdp", "dp"), None),
        P(("fsdp", "dp")),
        P(("fsdp", "dp"), None),
        P(("fsdp", "dp"), None),
        P(("fsdp", "dp"), None),
        P(None, ("fsdp", "dp"), None, None),
    )
    return jax.shard_map(
        local,
        mesh=mesh,
        in_specs=placed,
        out_specs=(
            P(None, ("fsdp", "dp"), None, None),
            P(None, ("fsdp", "dp"), None, None),
            P(("fsdp", "dp")),
            P(("fsdp", "dp"), None),
            P(("fsdp", "dp")),
            P(("fsdp", "dp"), None),
            P(("fsdp", "dp"), None),
            P(("fsdp", "dp")),
            P(("fsdp", "dp"), None),
            P(("fsdp", "dp"), None),
            P(("fsdp", "dp")),
            P(("fsdp", "dp"), None),
            P(("fsdp", "dp"), None),
            P(("fsdp", "dp"), None),
        ),
        check_vma=False,
    )
```

```python
import math

import jax
import jax.numpy as jnp
from jax import lax
from jax.sharding import PartitionSpec as P

HEADS = 40
NOPE = 64
ROPE = 32
VDIM = 64
KVRANK = 256


epsilon = 1e-05
depth_scale = 1.4 / math.sqrt(62.0)
masked_score = -1e30
AXES = ("fsdp", "dp")
LANES = 128


def matmul(left, right):
    return jnp.dot(left, right, preferred_element_type=jnp.float32)


def rows_product(left, right):
    return lax.dot_general(
        left, right, (((0,), (0,)), ((), ())), preferred_element_type=jnp.float32
    )


def back_product(left, right):
    return lax.dot_general(
        left, right, (((1,), (1,)), ((), ())), preferred_element_type=jnp.float32
    )


def normalize(values):
    inverse = lax.rsqrt(jnp.mean(values * values, axis=-1, keepdims=True) + epsilon)
    return (values * inverse, inverse)


def norm_back(grad, normed, inverse, gain):
    scaled = grad * gain.astype(jnp.float32)
    gain_grad = jnp.sum(grad * normed, axis=0)
    inner = jnp.mean(scaled * normed, axis=-1, keepdims=True)
    return (gain_grad, inverse * (scaled - normed * inner))


def rotate(values, cosines, sines):
    half = values.shape[-1] // 2
    first = values[..., :half]
    second = values[..., half:]
    return jnp.concatenate(
        [first * cosines - second * sines, second * cosines + first * sines], axis=-1
    )


def rotate_back(grad, cosines, sines):
    half = grad.shape[-1] // 2
    first = grad[..., :half]
    second = grad[..., half:]
    return jnp.concatenate(
        [first * cosines + second * sines, second * cosines - first * sines], axis=-1
    )


def padded(size):
    return -(-size // LANES) * LANES


def gather_packed(shards):
    flat = []
    for shard in shards:
        piece = shard.reshape(-1)
        flat.append(jnp.pad(piece, (0, padded(piece.size) - piece.size)))
    gathered = lax.all_gather(jnp.concatenate(flat), AXES, axis=0, tiled=False)
    devices = gathered.shape[0]
    results = []
    offset = 0
    for shard in shards:
        piece = gathered[:, offset : offset + shard.size]
        results.append(piece.reshape((devices * shard.shape[0],) + shard.shape[1:]))
        offset = offset + padded(shard.size)
    return results


def gather_tokens(values):
    return lax.all_gather(values, AXES, axis=0, tiled=True)


def column_shares(stacked, devices):
    tokens, count, width = stacked.shape
    blocks = stacked.reshape(tokens, count, devices, width // devices)
    moved = lax.all_to_all(blocks, AXES, 2, 0, tiled=True)
    return moved.reshape(devices * tokens, count, width // devices)


def rows_from_columns(grad, devices):
    rows, count, share = grad.shape
    moved = lax.all_to_all(grad, AXES, 0, 2, tiled=True)
    return moved.reshape(rows // devices, count, devices, share).reshape(
        rows // devices, count, devices * share
    )


def interleave(first, second, devices):
    rows, width = first.shape
    share = width // devices
    return jnp.stack(
        [first.reshape(rows, devices, share), second.reshape(rows, devices, share)], axis=2
    ).reshape(rows, 2 * width)


def split_exact(values):
    high = lax.reduce_precision(values, exponent_bits=8, mantissa_bits=7)
    return (high.astype(jnp.bfloat16), (values - high).astype(jnp.bfloat16))


def local(
    tokens,
    lengths,
    attn_gain,
    query_down,
    query_gain,
    query_up,
    latent_down,
    latent_gain,
    latent_up,
    output_weight,
    feed_gain,
    gate_weight,
    up_weight,
    down_weight,
    cotangent,
):
    micro, _, slot, width = tokens.shape
    rows = micro * slot
    devices = lax.axis_size(AXES)
    me = lax.axis_index(AXES)
    ffn = gate_weight.shape[1]
    attn_shards = (
        query_down,
        query_up,
        latent_down,
        latent_up,
        output_weight,
        attn_gain,
        query_gain,
        latent_gain,
        feed_gain,
    )
    (
        down_query,
        up_query,
        down_latent,
        up_latent,
        weight_out,
        gain_one,
        gain_query,
        gain_latent,
        gain_two,
    ) = gather_packed(attn_shards)
    ff_share = ffn // devices
    weight_gate_up = lax.all_gather(
        interleave(gate_weight, up_weight, devices), AXES, axis=0, tiled=True
    )
    weight_down = lax.all_gather(down_weight, AXES, axis=0, tiled=True)
    half = ROPE // 2
    freqs = 10000.0 ** (-(2.0 * jnp.arange(half, dtype=jnp.float32)) / ROPE)
    angles = jnp.arange(slot, dtype=jnp.float32)[:, None] * freqs[None, :]
    cosines = jnp.cos(angles)[:, None, :]
    sines = jnp.sin(angles)[:, None, :]
    positions = lax.broadcasted_iota(jnp.int32, (micro, slot), 1)
    valid_rows = (positions < lengths).astype(jnp.float32).reshape(rows, 1)
    query_pos = lax.broadcasted_iota(jnp.int32, (micro, 1, slot, slot), 2)
    key_pos = lax.broadcasted_iota(jnp.int32, (micro, 1, slot, slot), 3)
    allowed = (key_pos <= query_pos) & (key_pos < lengths[:, :, None, None])
    scale = 1.0 / math.sqrt(NOPE + ROPE)
    inputs = tokens.reshape(rows, width).astype(jnp.float32)
    normed_one, inverse_one = normalize(inputs)
    h_one = (normed_one * gain_one.astype(jnp.float32)).astype(jnp.bfloat16)
    latent_query = matmul(h_one, down_query)
    normed_query, inverse_query = normalize(latent_query)
    query_low = (normed_query * gain_query.astype(jnp.float32)).astype(jnp.bfloat16)
    query_raw = matmul(query_low, up_query).reshape(micro, slot, HEADS, NOPE + ROPE)
    queries = jnp.concatenate(
        [query_raw[..., :NOPE], rotate(query_raw[..., NOPE:], cosines, sines)], axis=-1
    ).astype(jnp.bfloat16)
    latent_all = matmul(h_one, down_latent)
    normed_latent, inverse_latent = normalize(latent_all[:, :KVRANK])
    latent_low = (normed_latent * gain_latent.astype(jnp.float32)).astype(jnp.bfloat16)
    kv_raw = matmul(latent_low, up_latent).reshape(micro, slot, HEADS, NOPE + VDIM)
    key_rope = rotate(latent_all[:, KVRANK:].reshape(micro, slot, 1, ROPE), cosines, sines)
    keys = jnp.concatenate(
        [kv_raw[..., :NOPE], jnp.broadcast_to(key_rope, (micro, slot, HEADS, ROPE))], axis=-1
    ).astype(jnp.bfloat16)
    values = kv_raw[..., NOPE:].astype(jnp.bfloat16)
    raw = jnp.einsum("mqhd,mkhd->mhqk", queries, keys, preferred_element_type=jnp.float32)
    scores = jnp.where(allowed, raw * scale, masked_score)
    top = jnp.max(scores, axis=-1, keepdims=True)
    expo = jnp.exp(scores - top)
    total = jnp.sum(expo, axis=-1, keepdims=True)
    probs = expo / total
    log_total = top + jnp.log(total)
    attended = jnp.einsum(
        "mhqk,mkhd->mqhd", probs.astype(jnp.bfloat16), values, preferred_element_type=jnp.float32
    )
    attended = attended.reshape(rows, HEADS * VDIM).astype(jnp.bfloat16)
    q_rank = query_low.shape[1]
    kv_rank = latent_low.shape[1]
    middle = inputs + depth_scale * matmul(attended, weight_out)
    normed_two, inverse_two = normalize(middle)
    h_two = (normed_two * gain_two.astype(jnp.float32)).astype(jnp.bfloat16)
    gate_up = matmul(h_two, weight_gate_up).reshape(rows, devices, 2, ff_share)
    gate = gate_up[:, :, 0].reshape(rows, ffn)
    upward = gate_up[:, :, 1].reshape(rows, ffn)
    sigma = jax.nn.sigmoid(gate)
    hidden = (gate * sigma * upward).astype(jnp.bfloat16)
    result = (middle + depth_scale * matmul(hidden, weight_down)) * valid_rows
    output = result.astype(jnp.bfloat16).reshape(tokens.shape)
    grad_out = cotangent.reshape(rows, width).astype(jnp.float32) * valid_rows
    grad_feed = (depth_scale * grad_out).astype(jnp.bfloat16)
    latents_all = gather_tokens(
        jnp.concatenate([query_low, latent_low, attended, h_two, grad_feed], axis=1)
    )
    query_low_all = latents_all[:, :q_rank]
    latent_low_all = latents_all[:, q_rank : q_rank + kv_rank]
    attended_all = latents_all[:, q_rank + kv_rank : q_rank + kv_rank + width]
    h_two_all = latents_all[:, q_rank + kv_rank + width : q_rank + kv_rank + 2 * width]
    grad_feed_all = latents_all[:, q_rank + kv_rank + 2 * width :]
    grad_hidden = back_product(grad_feed, weight_down)
    grad_gate = (grad_hidden * upward * sigma * (1.0 + gate * (1.0 - sigma))).astype(jnp.bfloat16)
    grad_up = (grad_hidden * gate * sigma).astype(jnp.bfloat16)
    grad_h_two = back_product(interleave(grad_gate, grad_up, devices), weight_gate_up)
    gain_two_term, grad_middle_norm = norm_back(grad_h_two, normed_two, inverse_two, gain_two)
    grad_middle = grad_out + grad_middle_norm
    grad_attn = (depth_scale * grad_middle).astype(jnp.bfloat16)
    attn_share = width // devices
    gate_up_c = matmul(
        h_two_all, lax.dynamic_slice_in_dim(weight_gate_up, me * 2 * ff_share, 2 * ff_share, 1)
    )
    gate_c = gate_up_c[:, :ff_share]
    up_c = gate_up_c[:, ff_share:]
    sigma_c = jax.nn.sigmoid(gate_c)
    hidden_c = (gate_c * sigma_c * up_c).astype(jnp.bfloat16)
    grad_hidden_c = back_product(grad_feed_all, down_weight)
    grad_gate_c = (grad_hidden_c * up_c * sigma_c * (1.0 + gate_c * (1.0 - sigma_c))).astype(
        jnp.bfloat16
    )
    grad_up_c = (grad_hidden_c * gate_c * sigma_c).astype(jnp.bfloat16)
    down_grad = rows_product(hidden_c, grad_feed_all)
    gate_cols_grad = rows_product(h_two_all, grad_gate_c)
    inner_cols = column_shares(jnp.stack([h_one, grad_attn], axis=1), devices)
    h_one_cols = inner_cols[:, 0]
    out_cols = rows_product(attended_all, inner_cols[:, 1])
    wide_rows = rows_from_columns(
        jnp.concatenate([gate_cols_grad, out_cols], axis=1)[:, None, :], devices
    ).reshape(width // devices, devices, ff_share + attn_share)
    gate_grad = wide_rows[:, :, :ff_share].reshape(width // devices, ffn)
    output_weight_grad = wide_rows[:, :, ff_share:].reshape(width // devices, width)
    up_cols_grad = rows_product(h_two_all, grad_up_c)
    up_grad = rows_from_columns(up_cols_grad[:, None, :], devices).reshape(width // devices, ffn)
    grad_heads = (
        back_product(grad_attn, weight_out).astype(jnp.bfloat16).reshape(micro, slot, HEADS, VDIM)
    )
    probs_again = jnp.exp(scores - log_total)
    grad_values = jnp.einsum(
        "mhqk,mqhd->mkhd",
        probs_again.astype(jnp.bfloat16),
        grad_heads,
        preferred_element_type=jnp.float32,
    )
    grad_probs = jnp.einsum(
        "mqhd,mkhd->mhqk", grad_heads, values, preferred_element_type=jnp.float32
    )
    inner = jnp.sum(probs_again * grad_probs, axis=-1, keepdims=True)
    grad_scores = (probs_again * (grad_probs - inner)).astype(jnp.bfloat16)
    grad_queries = scale * jnp.einsum(
        "mhqk,mkhd->mqhd", grad_scores, keys, preferred_element_type=jnp.float32
    )
    grad_keys = scale * jnp.einsum(
        "mhqk,mqhd->mkhd", grad_scores, queries, preferred_element_type=jnp.float32
    )
    grad_query_raw = jnp.concatenate(
        [grad_queries[..., :NOPE], rotate_back(grad_queries[..., NOPE:], cosines, sines)], axis=-1
    )
    grad_query_raw = grad_query_raw.reshape(rows, HEADS * (NOPE + ROPE)).astype(jnp.bfloat16)
    grad_query_low = back_product(grad_query_raw, up_query)
    grad_kv = (
        jnp.concatenate([grad_keys[..., :NOPE], grad_values], axis=-1)
        .reshape(rows, HEADS * (NOPE + VDIM))
        .astype(jnp.bfloat16)
    )
    grad_latent_low = back_product(grad_kv, up_latent)
    latent_gain_term, grad_latent = norm_back(
        grad_latent_low, normed_latent, inverse_latent, gain_latent
    )
    grad_key_rope = rotate_back(
        jnp.sum(grad_keys[..., NOPE:], axis=2, keepdims=True), cosines, sines
    ).reshape(rows, ROPE)
    grad_latent_all = jnp.concatenate([grad_latent, grad_key_rope], axis=-1).astype(jnp.bfloat16)
    query_gain_term, grad_latent_query = norm_back(
        grad_query_low, normed_query, inverse_query, gain_query
    )
    grad_latent_query = grad_latent_query.astype(jnp.bfloat16)
    query_width = up_query.shape[1]
    kv_width = up_latent.shape[1]
    up_cols = column_shares(
        jnp.concatenate(
            [
                grad_query_raw.reshape(rows, devices, query_width // devices),
                grad_kv.reshape(rows, devices, kv_width // devices),
            ],
            axis=2,
        ).reshape(rows, 1, query_width + kv_width),
        devices,
    )[:, 0]
    query_cols = query_width // devices
    query_up_cols = rows_product(query_low_all, up_cols[:, :query_cols])
    latent_up_cols = rows_product(latent_low_all, up_cols[:, query_cols:])
    grad_h_one = back_product(grad_latent_all, down_latent) + back_product(
        grad_latent_query, down_query
    )
    gain_one_term, grad_input_norm = norm_back(grad_h_one, normed_one, inverse_one, gain_one)
    input_grad = (grad_middle + grad_input_norm).reshape(tokens.shape)
    gain_terms = jnp.concatenate([gain_one_term, query_gain_term, latent_gain_term, gain_two_term])
    high, low = split_exact(gain_terms)
    down_grads = jnp.concatenate([grad_latent_all, grad_latent_query], axis=1)
    grad_width = down_grads.shape[1]
    gain_rows = -(-(2 * gain_terms.size) // grad_width)
    gain_block = jnp.pad(
        jnp.concatenate([high, low]), (0, gain_rows * grad_width - 2 * gain_terms.size)
    ).reshape(gain_rows, grad_width)
    last_all = lax.all_gather(
        jnp.concatenate([down_grads, gain_block], axis=0), AXES, axis=0, tiled=False
    )
    down_grads_all = last_all[:, :rows].reshape(devices * rows, grad_width)
    gain_parts = last_all[:, rows:].reshape(devices, gain_rows * grad_width)[:, : 2 * gain_terms.size]
    gain_sums = jnp.sum(
        gain_parts[:, : gain_terms.size].astype(jnp.float32)
        + gain_parts[:, gain_terms.size :].astype(jnp.float32),
        axis=0,
    )
    latent_width = grad_latent_all.shape[1]
    latent_down_grad = rows_product(h_one_cols, down_grads_all[:, :latent_width])
    query_down_grad = rows_product(h_one_cols, down_grads_all[:, latent_width:])
    up_rows = rows_from_columns(
        jnp.concatenate(
            [
                query_up_cols.reshape(devices, -1),
                latent_up_cols.reshape(devices, -1),
            ],
            axis=1,
        ).reshape(devices, 1, -1),
        devices,
    )
    q_rows = up_query.shape[0] // devices
    kv_rows = up_latent.shape[0] // devices
    kv_cols = kv_width // devices
    up_rows = up_rows.reshape(devices, -1)
    query_up_grad = (
        up_rows[:, : q_rows * query_cols]
        .reshape(devices, q_rows, query_cols)
        .transpose(1, 0, 2)
        .reshape(q_rows, query_width)
    )
    latent_up_grad = (
        up_rows[:, q_rows * query_cols :]
        .reshape(devices, kv_rows, kv_cols)
        .transpose(1, 0, 2)
        .reshape(kv_rows, kv_width)
    )

    def own(vector, offset, size):
        share = size // devices
        return lax.dynamic_slice(vector, (offset + me * share,), (share,))

    d_model = gain_one_term.size
    attn_gain_grad = own(gain_sums, 0, d_model)
    query_gain_grad = own(gain_sums, d_model, q_rank)
    latent_gain_grad = own(gain_sums, d_model + q_rank, kv_rank)
    feed_gain_grad = own(gain_sums, d_model + q_rank + kv_rank, d_model)
    return (
        output,
        input_grad,
        attn_gain_grad,
        query_down_grad,
        query_gain_grad,
        query_up_grad,
        latent_down_grad,
        latent_gain_grad,
        latent_up_grad,
        output_weight_grad,
        feed_gain_grad,
        gate_grad,
        up_grad,
        down_grad,
    )


def solution(mesh):
    placed = (
        P(None, ("fsdp", "dp"), None, None),
        P(None, ("fsdp", "dp")),
        P(("fsdp", "dp")),
        P(("fsdp", "dp"), None),
        P(("fsdp", "dp")),
        P(("fsdp", "dp"), None),
        P(("fsdp", "dp"), None),
        P(("fsdp", "dp")),
        P(("fsdp", "dp"), None),
        P(("fsdp", "dp"), None),
        P(("fsdp", "dp")),
        P(("fsdp", "dp"), None),
        P(("fsdp", "dp"), None),
        P(("fsdp", "dp"), None),
        P(None, ("fsdp", "dp"), None, None),
    )
    return jax.shard_map(
        local,
        mesh=mesh,
        in_specs=placed,
        out_specs=(
            P(None, ("fsdp", "dp"), None, None),
            P(None, ("fsdp", "dp"), None, None),
            P(("fsdp", "dp")),
            P(("fsdp", "dp"), None),
            P(("fsdp", "dp")),
            P(("fsdp", "dp"), None),
            P(("fsdp", "dp"), None),
            P(("fsdp", "dp")),
            P(("fsdp", "dp"), None),
            P(("fsdp", "dp"), None),
            P(("fsdp", "dp")),
            P(("fsdp", "dp"), None),
            P(("fsdp", "dp"), None),
            P(("fsdp", "dp"), None),
        ),
        check_vma=False,
    )
```

```python
import math

import jax
import jax.numpy as jnp
from jax import lax
from jax.sharding import PartitionSpec as P

HEADS = 40
NOPE = 64
ROPE = 32
VDIM = 64
KVRANK = 256


epsilon = 1e-05
depth_scale = 1.4 / math.sqrt(62.0)
masked_score = -1e30
AXES = ("fsdp", "dp")
LANES = 128


def matmul(left, right):
    return jnp.dot(left, right, preferred_element_type=jnp.float32)


def rows_product(left, right):
    return lax.dot_general(
        left, right, (((0,), (0,)), ((), ())), preferred_element_type=jnp.float32
    )


def back_product(left, right):
    return lax.dot_general(
        left, right, (((1,), (1,)), ((), ())), preferred_element_type=jnp.float32
    )


def normalize(values):
    inverse = lax.rsqrt(jnp.mean(values * values, axis=-1, keepdims=True) + epsilon)
    return (values * inverse, inverse)


def norm_back(grad, normed, inverse, gain):
    scaled = grad * gain.astype(jnp.float32)
    gain_grad = jnp.sum(grad * normed, axis=0)
    inner = jnp.mean(scaled * normed, axis=-1, keepdims=True)
    return (gain_grad, inverse * (scaled - normed * inner))


def rotate(values, cosines, sines):
    half = values.shape[-1] // 2
    first = values[..., :half]
    second = values[..., half:]
    return jnp.concatenate(
        [first * cosines - second * sines, second * cosines + first * sines], axis=-1
    )


def rotate_back(grad, cosines, sines):
    half = grad.shape[-1] // 2
    first = grad[..., :half]
    second = grad[..., half:]
    return jnp.concatenate(
        [first * cosines + second * sines, second * cosines - first * sines], axis=-1
    )


def padded(size):
    return -(-size // LANES) * LANES


def gather_packed(shards):
    flat = []
    for shard in shards:
        piece = shard.reshape(-1)
        flat.append(jnp.pad(piece, (0, padded(piece.size) - piece.size)))
    gathered = lax.all_gather(jnp.concatenate(flat), AXES, axis=0, tiled=False)
    devices = gathered.shape[0]
    results = []
    offset = 0
    for shard in shards:
        piece = gathered[:, offset : offset + shard.size]
        results.append(piece.reshape((devices * shard.shape[0],) + shard.shape[1:]))
        offset = offset + padded(shard.size)
    return results


def gather_tokens(values):
    return lax.all_gather(values, AXES, axis=0, tiled=True)


def column_shares(stacked, devices):
    tokens, count, width = stacked.shape
    blocks = stacked.reshape(tokens, count, devices, width // devices)
    moved = lax.all_to_all(blocks, AXES, 2, 0, tiled=True)
    return moved.reshape(devices * tokens, count, width // devices)


def rows_from_columns(grad, devices):
    rows, count, share = grad.shape
    moved = lax.all_to_all(grad, AXES, 0, 2, tiled=True)
    return moved.reshape(rows // devices, count, devices, share).reshape(
        rows // devices, count, devices * share
    )


def interleave(first, second, devices):
    rows, width = first.shape
    share = width // devices
    return jnp.stack(
        [first.reshape(rows, devices, share), second.reshape(rows, devices, share)], axis=2
    ).reshape(rows, 2 * width)


def split_exact(values):
    high = lax.reduce_precision(values, exponent_bits=8, mantissa_bits=7)
    return (high.astype(jnp.bfloat16), (values - high).astype(jnp.bfloat16))


def local(
    tokens,
    lengths,
    attn_gain,
    query_down,
    query_gain,
    query_up,
    latent_down,
    latent_gain,
    latent_up,
    output_weight,
    feed_gain,
    gate_weight,
    up_weight,
    down_weight,
    cotangent,
):
    micro, _, slot, width = tokens.shape
    rows = micro * slot
    devices = lax.axis_size(AXES)
    me = lax.axis_index(AXES)
    ffn = gate_weight.shape[1]
    attn_shards = (
        query_down,
        query_up,
        latent_down,
        latent_up,
        output_weight,
        attn_gain,
        query_gain,
        latent_gain,
        feed_gain,
    )
    (
        down_query,
        up_query,
        down_latent,
        up_latent,
        weight_out,
        gain_one,
        gain_query,
        gain_latent,
        gain_two,
    ) = gather_packed(attn_shards)
    ff_share = ffn // devices
    weight_gate_up = lax.all_gather(
        interleave(gate_weight, up_weight, devices), AXES, axis=0, tiled=True
    )
    weight_down = lax.all_gather(down_weight, AXES, axis=0, tiled=True)
    half = ROPE // 2
    freqs = 10000.0 ** (-(2.0 * jnp.arange(half, dtype=jnp.float32)) / ROPE)
    angles = jnp.arange(slot, dtype=jnp.float32)[:, None] * freqs[None, :]
    cosines = jnp.cos(angles)[:, None, :]
    sines = jnp.sin(angles)[:, None, :]
    positions = lax.broadcasted_iota(jnp.int32, (micro, slot), 1)
    valid_rows = (positions < lengths).astype(jnp.float32).reshape(rows, 1)
    query_pos = lax.broadcasted_iota(jnp.int32, (micro, 1, slot, slot), 2)
    key_pos = lax.broadcasted_iota(jnp.int32, (micro, 1, slot, slot), 3)
    allowed = (key_pos <= query_pos) & (key_pos < lengths[:, :, None, None])
    scale = 1.0 / math.sqrt(NOPE + ROPE)
    inputs = tokens.reshape(rows, width).astype(jnp.float32)
    normed_one, inverse_one = normalize(inputs)
    h_one = (normed_one * gain_one.astype(jnp.float32)).astype(jnp.bfloat16)
    latent_query = matmul(h_one, down_query)
    normed_query, inverse_query = normalize(latent_query)
    query_low = (normed_query * gain_query.astype(jnp.float32)).astype(jnp.bfloat16)
    query_raw = matmul(query_low, up_query).reshape(micro, slot, HEADS, NOPE + ROPE)
    queries = jnp.concatenate(
        [query_raw[..., :NOPE], rotate(query_raw[..., NOPE:], cosines, sines)], axis=-1
    ).astype(jnp.bfloat16)
    latent_all = matmul(h_one, down_latent)
    normed_latent, inverse_latent = normalize(latent_all[:, :KVRANK])
    latent_low = (normed_latent * gain_latent.astype(jnp.float32)).astype(jnp.bfloat16)
    kv_raw = matmul(latent_low, up_latent).reshape(micro, slot, HEADS, NOPE + VDIM)
    key_rope = rotate(latent_all[:, KVRANK:].reshape(micro, slot, 1, ROPE), cosines, sines)
    keys = jnp.concatenate(
        [kv_raw[..., :NOPE], jnp.broadcast_to(key_rope, (micro, slot, HEADS, ROPE))], axis=-1
    ).astype(jnp.bfloat16)
    values = kv_raw[..., NOPE:].astype(jnp.bfloat16)
    raw = jnp.einsum("mqhd,mkhd->mhqk", queries, keys, preferred_element_type=jnp.float32)
    scores = jnp.where(allowed, raw * scale, masked_score)
    top = jnp.max(scores, axis=-1, keepdims=True)
    expo = jnp.exp(scores - top)
    total = jnp.sum(expo, axis=-1, keepdims=True)
    probs = expo / total
    log_total = top + jnp.log(total)
    attended = jnp.einsum(
        "mhqk,mkhd->mqhd", probs.astype(jnp.bfloat16), values, preferred_element_type=jnp.float32
    )
    attended = attended.reshape(rows, HEADS * VDIM).astype(jnp.bfloat16)
    q_rank = query_low.shape[1]
    kv_rank = latent_low.shape[1]
    middle = inputs + depth_scale * matmul(attended, weight_out)
    normed_two, inverse_two = normalize(middle)
    h_two = (normed_two * gain_two.astype(jnp.float32)).astype(jnp.bfloat16)
    gate_up = matmul(h_two, weight_gate_up).reshape(rows, devices, 2, ff_share)
    gate = gate_up[:, :, 0].reshape(rows, ffn)
    upward = gate_up[:, :, 1].reshape(rows, ffn)
    sigma = jax.nn.sigmoid(gate)
    hidden = (gate * sigma * upward).astype(jnp.bfloat16)
    result = (middle + depth_scale * matmul(hidden, weight_down)) * valid_rows
    output = result.astype(jnp.bfloat16).reshape(tokens.shape)
    grad_out = cotangent.reshape(rows, width).astype(jnp.float32) * valid_rows
    grad_feed = (depth_scale * grad_out).astype(jnp.bfloat16)
    latents_all = gather_tokens(
        jnp.concatenate([query_low, latent_low, attended, h_two, grad_feed], axis=1)
    )
    query_low_all = latents_all[:, :q_rank]
    latent_low_all = latents_all[:, q_rank : q_rank + kv_rank]
    attended_all = latents_all[:, q_rank + kv_rank : q_rank + kv_rank + width]
    h_two_all = latents_all[:, q_rank + kv_rank + width : q_rank + kv_rank + 2 * width]
    grad_feed_all = latents_all[:, q_rank + kv_rank + 2 * width :]
    grad_hidden = back_product(grad_feed, weight_down)
    grad_gate = (grad_hidden * upward * sigma * (1.0 + gate * (1.0 - sigma))).astype(jnp.bfloat16)
    grad_up = (grad_hidden * gate * sigma).astype(jnp.bfloat16)
    grad_h_two = back_product(interleave(grad_gate, grad_up, devices), weight_gate_up)
    gain_two_term, grad_middle_norm = norm_back(grad_h_two, normed_two, inverse_two, gain_two)
    grad_middle = grad_out + grad_middle_norm
    grad_attn = (depth_scale * grad_middle).astype(jnp.bfloat16)
    attn_share = width // devices
    gate_up_c = matmul(
        h_two_all, lax.dynamic_slice_in_dim(weight_gate_up, me * 2 * ff_share, 2 * ff_share, 1)
    )
    gate_c = gate_up_c[:, :ff_share]
    up_c = gate_up_c[:, ff_share:]
    sigma_c = jax.nn.sigmoid(gate_c)
    hidden_c = (gate_c * sigma_c * up_c).astype(jnp.bfloat16)
    grad_hidden_c = back_product(grad_feed_all, down_weight)
    grad_gate_c = (grad_hidden_c * up_c * sigma_c * (1.0 + gate_c * (1.0 - sigma_c))).astype(
        jnp.bfloat16
    )
    grad_up_c = (grad_hidden_c * gate_c * sigma_c).astype(jnp.bfloat16)
    down_grad = rows_product(hidden_c, grad_feed_all)
    gate_up_cols = rows_product(h_two_all, jnp.concatenate([grad_gate_c, grad_up_c], axis=1))
    inner_cols = column_shares(jnp.stack([h_one, grad_attn], axis=1), devices)
    h_one_cols = inner_cols[:, 0]
    out_cols = rows_product(attended_all, inner_cols[:, 1])
    wide_cols = jnp.concatenate([gate_up_cols, out_cols], axis=1).reshape(devices, -1)
    grad_heads = (
        back_product(grad_attn, weight_out).astype(jnp.bfloat16).reshape(micro, slot, HEADS, VDIM)
    )
    probs_again = jnp.exp(scores - log_total)
    grad_values = jnp.einsum(
        "mhqk,mqhd->mkhd",
        probs_again.astype(jnp.bfloat16),
        grad_heads,
        preferred_element_type=jnp.float32,
    )
    grad_probs = jnp.einsum(
        "mqhd,mkhd->mhqk", grad_heads, values, preferred_element_type=jnp.float32
    )
    inner = jnp.sum(probs_again * grad_probs, axis=-1, keepdims=True)
    grad_scores = (probs_again * (grad_probs - inner)).astype(jnp.bfloat16)
    grad_queries = scale * jnp.einsum(
        "mhqk,mkhd->mqhd", grad_scores, keys, preferred_element_type=jnp.float32
    )
    grad_keys = scale * jnp.einsum(
        "mhqk,mqhd->mkhd", grad_scores, queries, preferred_element_type=jnp.float32
    )
    grad_query_raw = jnp.concatenate(
        [grad_queries[..., :NOPE], rotate_back(grad_queries[..., NOPE:], cosines, sines)], axis=-1
    )
    grad_query_raw = grad_query_raw.reshape(rows, HEADS * (NOPE + ROPE)).astype(jnp.bfloat16)
    grad_query_low = back_product(grad_query_raw, up_query)
    grad_kv = (
        jnp.concatenate([grad_keys[..., :NOPE], grad_values], axis=-1)
        .reshape(rows, HEADS * (NOPE + VDIM))
        .astype(jnp.bfloat16)
    )
    grad_latent_low = back_product(grad_kv, up_latent)
    latent_gain_term, grad_latent = norm_back(
        grad_latent_low, normed_latent, inverse_latent, gain_latent
    )
    grad_key_rope = rotate_back(
        jnp.sum(grad_keys[..., NOPE:], axis=2, keepdims=True), cosines, sines
    ).reshape(rows, ROPE)
    grad_latent_all = jnp.concatenate([grad_latent, grad_key_rope], axis=-1).astype(jnp.bfloat16)
    query_gain_term, grad_latent_query = norm_back(
        grad_query_low, normed_query, inverse_query, gain_query
    )
    grad_latent_query = grad_latent_query.astype(jnp.bfloat16)
    query_width = up_query.shape[1]
    kv_width = up_latent.shape[1]
    up_cols = column_shares(
        jnp.concatenate(
            [
                grad_query_raw.reshape(rows, devices, query_width // devices),
                grad_kv.reshape(rows, devices, kv_width // devices),
            ],
            axis=2,
        ).reshape(rows, 1, query_width + kv_width),
        devices,
    )[:, 0]
    query_cols = query_width // devices
    query_up_cols = rows_product(query_low_all, up_cols[:, :query_cols])
    latent_up_cols = rows_product(latent_low_all, up_cols[:, query_cols:])
    grad_h_one = back_product(grad_latent_all, down_latent) + back_product(
        grad_latent_query, down_query
    )
    gain_one_term, grad_input_norm = norm_back(grad_h_one, normed_one, inverse_one, gain_one)
    input_grad = (grad_middle + grad_input_norm).reshape(tokens.shape)
    gain_terms = jnp.concatenate([gain_one_term, query_gain_term, latent_gain_term, gain_two_term])
    high, low = split_exact(gain_terms)
    down_grads = jnp.concatenate([grad_latent_all, grad_latent_query], axis=1)
    grad_width = down_grads.shape[1]
    gain_rows = -(-(2 * gain_terms.size) // grad_width)
    gain_block = jnp.pad(
        jnp.concatenate([high, low]), (0, gain_rows * grad_width - 2 * gain_terms.size)
    ).reshape(gain_rows, grad_width)
    last_all = lax.all_gather(
        jnp.concatenate([down_grads, gain_block], axis=0), AXES, axis=0, tiled=False
    )
    down_grads_all = last_all[:, :rows].reshape(devices * rows, grad_width)
    gain_parts = last_all[:, rows:].reshape(devices, gain_rows * grad_width)[:, : 2 * gain_terms.size]
    gain_sums = jnp.sum(
        gain_parts[:, : gain_terms.size].astype(jnp.float32)
        + gain_parts[:, gain_terms.size :].astype(jnp.float32),
        axis=0,
    )
    latent_width = grad_latent_all.shape[1]
    latent_down_grad = rows_product(h_one_cols, down_grads_all[:, :latent_width])
    query_down_grad = rows_product(h_one_cols, down_grads_all[:, latent_width:])
    wide_size = wide_cols.shape[1]
    all_rows = rows_from_columns(
        jnp.concatenate(
            [
                wide_cols,
                query_up_cols.reshape(devices, -1),
                latent_up_cols.reshape(devices, -1),
            ],
            axis=1,
        ).reshape(devices, 1, -1),
        devices,
    ).reshape(devices, -1)
    wide_rows = (
        all_rows[:, :wide_size]
        .reshape(devices, width // devices, 2 * ff_share + attn_share)
        .transpose(1, 0, 2)
    )
    gate_grad = wide_rows[:, :, :ff_share].reshape(width // devices, ffn)
    up_grad = wide_rows[:, :, ff_share : 2 * ff_share].reshape(width // devices, ffn)
    output_weight_grad = wide_rows[:, :, 2 * ff_share :].reshape(width // devices, width)
    up_rows = all_rows[:, wide_size:]
    q_rows = up_query.shape[0] // devices
    kv_rows = up_latent.shape[0] // devices
    kv_cols = kv_width // devices
    up_rows = up_rows.reshape(devices, -1)
    query_up_grad = (
        up_rows[:, : q_rows * query_cols]
        .reshape(devices, q_rows, query_cols)
        .transpose(1, 0, 2)
        .reshape(q_rows, query_width)
    )
    latent_up_grad = (
        up_rows[:, q_rows * query_cols :]
        .reshape(devices, kv_rows, kv_cols)
        .transpose(1, 0, 2)
        .reshape(kv_rows, kv_width)
    )

    def own(vector, offset, size):
        share = size // devices
        return lax.dynamic_slice(vector, (offset + me * share,), (share,))

    d_model = gain_one_term.size
    attn_gain_grad = own(gain_sums, 0, d_model)
    query_gain_grad = own(gain_sums, d_model, q_rank)
    latent_gain_grad = own(gain_sums, d_model + q_rank, kv_rank)
    feed_gain_grad = own(gain_sums, d_model + q_rank + kv_rank, d_model)
    return (
        output,
        input_grad,
        attn_gain_grad,
        query_down_grad,
        query_gain_grad,
        query_up_grad,
        latent_down_grad,
        latent_gain_grad,
        latent_up_grad,
        output_weight_grad,
        feed_gain_grad,
        gate_grad,
        up_grad,
        down_grad,
    )


def solution(mesh):
    placed = (
        P(None, ("fsdp", "dp"), None, None),
        P(None, ("fsdp", "dp")),
        P(("fsdp", "dp")),
        P(("fsdp", "dp"), None),
        P(("fsdp", "dp")),
        P(("fsdp", "dp"), None),
        P(("fsdp", "dp"), None),
        P(("fsdp", "dp")),
        P(("fsdp", "dp"), None),
        P(("fsdp", "dp"), None),
        P(("fsdp", "dp")),
        P(("fsdp", "dp"), None),
        P(("fsdp", "dp"), None),
        P(("fsdp", "dp"), None),
        P(None, ("fsdp", "dp"), None, None),
    )
    return jax.shard_map(
        local,
        mesh=mesh,
        in_specs=placed,
        out_specs=(
            P(None, ("fsdp", "dp"), None, None),
            P(None, ("fsdp", "dp"), None, None),
            P(("fsdp", "dp")),
            P(("fsdp", "dp"), None),
            P(("fsdp", "dp")),
            P(("fsdp", "dp"), None),
            P(("fsdp", "dp"), None),
            P(("fsdp", "dp")),
            P(("fsdp", "dp"), None),
            P(("fsdp", "dp"), None),
            P(("fsdp", "dp")),
            P(("fsdp", "dp"), None),
            P(("fsdp", "dp"), None),
            P(("fsdp", "dp"), None),
        ),
        check_vma=False,
    )
```
